32 devices in a mesh: user: 16 (over z, y, x), item: 2 (over core).
Axes of the slice: x: 2, y: 2, z: 4, core: 2. Of those that a mesh axis runs over, the one named last changes fastest.
Arguments:
- draws_user: float32 [16, 768, 256], P('user', 'item'), may hold values from -200 to 200
- draws_item: float32 [2, 1024, 256], P('item', 'user'), may hold values from -200 to 200
- prior_user: float32 [64, 64], replicated, may hold values from -1 to 5, as said below
- prior_item: float32 [64, 64], replicated, may hold values from -1 to 5, as said below
- count_tiles: int32 [16, 2, 12, 256, 256], P('user', 'item'), may hold values from 0 to 3
- tile_blocks: int32 [16, 2, 12, 2], P('user', 'item'), may hold values from 0 to 3, as said below
- tile_count: int32 [16, 2], P('user', 'item'), may hold values from 4 to 12, as said below
Outputs:
- solution_user: float32 [16, 768, 256], P('user', 'item')
- solution_item: float32 [2, 1024, 256], P('item', 'user')
- residual_user: float32 [16, 768, 256], P('user', 'item')
- residual_item: float32 [2, 1024, 256], P('item', 'user')
The draws below stay inside these ranges and needn't reach their ends.
Inputs may be any that keep to these rules, and one draw needn't show every extreme that they name: `tile_blocks`: each device's list names 12 distinct pairs (row block from 0 to 2, column block from 0 to 3); entries after tile_count are not in use. `tile_count`: some device uses all 12 tiles. `prior_user`: symmetric, diagonal from 2.5 to 4.5, each off-diagonal entry within 2 / 64 in magnitude. `prior_item`: symmetric, diagonal from 2.5 to 4.5, each off-diagonal entry within 2 / 64 in magnitude.
All inputs are finite; a program needn't handle non-finite values.
Results may differ from the reference program's by a relative error of at most 0.028.
Values may be sent and summed in bfloat16 or wider, within the bound.
No kernel may reach another device: no remote copies, remote signals or barrier semaphores. Data moves between devices by JAX's collectives and lax.ppermute only.
A program may use at most 64 MiB of HBM per device.

```python
import jax
import jax.numpy as jnp
from jax import lax

DIM = 64
DRAWS = 4
TILE = 256
RB = 3
CB = 4
TMAX = 12
ITERS = 2
N_USER = 16
N_ITEM = 2


def offset_field(key, dev_total, rows_dev, spread):
    noise_key, shift_key = jax.random.split(key, 2)
    width = DRAWS * DIM
    row_total = dev_total * rows_dev
    place = jnp.arange(dev_total, dtype=jnp.float32) / max(dev_total - 1, 1)
    noise_part = jax.random.normal(noise_key, (row_total, width), jnp.float32)
    shift_row = 0.1 * jax.random.normal(shift_key, (1, width), jnp.float32)
    rising = jnp.exp(jnp.log(3.0) * place)
    field_vec = (noise_part + shift_row).reshape(dev_total, rows_dev, width)
    return spread * field_vec * rising[:, None, None]


def draw_draws_user(key, part):
    return offset_field(jax.random.fold_in(key, 21), N_USER, RB * TILE, 4.0)


def draw_draws_item(key, part):
    return offset_field(jax.random.fold_in(key, 22), N_ITEM, CB * TILE, 2.5)


def precision_matrix(key):
    off_key, diag_key = jax.random.split(key)
    raw_off = jax.random.uniform(off_key, (DIM, DIM), jnp.float32, -2.0 / DIM, 2.0 / DIM)
    sym_off = 0.5 * (raw_off + raw_off.T)
    diag_vals = jax.random.uniform(diag_key, (DIM,), jnp.float32, 2.5, 4.5)
    on_diag = jnp.eye(DIM, dtype=bool)
    return jnp.where(on_diag, diag_vals[None, :], sym_off)


def draw_prior_user(key, part):
    return precision_matrix(jax.random.fold_in(key, 11))


def draw_prior_item(key, part):
    return precision_matrix(jax.random.fold_in(key, 12))


def block_lists(key):
    dev_keys = jax.random.split(jax.random.fold_in(key, 31), N_USER * N_ITEM)

    def one_list(dev_key):
        slot_ids = jax.random.permutation(dev_key, RB * CB)[:TMAX].astype(jnp.int32)
        return jnp.stack([slot_ids // CB, slot_ids % CB], axis=1)
    return jax.vmap(one_list)(dev_keys).reshape(N_USER, N_ITEM, TMAX, 2)


def draw_tile_blocks(key, part):
    return block_lists(key)


def draw_count_tiles(key, part):
    blocks = block_lists(key).reshape(N_USER * N_ITEM, TMAX, 2)
    user_level = jax.random.randint(jax.random.fold_in(key, 41), (N_USER * RB * TILE,), 0, 3).astype(jnp.int32)
    item_level = jax.random.randint(jax.random.fold_in(key, 42), (N_ITEM * CB * TILE,), 0, 3).astype(jnp.int32)
    cell_key = jax.random.fold_in(key, 43)
    span = 3 * TILE // 2
    offsets = jnp.arange(TILE, dtype=jnp.int32)

    def one_device(dev_id):
        user_dev = dev_id // N_ITEM
        item_dev = dev_id % N_ITEM
        dev_blocks = blocks[dev_id]
        user_index = (user_dev * RB + dev_blocks[:, 0])[:, None] * TILE + offsets[None, :]
        item_index = (item_dev * CB + dev_blocks[:, 1])[:, None] * TILE + offsets[None, :]
        levels = user_level[user_index][:, :, None] + item_level[item_index][:, None, :]
        limit = jnp.left_shift(jnp.ones_like(levels), levels)
        raw = jax.random.randint(jax.random.fold_in(cell_key, dev_id), (TMAX, TILE, TILE), 0, 3 * span).astype(jnp.int32)
        return jnp.where(raw % span < limit, raw // span + 1, 0).astype(jnp.int32)
    tiles = lax.map(one_device, jnp.arange(N_USER * N_ITEM, dtype=jnp.int32))
    return tiles.reshape(N_USER, N_ITEM, TMAX, TILE, TILE)


def draw_tile_count(key, part):
    base_key = jax.random.fold_in(key, 32)
    lowest = max(1, TMAX // 3)
    counts = jax.random.randint(base_key, (N_USER * N_ITEM,), lowest, TMAX + 1).astype(jnp.int32)
    full_dev = jax.random.randint(jax.random.fold_in(base_key, 7), (), 0, N_USER * N_ITEM)
    counts = jnp.where(jnp.arange(N_USER * N_ITEM, dtype=jnp.int32) == full_dev, TMAX, counts)
    return counts.astype(jnp.int32).reshape(N_USER, N_ITEM)


def setup_inputs(seed: int = 0) -> dict:
    keys = jax.random.split(jax.random.key(seed), 8)
    draws_user = draw_draws_user(jax.random.fold_in(keys[7], 71), 0)
    draws_item = draw_draws_item(jax.random.fold_in(keys[7], 71), 0)
    prior_user = draw_prior_user(jax.random.fold_in(keys[7], 71), 0)
    prior_item = draw_prior_item(jax.random.fold_in(keys[7], 71), 0)
    count_tiles = draw_count_tiles(jax.random.fold_in(keys[7], 71), 0)
    tile_blocks = draw_tile_blocks(jax.random.fold_in(keys[7], 71), 0)
    tile_count = draw_tile_count(jax.random.fold_in(keys[7], 71), 0)
    return {"draws_user": draws_user, "draws_item": draws_item, "prior_user": prior_user, "prior_item": prior_item, "count_tiles": count_tiles, "tile_blocks": tile_blocks, "tile_count": tile_count}


top_prec = lax.Precision.HIGHEST
noise_prec = 0.03125


def prior_term(field_vec, prior_mat):
    row_total = field_vec.shape[0]
    grouped = field_vec.reshape(row_total, DRAWS, DIM)
    mixed = jnp.einsum("nde,ef->ndf", grouped, prior_mat, precision=top_prec)
    return mixed.reshape(row_total, DRAWS * DIM)


def cross_terms(user_dir, item_dir, count_tiles, tile_blocks, tile_count):
    width = DRAWS * DIM
    item_blocks = item_dir.astype(jnp.float32).reshape(N_ITEM, CB, TILE, width)
    slot_ids = jnp.arange(TMAX, dtype=jnp.int32)

    def one_user(running, inputs):
        tiles_here, blocks_here, count_here, user_here = inputs
        in_use = slot_ids[None, :] < count_here[:, None]
        counts_f = jnp.where(in_use[:, :, None, None], tiles_here, 0).astype(jnp.float32)
        row_pick = ((blocks_here[:, :, 0][:, :, None] == jnp.arange(RB, dtype=jnp.int32)) & in_use[:, :, None]).astype(jnp.float32)
        col_pick = ((blocks_here[:, :, 1][:, :, None] == jnp.arange(CB, dtype=jnp.int32)) & in_use[:, :, None]).astype(jnp.float32)
        user_blocks = user_here.astype(jnp.float32).reshape(RB, TILE, width)
        user_sel = jnp.einsum("btr,ris->btis", row_pick, user_blocks, precision=top_prec)
        item_sel = jnp.einsum("btc,bcjs->btjs", col_pick, item_blocks, precision=top_prec)
        to_users = jnp.einsum("btij,btjs->btis", counts_f, item_sel, precision=top_prec) + jnp.sum(counts_f, axis=3)[..., None] * user_sel
        to_items = jnp.einsum("btij,btis->btjs", counts_f, user_sel, precision=top_prec) + jnp.sum(counts_f, axis=2)[..., None] * item_sel
        cross_user = jnp.einsum("btr,btis->ris", row_pick, to_users, precision=top_prec).reshape(RB * TILE, width)
        cross_item = jnp.einsum("btc,btjs->bcjs", col_pick, to_items, precision=top_prec).reshape(N_ITEM, CB * TILE, width)
        return running + cross_item, cross_user

    zero_items = jnp.zeros((N_ITEM, CB * TILE, width), jnp.float32)
    cross_item, cross_user = lax.scan(one_user, zero_items, (count_tiles, tile_blocks, tile_count, user_dir))
    return cross_user, cross_item


def per_draw(left, right):
    product = (left * right).reshape(-1, DRAWS, DIM)
    return jnp.sum(product, axis=(0, 2))


def inner(a_user, a_item, b_user, b_item):
    return per_draw(a_user, b_user) + per_draw(a_item, b_item)


def widen(coef):
    return jnp.repeat(coef, DIM)


def reference(draws_user, draws_item, prior_user, prior_item, count_tiles, tile_blocks, tile_count):
    width = DRAWS * DIM
    weight = noise_prec

    def operate(user_vec, item_vec):
        cross_user, cross_item = cross_terms(user_vec.astype(jnp.bfloat16), item_vec.astype(jnp.bfloat16), count_tiles, tile_blocks, tile_count)
        image_user = prior_term(user_vec.reshape(-1, width), prior_user).reshape(user_vec.shape) + weight * cross_user
        image_item = prior_term(item_vec.reshape(-1, width), prior_item).reshape(item_vec.shape) + weight * cross_item
        return image_user, image_item

    sol_user = jnp.zeros_like(draws_user)
    sol_item = jnp.zeros_like(draws_item)
    res_user, res_item = draws_user, draws_item
    dir_user, dir_item = draws_user, draws_item
    norm_now = inner(res_user, res_item, res_user, res_item)
    for iteration in range(ITERS):
        image_user, image_item = operate(dir_user, dir_item)
        step_len = norm_now / inner(dir_user, dir_item, image_user, image_item)
        sol_user = sol_user + widen(step_len) * dir_user
        sol_item = sol_item + widen(step_len) * dir_item
        res_user = res_user - widen(step_len) * image_user
        res_item = res_item - widen(step_len) * image_item
        if iteration + 1 < ITERS:
            norm_next = inner(res_user, res_item, res_user, res_item)
            beta_coef = norm_next / norm_now
            dir_user = res_user + widen(beta_coef) * dir_user
            dir_item = res_item + widen(beta_coef) * dir_item
            norm_now = norm_next
    return (sol_user, sol_item, res_user, res_item)
```

```python
import jax
import jax.numpy as jnp
from jax import lax
from jax.sharding import PartitionSpec as P

DIM = 64
DRAWS = 4
TILE = 256
RB = 3
CB = 4
TMAX = 12
ITERS = 2


top_prec = lax.Precision.HIGHEST
noise_prec = 0.03125


def prior_term(field_vec, prior_mat):
    row_total = field_vec.shape[0]
    grouped = field_vec.reshape(row_total, DRAWS, DIM)
    mixed = jnp.einsum("nde,ef->ndf", grouped, prior_mat, precision=top_prec)
    return mixed.reshape(row_total, DRAWS * DIM)


def per_draw(left, right):
    product = (left * right).reshape(-1, DRAWS, DIM)
    return jnp.sum(product, axis=(0, 2))


def widen(coef):
    return jnp.repeat(coef, DIM)


def bit_count(axis):
    size = lax.axis_size(axis)
    bits = size.bit_length() - 1
    assert size == 1 << bits
    return size, bits


def swap_with(value, axis, size, bit):
    pairs = [(i, i ^ (1 << bit)) for i in range(size)]
    return lax.ppermute(value, axis, pairs)


def butterfly_psum(values):
    values = jnp.stack(values)
    for axis in ("item", "user"):
        size, bits = bit_count(axis)
        for bit in range(bits):
            values = values + swap_with(values, axis, size, bit)
    return values[0], values[1]


def halve_sum(part, axis, send_type):
    size, bits = bit_count(axis)
    me = lax.axis_index(axis)
    rows, width = part.shape[0] // size, part.shape[1]
    left = list(range(bits))[::-1]
    buf = part.reshape([2] * bits + [rows, width])
    for bit in range(bits):
        pos = left.index(bit)
        low = lax.index_in_dim(buf, 0, pos, keepdims=False)
        high = lax.index_in_dim(buf, 1, pos, keepdims=False)
        upper = ((me >> bit) & 1) == 1
        keep = jnp.where(upper, high, low)
        send = jnp.where(upper, low, high).astype(send_type)
        buf = keep + swap_with(send, axis, size, bit).astype(jnp.float32)
        left.remove(bit)
    return buf.reshape(rows, width)


def double_gather(piece, axis):
    size, bits = bit_count(axis)
    me = lax.axis_index(axis)
    buf = piece[None]
    for step, bit in enumerate(reversed(range(bits))):
        other = swap_with(buf, axis, size, bit)
        upper = ((me >> bit) & 1) == 1
        first = jnp.where(upper, other, buf)
        second = jnp.where(upper, buf, other)
        buf = jnp.stack([first, second], axis=step)
        buf = buf.reshape((-1,) + piece.shape)
        buf = buf.reshape([2] * (step + 1) + list(piece.shape))
    return buf.reshape((size * piece.shape[0],) + piece.shape[1:])


def per_device(
    draws_user, draws_item, prior_user, prior_item, count_tiles, tile_blocks, tile_count
):
    width = DRAWS * DIM
    user_own = draws_user[0]
    item_own = draws_item[0]
    in_use = jnp.arange(TMAX, dtype=jnp.int32) < tile_count[0, 0]
    counts_bf = jnp.where(in_use[:, None, None], count_tiles[0, 0], 0).astype(jnp.bfloat16)
    row_pick = (
        (tile_blocks[0, 0, :, 0][:, None] == jnp.arange(RB, dtype=jnp.int32)) & in_use[:, None]
    ).astype(jnp.float32)
    col_pick = (
        (tile_blocks[0, 0, :, 1][:, None] == jnp.arange(CB, dtype=jnp.int32)) & in_use[:, None]
    ).astype(jnp.float32)
    row_pick_bf = row_pick.astype(jnp.bfloat16)
    col_pick_bf = col_pick.astype(jnp.bfloat16)
    row_sums = jnp.sum(counts_bf, axis=2, dtype=jnp.float32)
    col_sums = jnp.sum(counts_bf, axis=1, dtype=jnp.float32)

    def cross_parts(user_range, item_range):
        user_sel = jnp.einsum(
            "tr,ris->tis",
            row_pick_bf,
            user_range.reshape(RB, TILE, width),
            preferred_element_type=jnp.float32,
        )
        item_sel = jnp.einsum(
            "tc,cjs->tjs",
            col_pick_bf,
            item_range.reshape(CB, TILE, width),
            preferred_element_type=jnp.float32,
        )
        to_users = (
            jnp.einsum(
                "tij,tjs->tis",
                counts_bf,
                item_sel.astype(jnp.bfloat16),
                preferred_element_type=jnp.float32,
            )
            + row_sums[:, :, None] * user_sel
        )
        to_items = (
            jnp.einsum(
                "tij,tis->tjs",
                counts_bf,
                user_sel.astype(jnp.bfloat16),
                preferred_element_type=jnp.float32,
            )
            + col_sums[:, :, None] * item_sel
        )
        part_user = jnp.einsum("tr,tis->ris", row_pick, to_users, precision=top_prec).reshape(
            RB * TILE, width
        )
        part_item = jnp.einsum("tc,tjs->cjs", col_pick, to_items, precision=top_prec).reshape(
            CB * TILE, width
        )
        return (part_user, part_item)

    def user_range_of(user_vec):
        return lax.all_gather(user_vec.astype(jnp.bfloat16), "item", axis=0, tiled=True)

    def finish_users(user_vec, part_user):
        total = halve_sum(part_user, "item", jnp.bfloat16)
        return prior_term(user_vec, prior_user) + noise_prec * total

    def item_range_of(item_vec):
        return double_gather(item_vec.astype(jnp.bfloat16), "user")

    def finish_items(item_vec, part_item):
        total = halve_sum(part_item, "user", jnp.float32)
        return prior_term(item_vec, prior_item) + noise_prec * total

    def operate(user_vec, item_vec):
        part_user, part_item = cross_parts(user_range_of(user_vec), item_range_of(item_vec))
        return (finish_users(user_vec, part_user), finish_items(item_vec, part_item))

    def inner(a_user, a_item, b_user, b_item):
        return per_draw(a_user, b_user) + per_draw(a_item, b_item)

    sol_user = jnp.zeros_like(user_own)
    sol_item = jnp.zeros_like(item_own)
    res_user, res_item = (user_own, item_own)
    dir_user, dir_item = (user_own, item_own)

    def two_sums(u_vec, v_vec, image_u, image_v):
        return butterfly_psum(
            (inner(u_vec, v_vec, u_vec, v_vec), inner(u_vec, v_vec, image_u, image_v)),
        )

    along_user, along_item = operate(res_user, res_item)
    norm_now, curve = two_sums(res_user, res_item, along_user, along_item)
    step_len = norm_now / curve
    for iteration in range(ITERS):
        sol_user = sol_user + widen(step_len) * dir_user
        sol_item = sol_item + widen(step_len) * dir_item
        res_user = res_user - widen(step_len) * along_user
        res_item = res_item - widen(step_len) * along_item
        if iteration + 1 < ITERS:
            image_user, image_item = operate(res_user, res_item)
            norm_next, curve = two_sums(res_user, res_item, image_user, image_item)
            beta_coef = norm_next / norm_now
            step_len = norm_next / (curve - beta_coef * norm_next / step_len)
            dir_user = res_user + widen(beta_coef) * dir_user
            dir_item = res_item + widen(beta_coef) * dir_item
            along_user = image_user + widen(beta_coef) * along_user
            along_item = image_item + widen(beta_coef) * along_item
            norm_now = norm_next
    return (sol_user[None], sol_item[None], res_user[None], res_item[None])


def solution(mesh):
    in_specs = (
        P("user", "item", None),
        P("item", "user", None),
        P(),
        P(),
        P("user", "item", None, None, None),
        P("user", "item", None, None),
        P("user", "item"),
    )
    out_specs = (
        P("user", "item", None),
        P("item", "user", None),
        P("user", "item", None),
        P("item", "user", None),
    )
    return jax.shard_map(
        per_device, mesh=mesh, in_specs=in_specs, out_specs=out_specs, check_vma=False
    )
```

```python
import jax
import jax.numpy as jnp
from jax import lax
from jax.sharding import PartitionSpec as P

DIM = 64
DRAWS = 4
TILE = 256
RB = 3
CB = 4
TMAX = 12
ITERS = 2


top_prec = lax.Precision.HIGHEST
noise_prec = 0.03125


def prior_term(field_vec, prior_mat):
    row_total = field_vec.shape[0]
    grouped = field_vec.reshape(row_total, DRAWS, DIM)
    mixed = jnp.einsum("nde,ef->ndf", grouped, prior_mat, precision=top_prec)
    return mixed.reshape(row_total, DRAWS * DIM)


def per_draw(left, right):
    product = (left * right).reshape(-1, DRAWS, DIM)
    return jnp.sum(product, axis=(0, 2))


def widen(coef):
    return jnp.repeat(coef, DIM)


def bit_count(axis):
    size = lax.axis_size(axis)
    bits = size.bit_length() - 1
    assert size == 1 << bits
    return size, bits


def swap_with(value, axis, size, bit):
    pairs = [(i, i ^ (1 << bit)) for i in range(size)]
    return lax.ppermute(value, axis, pairs)


def butterfly_psum(values):
    values = jnp.stack(values)
    for axis in ("item", "user"):
        size, bits = bit_count(axis)
        for bit in range(bits):
            values = values + swap_with(values, axis, size, bit)
    return values[0], values[1]


def halve_sum(part, axis, send_type):
    size, bits = bit_count(axis)
    me = lax.axis_index(axis)
    rows, width = part.shape[0] // size, part.shape[1]
    left = list(range(bits))[::-1]
    buf = part.reshape([2] * bits + [rows, width])
    for bit in range(bits):
        pos = left.index(bit)
        low = lax.index_in_dim(buf, 0, pos, keepdims=False)
        high = lax.index_in_dim(buf, 1, pos, keepdims=False)
        upper = ((me >> bit) & 1) == 1
        keep = jnp.where(upper, high, low)
        send = jnp.where(upper, low, high).astype(send_type)
        buf = keep + swap_with(send, axis, size, bit).astype(jnp.float32)
        left.remove(bit)
    return buf.reshape(rows, width)


def double_gather(piece, axis):
    size, bits = bit_count(axis)
    me = lax.axis_index(axis)
    buf = piece[None]
    for step, bit in enumerate(reversed(range(bits))):
        other = swap_with(buf, axis, size, bit)
        upper = ((me >> bit) & 1) == 1
        first = jnp.where(upper, other, buf)
        second = jnp.where(upper, buf, other)
        buf = jnp.stack([first, second], axis=step)
        buf = buf.reshape((-1,) + piece.shape)
        buf = buf.reshape([2] * (step + 1) + list(piece.shape))
    return buf.reshape((size * piece.shape[0],) + piece.shape[1:])


def per_device(
    draws_user, draws_item, prior_user, prior_item, count_tiles, tile_blocks, tile_count
):
    width = DRAWS * DIM
    user_own = draws_user[0]
    item_own = draws_item[0]
    in_use = jnp.arange(TMAX, dtype=jnp.int32) < tile_count[0, 0]
    row_pick = (tile_blocks[0, 0, :, 0][:, None] == jnp.arange(RB, dtype=jnp.int32)) & in_use[:, None]
    col_pick = (tile_blocks[0, 0, :, 1][:, None] == jnp.arange(CB, dtype=jnp.int32)) & in_use[:, None]
    place = (row_pick[:, :, None] & col_pick[:, None, :]).astype(jnp.bfloat16)
    block_counts = jnp.einsum(
        "trc,tij->ricj",
        place,
        count_tiles[0, 0].astype(jnp.bfloat16),
        preferred_element_type=jnp.float32,
    ).reshape(RB * TILE, CB * TILE)
    user_deg = jnp.sum(block_counts, axis=1)
    item_deg = jnp.sum(block_counts, axis=0)
    counts_bf = block_counts.astype(jnp.bfloat16)

    def cross_parts(user_range, item_range):
        to_users = jnp.dot(counts_bf, item_range, preferred_element_type=jnp.float32)
        to_users = to_users + user_deg[:, None] * user_range.astype(jnp.float32)
        to_items = lax.dot_general(
            counts_bf, user_range, (((0,), (0,)), ((), ())), preferred_element_type=jnp.float32
        )
        to_items = to_items + item_deg[:, None] * item_range.astype(jnp.float32)
        return (to_users, to_items)

    def user_range_of(user_vec):
        return lax.all_gather(user_vec.astype(jnp.bfloat16), "item", axis=0, tiled=True)

    def finish_users(user_vec, part_user):
        total = halve_sum(part_user, "item", jnp.bfloat16)
        return prior_term(user_vec, prior_user) + noise_prec * total

    def item_range_of(item_vec):
        return double_gather(item_vec.astype(jnp.bfloat16), "user")

    def finish_items(item_vec, part_item):
        total = halve_sum(part_item, "user", jnp.float32)
        return prior_term(item_vec, prior_item) + noise_prec * total

    def operate(user_vec, item_vec):
        part_user, part_item = cross_parts(user_range_of(user_vec), item_range_of(item_vec))
        return (finish_users(user_vec, part_user), finish_items(item_vec, part_item))

    def inner(a_user, a_item, b_user, b_item):
        return per_draw(a_user, b_user) + per_draw(a_item, b_item)

    sol_user = jnp.zeros_like(user_own)
    sol_item = jnp.zeros_like(item_own)
    res_user, res_item = (user_own, item_own)
    dir_user, dir_item = (user_own, item_own)

    def two_sums(u_vec, v_vec, image_u, image_v):
        return butterfly_psum(
            (inner(u_vec, v_vec, u_vec, v_vec), inner(u_vec, v_vec, image_u, image_v)),
        )

    along_user, along_item = operate(res_user, res_item)
    norm_now, curve = two_sums(res_user, res_item, along_user, along_item)
    step_len = norm_now / curve
    for iteration in range(ITERS):
        sol_user = sol_user + widen(step_len) * dir_user
        sol_item = sol_item + widen(step_len) * dir_item
        res_user = res_user - widen(step_len) * along_user
        res_item = res_item - widen(step_len) * along_item
        if iteration + 1 < ITERS:
            image_user, image_item = operate(res_user, res_item)
            norm_next, curve = two_sums(res_user, res_item, image_user, image_item)
            beta_coef = norm_next / norm_now
            step_len = norm_next / (curve - beta_coef * norm_next / step_len)
            dir_user = res_user + widen(beta_coef) * dir_user
            dir_item = res_item + widen(beta_coef) * dir_item
            along_user = image_user + widen(beta_coef) * along_user
            along_item = image_item + widen(beta_coef) * along_item
            norm_now = norm_next
    return (sol_user[None], sol_item[None], res_user[None], res_item[None])


def solution(mesh):
    in_specs = (
        P("user", "item", None),
        P("item", "user", None),
        P(),
        P(),
        P("user", "item", None, None, None),
        P("user", "item", None, None),
        P("user", "item"),
    )
    out_specs = (
        P("user", "item", None),
        P("item", "user", None),
        P("user", "item", None),
        P("item", "user", None),
    )
    return jax.shard_map(
        per_device, mesh=mesh, in_specs=in_specs, out_specs=out_specs, check_vma=False
    )
```

```python
import jax
import jax.numpy as jnp
from jax import lax
from jax.sharding import PartitionSpec as P

DIM = 64
DRAWS = 4
TILE = 256
RB = 3
CB = 4
TMAX = 12
ITERS = 2


top_prec = lax.Precision.HIGHEST
noise_prec = 0.03125


def prior_term(field_vec, prior_mat):
    row_total = field_vec.shape[0]
    grouped = field_vec.reshape(row_total, DRAWS, DIM)
    mixed = jnp.einsum("nde,ef->ndf", grouped, prior_mat, precision=top_prec)
    return mixed.reshape(row_total, DRAWS * DIM)


def per_draw(left, right):
    product = (left * right).reshape(-1, DRAWS, DIM)
    return jnp.sum(product, axis=(0, 2))


def widen(coef):
    return jnp.repeat(coef, DIM)


def bit_count(axis):
    size = lax.axis_size(axis)
    bits = size.bit_length() - 1
    assert size == 1 << bits
    return size, bits


def swap_with(value, axis, size, bit):
    pairs = [(i, i ^ (1 << bit)) for i in range(size)]
    return lax.ppermute(value, axis, pairs)


def butterfly_psum(values):
    values = jnp.stack(values)
    for axis in ("item", "user"):
        size, bits = bit_count(axis)
        for bit in range(bits):
            values = values + swap_with(values, axis, size, bit)
    return values[0], values[1]


def halve_sum(part, axis, send_type, extra=None):
    size, bits = bit_count(axis)
    me = lax.axis_index(axis)
    rows, width = part.shape[0] // size, part.shape[1]
    left = list(range(bits))[::-1]
    buf = part.reshape([2] * bits + [rows, width])
    for bit in range(bits):
        pos = left.index(bit)
        low = lax.index_in_dim(buf, 0, pos, keepdims=False)
        high = lax.index_in_dim(buf, 1, pos, keepdims=False)
        upper = ((me >> bit) & 1) == 1
        keep = jnp.where(upper, high, low)
        send = jnp.where(upper, low, high).astype(send_type)
        if extra is None:
            buf = keep + swap_with(send, axis, size, bit).astype(jnp.float32)
        else:
            message = jnp.concatenate([send.reshape(-1, width), extra])
            got = swap_with(message, axis, size, bit)
            buf = keep + got[: -extra.shape[0]].reshape(keep.shape)
            extra = extra + got[-extra.shape[0] :]
        left.remove(bit)
    return buf.reshape(rows, width), extra


def double_gather(piece, axis):
    size, bits = bit_count(axis)
    me = lax.axis_index(axis)
    buf = piece[None]
    for step, bit in enumerate(reversed(range(bits))):
        other = swap_with(buf, axis, size, bit)
        upper = ((me >> bit) & 1) == 1
        first = jnp.where(upper, other, buf)
        second = jnp.where(upper, buf, other)
        buf = jnp.stack([first, second], axis=step)
        buf = buf.reshape((-1,) + piece.shape)
        buf = buf.reshape([2] * (step + 1) + list(piece.shape))
    return buf.reshape((size * piece.shape[0],) + piece.shape[1:])


def per_device(
    draws_user, draws_item, prior_user, prior_item, count_tiles, tile_blocks, tile_count
):
    width = DRAWS * DIM
    user_own = draws_user[0]
    item_own = draws_item[0]
    in_use = jnp.arange(TMAX, dtype=jnp.int32) < tile_count[0, 0]
    row_pick = (tile_blocks[0, 0, :, 0][:, None] == jnp.arange(RB, dtype=jnp.int32)) & in_use[:, None]
    col_pick = (tile_blocks[0, 0, :, 1][:, None] == jnp.arange(CB, dtype=jnp.int32)) & in_use[:, None]
    place = (row_pick[:, :, None] & col_pick[:, None, :]).astype(jnp.bfloat16)
    block_counts = jnp.einsum(
        "trc,tij->ricj",
        place,
        count_tiles[0, 0].astype(jnp.bfloat16),
        preferred_element_type=jnp.float32,
    ).reshape(RB * TILE, CB * TILE)
    user_deg = jnp.sum(block_counts, axis=1)
    item_deg = jnp.sum(block_counts, axis=0)
    counts_bf = block_counts.astype(jnp.bfloat16)

    def cross_parts(user_range, item_range):
        to_users = jnp.dot(counts_bf, item_range, preferred_element_type=jnp.float32)
        to_users = to_users + user_deg[:, None] * user_range.astype(jnp.float32)
        to_items = lax.dot_general(
            counts_bf, user_range, (((0,), (0,)), ((), ())), preferred_element_type=jnp.float32
        )
        to_items = to_items + item_deg[:, None] * item_range.astype(jnp.float32)
        return (to_users, to_items)

    def user_range_of(user_vec):
        return lax.all_gather(user_vec.astype(jnp.bfloat16), "item", axis=0, tiled=True)

    def item_range_of(item_vec):
        return double_gather(item_vec.astype(jnp.bfloat16), "user")

    def operate(user_vec, item_vec):
        user_range = user_range_of(user_vec)
        item_range = item_range_of(item_vec)
        part_user, part_item = cross_parts(user_range, item_range)
        prior_user_part = prior_term(user_vec, prior_user)
        prior_item_part = prior_term(item_vec, prior_item)
        norm_part = per_draw(user_vec, user_vec) + per_draw(item_vec, item_vec)
        cross_dot = per_draw(user_range.astype(jnp.float32), part_user) + per_draw(
            item_range.astype(jnp.float32), part_item
        )
        curve_part = (
            per_draw(user_vec, prior_user_part)
            + per_draw(item_vec, prior_item_part)
            + noise_prec * cross_dot
        )
        sums = jnp.concatenate([norm_part, curve_part]).reshape(1, 2 * DRAWS)
        sums = jnp.pad(sums, ((0, 7), (0, width - 2 * DRAWS)))
        total_user, _ = halve_sum(part_user, "item", jnp.bfloat16)
        total_item, sums = halve_sum(part_item, "user", jnp.float32, sums)
        sums = sums[0, : 2 * DRAWS]
        size, bits = bit_count("item")
        for bit in range(bits):
            sums = sums + swap_with(sums, "item", size, bit)
        image_user = prior_user_part + noise_prec * total_user
        image_item = prior_item_part + noise_prec * total_item
        return (image_user, image_item, sums[:DRAWS], sums[DRAWS:])

    sol_user = jnp.zeros_like(user_own)
    sol_item = jnp.zeros_like(item_own)
    res_user, res_item = (user_own, item_own)
    dir_user, dir_item = (user_own, item_own)

    along_user, along_item, norm_now, curve = operate(res_user, res_item)
    step_len = norm_now / curve
    for iteration in range(ITERS):
        sol_user = sol_user + widen(step_len) * dir_user
        sol_item = sol_item + widen(step_len) * dir_item
        res_user = res_user - widen(step_len) * along_user
        res_item = res_item - widen(step_len) * along_item
        if iteration + 1 < ITERS:
            image_user, image_item, norm_next, curve = operate(res_user, res_item)
            beta_coef = norm_next / norm_now
            step_len = norm_next / (curve - beta_coef * norm_next / step_len)
            dir_user = res_user + widen(beta_coef) * dir_user
            dir_item = res_item + widen(beta_coef) * dir_item
            along_user = image_user + widen(beta_coef) * along_user
            along_item = image_item + widen(beta_coef) * along_item
            norm_now = norm_next
    return (sol_user[None], sol_item[None], res_user[None], res_item[None])


def solution(mesh):
    in_specs = (
        P("user", "item", None),
        P("item", "user", None),
        P(),
        P(),
        P("user", "item", None, None, None),
        P("user", "item", None, None),
        P("user", "item"),
    )
    out_specs = (
        P("user", "item", None),
        P("item", "user", None),
        P("user", "item", None),
        P("item", "user", None),
    )
    return jax.shard_map(
        per_device, mesh=mesh, in_specs=in_specs, out_specs=out_specs, check_vma=False
    )
```

```python
import jax
import jax.numpy as jnp
from jax import lax
from jax.sharding import PartitionSpec as P

DIM = 64
DRAWS = 4
TILE = 256
RB = 3
CB = 4
TMAX = 12
ITERS = 2


top_prec = lax.Precision.HIGHEST
noise_prec = 0.03125


def prior_term(field_vec, prior_mat):
    row_total = field_vec.shape[0]
    grouped = field_vec.reshape(row_total, DRAWS, DIM)
    mixed = jnp.einsum("nde,ef->ndf", grouped, prior_mat, precision=top_prec)
    return mixed.reshape(row_total, DRAWS * DIM)


def per_draw(left, right):
    product = (left * right).reshape(-1, DRAWS, DIM)
    return jnp.sum(product, axis=(0, 2))


def widen(coef):
    return jnp.repeat(coef, DIM)


def bit_count(axis):
    size = lax.axis_size(axis)
    bits = size.bit_length() - 1
    assert size == 1 << bits
    return size, bits


def swap_with(value, axis, size, bit):
    pairs = [(i, i ^ (1 << bit)) for i in range(size)]
    return lax.ppermute(value, axis, pairs)


def butterfly_psum(values):
    values = jnp.stack(values)
    for axis in ("item", "user"):
        size, bits = bit_count(axis)
        for bit in range(bits):
            values = values + swap_with(values, axis, size, bit)
    return values[0], values[1]


def halve_sum(part, axis, send_type, extra=None):
    size, bits = bit_count(axis)
    me = lax.axis_index(axis)
    rows, width = part.shape[0] // size, part.shape[1]
    left = list(range(bits))[::-1]
    buf = part.reshape([2] * bits + [rows, width])
    for bit in range(bits):
        pos = left.index(bit)
        low = lax.index_in_dim(buf, 0, pos, keepdims=False)
        high = lax.index_in_dim(buf, 1, pos, keepdims=False)
        upper = ((me >> bit) & 1) == 1
        keep = jnp.where(upper, high, low)
        send = jnp.where(upper, low, high).astype(send_type)
        if extra is None:
            buf = keep + swap_with(send, axis, size, bit).astype(jnp.float32)
        else:
            got, got_extra = swap_with((send, extra), axis, size, bit)
            buf = keep + got
            extra = extra + got_extra
        left.remove(bit)
    return buf.reshape(rows, width), extra


def double_gather(piece, axis):
    size, bits = bit_count(axis)
    me = lax.axis_index(axis)
    buf = piece[None]
    for step, bit in enumerate(reversed(range(bits))):
        other = swap_with(buf, axis, size, bit)
        upper = ((me >> bit) & 1) == 1
        first = jnp.where(upper, other, buf)
        second = jnp.where(upper, buf, other)
        buf = jnp.stack([first, second], axis=step)
        buf = buf.reshape((-1,) + piece.shape)
        buf = buf.reshape([2] * (step + 1) + list(piece.shape))
    return buf.reshape((size * piece.shape[0],) + piece.shape[1:])


def per_device(
    draws_user, draws_item, prior_user, prior_item, count_tiles, tile_blocks, tile_count
):
    width = DRAWS * DIM
    user_own = draws_user[0]
    item_own = draws_item[0]
    in_use = jnp.arange(TMAX, dtype=jnp.int32) < tile_count[0, 0]
    row_pick = (tile_blocks[0, 0, :, 0][:, None] == jnp.arange(RB, dtype=jnp.int32)) & in_use[:, None]
    col_pick = (tile_blocks[0, 0, :, 1][:, None] == jnp.arange(CB, dtype=jnp.int32)) & in_use[:, None]
    place = (row_pick[:, :, None] & col_pick[:, None, :]).astype(jnp.bfloat16)
    block_counts = jnp.einsum(
        "trc,tij->ricj",
        place,
        count_tiles[0, 0].astype(jnp.bfloat16),
        preferred_element_type=jnp.float32,
    ).reshape(RB * TILE, CB * TILE)
    user_deg = jnp.sum(block_counts, axis=1)
    item_deg = jnp.sum(block_counts, axis=0)
    counts_bf = block_counts.astype(jnp.bfloat16)

    def cross_parts(user_range, item_range):
        to_users = jnp.dot(counts_bf, item_range, preferred_element_type=jnp.float32)
        to_users = to_users + user_deg[:, None] * user_range.astype(jnp.float32)
        to_items = lax.dot_general(
            counts_bf, user_range, (((0,), (0,)), ((), ())), preferred_element_type=jnp.float32
        )
        to_items = to_items + item_deg[:, None] * item_range.astype(jnp.float32)
        return (to_users, to_items)

    def user_range_of(user_vec):
        return lax.all_gather(user_vec.astype(jnp.bfloat16), "item", axis=0, tiled=True)

    def item_range_of(item_vec):
        return double_gather(item_vec.astype(jnp.bfloat16), "user")

    def operate(user_vec, item_vec):
        user_range = user_range_of(user_vec)
        item_range = item_range_of(item_vec)
        part_user, part_item = cross_parts(user_range, item_range)
        prior_user_part = prior_term(user_vec, prior_user)
        prior_item_part = prior_term(item_vec, prior_item)
        norm_part = per_draw(user_vec, user_vec) + per_draw(item_vec, item_vec)
        cross_dot = per_draw(user_range.astype(jnp.float32), part_user) + per_draw(
            item_range.astype(jnp.float32), part_item
        )
        curve_part = (
            per_draw(user_vec, prior_user_part)
            + per_draw(item_vec, prior_item_part)
            + noise_prec * cross_dot
        )
        sums = jnp.concatenate([norm_part, curve_part]).reshape(1, 2 * DRAWS)
        sums = jnp.pad(sums, ((0, 7), (0, width - 2 * DRAWS)))
        total_user, _ = halve_sum(part_user, "item", jnp.bfloat16)
        total_item, sums = halve_sum(part_item, "user", jnp.float32, sums)
        sums = sums[0, : 2 * DRAWS]
        size, bits = bit_count("item")
        for bit in range(bits):
            sums = sums + swap_with(sums, "item", size, bit)
        image_user = prior_user_part + noise_prec * total_user
        image_item = prior_item_part + noise_prec * total_item
        return (image_user, image_item, sums[:DRAWS], sums[DRAWS:])

    sol_user = jnp.zeros_like(user_own)
    sol_item = jnp.zeros_like(item_own)
    res_user, res_item = (user_own, item_own)
    dir_user, dir_item = (user_own, item_own)

    along_user, along_item, norm_now, curve = operate(res_user, res_item)
    step_len = norm_now / curve
    for iteration in range(ITERS):
        sol_user = sol_user + widen(step_len) * dir_user
        sol_item = sol_item + widen(step_len) * dir_item
        res_user = res_user - widen(step_len) * along_user
        res_item = res_item - widen(step_len) * along_item
        if iteration + 1 < ITERS:
            image_user, image_item, norm_next, curve = operate(res_user, res_item)
            beta_coef = norm_next / norm_now
            step_len = norm_next / (curve - beta_coef * norm_next / step_len)
            dir_user = res_user + widen(beta_coef) * dir_user
            dir_item = res_item + widen(beta_coef) * dir_item
            along_user = image_user + widen(beta_coef) * along_user
            along_item = image_item + widen(beta_coef) * along_item
            norm_now = norm_next
    return (sol_user[None], sol_item[None], res_user[None], res_item[None])


def solution(mesh):
    in_specs = (
        P("user", "item", None),
        P("item", "user", None),
        P(),
        P(),
        P("user", "item", None, None, None),
        P("user", "item", None, None),
        P("user", "item"),
    )
    out_specs = (
        P("user", "item", None),
        P("item", "user", None),
        P("user", "item", None),
        P("item", "user", None),
    )
    return jax.shard_map(
        per_device, mesh=mesh, in_specs=in_specs, out_specs=out_specs, check_vma=False
    )
```

```python
import jax
import jax.numpy as jnp
from jax import lax
from jax.sharding import PartitionSpec as P

DIM = 64
DRAWS = 4
TILE = 256
RB = 3
CB = 4
TMAX = 12
ITERS = 2


top_prec = lax.Precision.HIGHEST
noise_prec = 0.03125


def prior_term(field_vec, prior_mat):
    row_total = field_vec.shape[0]
    grouped = field_vec.reshape(row_total, DRAWS, DIM)
    mixed = jnp.einsum("nde,ef->ndf", grouped, prior_mat, precision=top_prec)
    return mixed.reshape(row_total, DRAWS * DIM)


def per_draw(left, right):
    product = (left * right).reshape(-1, DRAWS, DIM)
    return jnp.sum(product, axis=(0, 2))


def widen(coef):
    return jnp.repeat(coef, DIM)


def bit_count(axis):
    size = lax.axis_size(axis)
    bits = size.bit_length() - 1
    assert size == 1 << bits
    return size, bits


def swap_with(value, axis, size, bit, mask=None):
    mask = (1 << bit) if mask is None else mask
    pairs = [(i, i ^ mask) for i in range(size)]
    return lax.ppermute(value, axis, pairs)


def butterfly_psum(values):
    values = jnp.stack(values)
    for axis in ("item", "user"):
        size, bits = bit_count(axis)
        for bit in range(bits):
            values = values + swap_with(values, axis, size, bit)
    return values[0], values[1]


def halve_sum(part, axis, send_type, extra=None):
    size, bits = bit_count(axis)
    me = lax.axis_index(axis)
    rows, width = part.shape[0] // size, part.shape[1]
    left = list(range(bits))[::-1]
    buf = part.reshape([2] * bits + [rows, width])
    for bit in range(bits):
        pos = left.index(bit)
        low = lax.index_in_dim(buf, 0, pos, keepdims=False)
        high = lax.index_in_dim(buf, 1, pos, keepdims=False)
        upper = ((me >> bit) & 1) == 1
        keep = jnp.where(upper, high, low)
        send = jnp.where(upper, low, high).astype(send_type)
        if extra is None:
            buf = keep + swap_with(send, axis, size, bit).astype(jnp.float32)
        else:
            got, got_extra = swap_with((send, extra), axis, size, bit)
            buf = keep + got
            extra = extra + got_extra
        left.remove(bit)
    return buf.reshape(rows, width), extra


def double_gather(piece, axis):
    size, bits = bit_count(axis)
    me = lax.axis_index(axis)
    order = list(range(bits))[::-1]
    groups = [order[:1]] if bits % 2 else []
    groups += [order[i : i + 2] for i in range(bits % 2, bits, 2)]
    buf = piece[None]
    for group in groups:
        masks = [sum(1 << group[-1 - j] for j in range(len(group)) if (k >> j) & 1) for k in range(1 << len(group))]
        pieces = [buf] + [swap_with(buf, axis, size, None, mask) for mask in masks[1:]]
        digit = sum(((me >> group[-1 - j]) & 1) << j for j in range(len(group)))
        ordered = []
        for place in range(len(masks)):
            pick = pieces[place]
            for held in range(1, len(masks)):
                pick = jnp.where(digit == held, pieces[place ^ held], pick)
            ordered.append(pick)
        buf = jnp.stack(ordered, axis=1).reshape((-1,) + piece.shape)
    return buf.reshape((size * piece.shape[0],) + piece.shape[1:])

def per_device(
    draws_user, draws_item, prior_user, prior_item, count_tiles, tile_blocks, tile_count
):
    width = DRAWS * DIM
    user_own = draws_user[0]
    item_own = draws_item[0]
    in_use = jnp.arange(TMAX, dtype=jnp.int32) < tile_count[0, 0]
    row_pick = (tile_blocks[0, 0, :, 0][:, None] == jnp.arange(RB, dtype=jnp.int32)) & in_use[:, None]
    col_pick = (tile_blocks[0, 0, :, 1][:, None] == jnp.arange(CB, dtype=jnp.int32)) & in_use[:, None]
    place = (row_pick[:, :, None] & col_pick[:, None, :]).astype(jnp.bfloat16)
    block_counts = jnp.einsum(
        "trc,tij->ricj",
        place,
        count_tiles[0, 0].astype(jnp.bfloat16),
        preferred_element_type=jnp.float32,
    ).reshape(RB * TILE, CB * TILE)
    user_deg = jnp.sum(block_counts, axis=1)
    item_deg = jnp.sum(block_counts, axis=0)
    counts_bf = block_counts.astype(jnp.bfloat16)

    def cross_parts(user_range, item_range):
        to_users = jnp.dot(counts_bf, item_range, preferred_element_type=jnp.float32)
        to_users = to_users + user_deg[:, None] * user_range.astype(jnp.float32)
        to_items = lax.dot_general(
            counts_bf, user_range, (((0,), (0,)), ((), ())), preferred_element_type=jnp.float32
        )
        to_items = to_items + item_deg[:, None] * item_range.astype(jnp.float32)
        return (to_users, to_items)

    def user_range_of(user_vec):
        return double_gather(user_vec.astype(jnp.bfloat16), "item")

    def item_range_of(item_vec):
        return double_gather(item_vec.astype(jnp.bfloat16), "user")

    def operate(user_vec, item_vec):
        user_range = user_range_of(user_vec)
        item_range = item_range_of(item_vec)
        part_user, part_item = cross_parts(user_range, item_range)
        prior_user_part = prior_term(user_vec, prior_user)
        prior_item_part = prior_term(item_vec, prior_item)
        norm_part = per_draw(user_vec, user_vec) + per_draw(item_vec, item_vec)
        cross_dot = per_draw(user_range.astype(jnp.float32), part_user) + per_draw(
            item_range.astype(jnp.float32), part_item
        )
        curve_part = (
            per_draw(user_vec, prior_user_part)
            + per_draw(item_vec, prior_item_part)
            + noise_prec * cross_dot
        )
        sums = jnp.concatenate([norm_part, curve_part]).reshape(1, 2 * DRAWS)
        sums = jnp.pad(sums, ((0, 7), (0, width - 2 * DRAWS)))
        total_user, _ = halve_sum(part_user, "item", jnp.bfloat16)
        total_item, sums = halve_sum(part_item, "user", jnp.float32, sums)
        sums = sums[0, : 2 * DRAWS]
        size, bits = bit_count("item")
        for bit in range(bits):
            sums = sums + swap_with(sums, "item", size, bit)
        image_user = prior_user_part + noise_prec * total_user
        image_item = prior_item_part + noise_prec * total_item
        return (image_user, image_item, sums[:DRAWS], sums[DRAWS:])

    sol_user = jnp.zeros_like(user_own)
    sol_item = jnp.zeros_like(item_own)
    res_user, res_item = (user_own, item_own)
    dir_user, dir_item = (user_own, item_own)

    along_user, along_item, norm_now, curve = operate(res_user, res_item)
    step_len = norm_now / curve
    for iteration in range(ITERS):
        sol_user = sol_user + widen(step_len) * dir_user
        sol_item = sol_item + widen(step_len) * dir_item
        res_user = res_user - widen(step_len) * along_user
        res_item = res_item - widen(step_len) * along_item
        if iteration + 1 < ITERS:
            image_user, image_item, norm_next, curve = operate(res_user, res_item)
            beta_coef = norm_next / norm_now
            step_len = norm_next / (curve - beta_coef * norm_next / step_len)
            dir_user = res_user + widen(beta_coef) * dir_user
            dir_item = res_item + widen(beta_coef) * dir_item
            along_user = image_user + widen(beta_coef) * along_user
            along_item = image_item + widen(beta_coef) * along_item
            norm_now = norm_next
    return (sol_user[None], sol_item[None], res_user[None], res_item[None])


def solution(mesh):
    in_specs = (
        P("user", "item", None),
        P("item", "user", None),
        P(),
        P(),
        P("user", "item", None, None, None),
        P("user", "item", None, None),
        P("user", "item"),
    )
    out_specs = (
        P("user", "item", None),
        P("item", "user", None),
        P("user", "item", None),
        P("item", "user", None),
    )
    return jax.shard_map(
        per_device, mesh=mesh, in_specs=in_specs, out_specs=out_specs, check_vma=False
    )
```

```python
import jax
import jax.numpy as jnp
from jax import lax
from jax.sharding import PartitionSpec as P

DIM = 64
DRAWS = 4
TILE = 256
RB = 3
CB = 4
TMAX = 12
ITERS = 2


top_prec = lax.Precision.HIGHEST
noise_prec = 0.03125


def prior_term(field_vec, prior_mat):
    row_total = field_vec.shape[0]
    grouped = field_vec.reshape(row_total, DRAWS, DIM)
    mixed = jnp.einsum("nde,ef->ndf", grouped, prior_mat, precision=top_prec)
    return mixed.reshape(row_total, DRAWS * DIM)


def per_draw(left, right):
    product = (left * right).reshape(-1, DRAWS, DIM)
    return jnp.sum(product, axis=(0, 2))


def widen(coef):
    return jnp.repeat(coef, DIM)


def bit_count(axis):
    size = lax.axis_size(axis)
    bits = size.bit_length() - 1
    assert size == 1 << bits
    return size, bits


def swap_with(value, axis, size, bit, mask=None):
    mask = (1 << bit) if mask is None else mask
    pairs = [(i, i ^ mask) for i in range(size)]
    return lax.ppermute(value, axis, pairs)


def butterfly_psum(values):
    values = jnp.stack(values)
    for axis in ("item", "user"):
        size, bits = bit_count(axis)
        for bit in range(bits):
            values = values + swap_with(values, axis, size, bit)
    return values[0], values[1]


def halve_sum(part, axis, send_type, extra=None):
    size, bits = bit_count(axis)
    me = lax.axis_index(axis)
    rows, width = part.shape[0] // size, part.shape[1]
    groups = [list(range(bits))[i : i + 2] for i in range(0, bits, 2)]
    left = list(range(bits))[::-1]
    buf = part.reshape([2] * bits + [rows, width])
    for group in groups:
        masks = [sum(1 << group[j] for j in range(len(group)) if (k >> j) & 1) for k in range(1 << len(group))]
        digit = sum(((me >> group[j]) & 1) << j for j in range(len(group)))

        def block_of(value):
            out = buf
            for j in sorted(range(len(group)), key=lambda j: -left.index(group[j])):
                out = lax.dynamic_index_in_dim(out, (value >> j) & 1, left.index(group[j]), keepdims=False)
            return out

        total = block_of(digit)
        sent_extra = extra
        for k in range(1, len(masks)):
            send = block_of(digit ^ k).astype(send_type)
            if extra is None:
                total = total + swap_with(send, axis, size, None, masks[k]).astype(jnp.float32)
            else:
                message = jnp.concatenate([send.reshape(-1, width), sent_extra])
                got = swap_with(message, axis, size, None, masks[k])
                total = total + got[: -extra.shape[0]].reshape(total.shape)
                extra = extra + got[-extra.shape[0] :]
        for bit in group:
            left.remove(bit)
        buf = total
    return buf.reshape(rows, width), extra


def double_gather(piece, axis):
    size, bits = bit_count(axis)
    me = lax.axis_index(axis)
    order = list(range(bits))[::-1]
    groups = [order[:1]] if bits % 2 else []
    groups += [order[i : i + 2] for i in range(bits % 2, bits, 2)]
    buf = piece[None]
    for group in groups:
        masks = [sum(1 << group[-1 - j] for j in range(len(group)) if (k >> j) & 1) for k in range(1 << len(group))]
        pieces = [buf] + [swap_with(buf, axis, size, None, mask) for mask in masks[1:]]
        digit = sum(((me >> group[-1 - j]) & 1) << j for j in range(len(group)))
        ordered = []
        for place in range(len(masks)):
            pick = pieces[place]
            for held in range(1, len(masks)):
                pick = jnp.where(digit == held, pieces[place ^ held], pick)
            ordered.append(pick)
        buf = jnp.stack(ordered, axis=1).reshape((-1,) + piece.shape)
    return buf.reshape((size * piece.shape[0],) + piece.shape[1:])

def per_device(
    draws_user, draws_item, prior_user, prior_item, count_tiles, tile_blocks, tile_count
):
    width = DRAWS * DIM
    user_own = draws_user[0]
    item_own = draws_item[0]
    in_use = jnp.arange(TMAX, dtype=jnp.int32) < tile_count[0, 0]
    row_pick = (tile_blocks[0, 0, :, 0][:, None] == jnp.arange(RB, dtype=jnp.int32)) & in_use[:, None]
    col_pick = (tile_blocks[0, 0, :, 1][:, None] == jnp.arange(CB, dtype=jnp.int32)) & in_use[:, None]
    place = (row_pick[:, :, None] & col_pick[:, None, :]).astype(jnp.bfloat16)
    block_counts = jnp.einsum(
        "trc,tij->ricj",
        place,
        count_tiles[0, 0].astype(jnp.bfloat16),
        preferred_element_type=jnp.float32,
    ).reshape(RB * TILE, CB * TILE)
    user_deg = jnp.sum(block_counts, axis=1)
    item_deg = jnp.sum(block_counts, axis=0)
    counts_bf = block_counts.astype(jnp.bfloat16)

    def cross_parts(user_range, item_range):
        to_users = jnp.dot(counts_bf, item_range, preferred_element_type=jnp.float32)
        to_users = to_users + user_deg[:, None] * user_range.astype(jnp.float32)
        to_items = lax.dot_general(
            counts_bf, user_range, (((0,), (0,)), ((), ())), preferred_element_type=jnp.float32
        )
        to_items = to_items + item_deg[:, None] * item_range.astype(jnp.float32)
        return (to_users, to_items)

    def user_range_of(user_vec):
        return double_gather(user_vec.astype(jnp.bfloat16), "item")

    def item_range_of(item_vec):
        return double_gather(item_vec.astype(jnp.bfloat16), "user")

    def operate(user_vec, item_vec):
        user_range = user_range_of(user_vec)
        item_range = item_range_of(item_vec)
        part_user, part_item = cross_parts(user_range, item_range)
        prior_user_part = prior_term(user_vec, prior_user)
        prior_item_part = prior_term(item_vec, prior_item)
        norm_part = per_draw(user_vec, user_vec) + per_draw(item_vec, item_vec)
        cross_dot = per_draw(user_range.astype(jnp.float32), part_user) + per_draw(
            item_range.astype(jnp.float32), part_item
        )
        curve_part = (
            per_draw(user_vec, prior_user_part)
            + per_draw(item_vec, prior_item_part)
            + noise_prec * cross_dot
        )
        sums = jnp.concatenate([norm_part, curve_part]).reshape(1, 2 * DRAWS)
        sums = jnp.pad(sums, ((0, 7), (0, width - 2 * DRAWS)))
        total_user, _ = halve_sum(part_user, "item", jnp.bfloat16)
        total_item, sums = halve_sum(part_item, "user", jnp.float32, sums)
        sums = sums[0, : 2 * DRAWS]
        size, bits = bit_count("item")
        for bit in range(bits):
            sums = sums + swap_with(sums, "item", size, bit)
        image_user = prior_user_part + noise_prec * total_user
        image_item = prior_item_part + noise_prec * total_item
        return (image_user, image_item, sums[:DRAWS], sums[DRAWS:])

    sol_user = jnp.zeros_like(user_own)
    sol_item = jnp.zeros_like(item_own)
    res_user, res_item = (user_own, item_own)
    dir_user, dir_item = (user_own, item_own)

    along_user, along_item, norm_now, curve = operate(res_user, res_item)
    step_len = norm_now / curve
    for iteration in range(ITERS):
        sol_user = sol_user + widen(step_len) * dir_user
        sol_item = sol_item + widen(step_len) * dir_item
        res_user = res_user - widen(step_len) * along_user
        res_item = res_item - widen(step_len) * along_item
        if iteration + 1 < ITERS:
            image_user, image_item, norm_next, curve = operate(res_user, res_item)
            beta_coef = norm_next / norm_now
            step_len = norm_next / (curve - beta_coef * norm_next / step_len)
            dir_user = res_user + widen(beta_coef) * dir_user
            dir_item = res_item + widen(beta_coef) * dir_item
            along_user = image_user + widen(beta_coef) * along_user
            along_item = image_item + widen(beta_coef) * along_item
            norm_now = norm_next
    return (sol_user[None], sol_item[None], res_user[None], res_item[None])


def solution(mesh):
    in_specs = (
        P("user", "item", None),
        P("item", "user", None),
        P(),
        P(),
        P("user", "item", None, None, None),
        P("user", "item", None, None),
        P("user", "item"),
    )
    out_specs = (
        P("user", "item", None),
        P("item", "user", None),
        P("user", "item", None),
        P("item", "user", None),
    )
    return jax.shard_map(
        per_device, mesh=mesh, in_specs=in_specs, out_specs=out_specs, check_vma=False
    )
```

```python
import jax
import jax.numpy as jnp
from jax import lax
from jax.sharding import PartitionSpec as P

DIM = 64
DRAWS = 4
TILE = 256
RB = 3
CB = 4
TMAX = 12
ITERS = 2


top_prec = lax.Precision.HIGHEST
noise_prec = 0.03125


def prior_term(field_vec, prior_mat):
    row_total = field_vec.shape[0]
    grouped = field_vec.reshape(row_total, DRAWS, DIM)
    mixed = jnp.einsum("nde,ef->ndf", grouped, prior_mat, precision=top_prec)
    return mixed.reshape(row_total, DRAWS * DIM)


def per_draw(left, right):
    product = (left * right).reshape(-1, DRAWS, DIM)
    return jnp.sum(product, axis=(0, 2))


def widen(coef):
    return jnp.repeat(coef, DIM)


def bit_count(axis):
    size = lax.axis_size(axis)
    bits = size.bit_length() - 1
    assert size == 1 << bits
    return size, bits


def swap_with(value, axis, size, bit, mask=None):
    mask = (1 << bit) if mask is None else mask
    pairs = [(i, i ^ mask) for i in range(size)]
    return lax.ppermute(value, axis, pairs)


def butterfly_psum(values):
    values = jnp.stack(values)
    for axis in ("item", "user"):
        size, bits = bit_count(axis)
        for bit in range(bits):
            values = values + swap_with(values, axis, size, bit)
    return values[0], values[1]


def halve_sum(part, axis, send_type, extra=None):
    size, bits = bit_count(axis)
    me = lax.axis_index(axis)
    rows, width = part.shape[0] // size, part.shape[1]
    groups = [list(range(bits))[i : i + 2] for i in range(0, bits, 2)]
    left = list(range(bits))[::-1]
    buf = part.reshape([2] * bits + [rows, width])
    for group in groups:
        masks = [sum(1 << group[j] for j in range(len(group)) if (k >> j) & 1) for k in range(1 << len(group))]
        digit = sum(((me >> group[j]) & 1) << j for j in range(len(group)))

        def block_of(value):
            out = buf
            for j in sorted(range(len(group)), key=lambda j: -left.index(group[j])):
                out = lax.dynamic_index_in_dim(out, (value >> j) & 1, left.index(group[j]), keepdims=False)
            return out

        total = block_of(digit)
        shape = total.shape
        if extra is not None:
            total = jnp.concatenate([total.reshape(-1, width), extra])
        for k in range(1, len(masks)):
            send = block_of(digit ^ k).astype(send_type)
            if extra is not None:
                send = jnp.concatenate([send.reshape(-1, width), extra])
            total = total + swap_with(send, axis, size, None, masks[k]).astype(jnp.float32)
        if extra is not None:
            extra = total[-extra.shape[0] :]
            total = total[: -extra.shape[0]].reshape(shape)
        for bit in group:
            left.remove(bit)
        buf = total
    return buf.reshape(rows, width), extra


def double_gather(piece, axis):
    size, bits = bit_count(axis)
    me = lax.axis_index(axis)
    order = list(range(bits))[::-1]
    groups = [order[:1]] if bits % 2 else []
    groups += [order[i : i + 2] for i in range(bits % 2, bits, 2)]
    buf = piece[None]
    for group in groups:
        masks = [sum(1 << group[-1 - j] for j in range(len(group)) if (k >> j) & 1) for k in range(1 << len(group))]
        pieces = [buf] + [swap_with(buf, axis, size, None, mask) for mask in masks[1:]]
        digit = sum(((me >> group[-1 - j]) & 1) << j for j in range(len(group)))
        ordered = []
        for place in range(len(masks)):
            pick = pieces[place]
            for held in range(1, len(masks)):
                pick = jnp.where(digit == held, pieces[place ^ held], pick)
            ordered.append(pick)
        buf = jnp.stack(ordered, axis=1).reshape((-1,) + piece.shape)
    return buf.reshape((size * piece.shape[0],) + piece.shape[1:])

def per_device(
    draws_user, draws_item, prior_user, prior_item, count_tiles, tile_blocks, tile_count
):
    width = DRAWS * DIM
    user_own = draws_user[0]
    item_own = draws_item[0]
    in_use = jnp.arange(TMAX, dtype=jnp.int32) < tile_count[0, 0]
    row_pick = (tile_blocks[0, 0, :, 0][:, None] == jnp.arange(RB, dtype=jnp.int32)) & in_use[:, None]
    col_pick = (tile_blocks[0, 0, :, 1][:, None] == jnp.arange(CB, dtype=jnp.int32)) & in_use[:, None]
    place = (row_pick[:, :, None] & col_pick[:, None, :]).astype(jnp.bfloat16)
    tiles_bf = count_tiles[0, 0].astype(jnp.bfloat16)
    counts_bf = jnp.einsum(
        "trc,tij->ricj", place, tiles_bf, preferred_element_type=jnp.bfloat16
    ).reshape(RB * TILE, CB * TILE)
    tile_rows = jnp.sum(tiles_bf, axis=2, dtype=jnp.float32)
    tile_cols = jnp.sum(tiles_bf, axis=1, dtype=jnp.float32)
    user_deg = jnp.sum(jnp.where(row_pick[:, :, None], tile_rows[:, None, :], 0.0), axis=0).reshape(-1)
    item_deg = jnp.sum(jnp.where(col_pick[:, :, None], tile_cols[:, None, :], 0.0), axis=0).reshape(-1)

    def cross_parts(user_range, item_range):
        to_users = jnp.dot(counts_bf, item_range, preferred_element_type=jnp.float32)
        to_users = to_users + user_deg[:, None] * user_range.astype(jnp.float32)
        to_items = lax.dot_general(
            counts_bf, user_range, (((0,), (0,)), ((), ())), preferred_element_type=jnp.float32
        )
        to_items = to_items + item_deg[:, None] * item_range.astype(jnp.float32)
        return (to_users, to_items)

    def user_range_of(user_vec):
        return double_gather(user_vec.astype(jnp.bfloat16), "item")

    def item_range_of(item_vec):
        return double_gather(item_vec.astype(jnp.bfloat16), "user")

    def operate(user_vec, item_vec):
        user_range = user_range_of(user_vec)
        item_range = item_range_of(item_vec)
        part_user, part_item = cross_parts(user_range, item_range)
        prior_user_part = prior_term(user_vec, prior_user)
        prior_item_part = prior_term(item_vec, prior_item)
        norm_part = per_draw(user_vec, user_vec) + per_draw(item_vec, item_vec)
        cross_dot = per_draw(user_range.astype(jnp.float32), part_user) + per_draw(
            item_range.astype(jnp.float32), part_item
        )
        curve_part = (
            per_draw(user_vec, prior_user_part)
            + per_draw(item_vec, prior_item_part)
            + noise_prec * cross_dot
        )
        sums = jnp.concatenate([norm_part, curve_part]).reshape(1, 2 * DRAWS)
        sums = jnp.pad(sums, ((0, 7), (0, width - 2 * DRAWS)))
        total_user, _ = halve_sum(part_user, "item", jnp.bfloat16)
        total_item, sums = halve_sum(part_item, "user", jnp.float32, sums)
        sums = sums[0, : 2 * DRAWS]
        size, bits = bit_count("item")
        for bit in range(bits):
            sums = sums + swap_with(sums, "item", size, bit)
        image_user = prior_user_part + noise_prec * total_user
        image_item = prior_item_part + noise_prec * total_item
        return (image_user, image_item, sums[:DRAWS], sums[DRAWS:])

    sol_user = jnp.zeros_like(user_own)
    sol_item = jnp.zeros_like(item_own)
    res_user, res_item = (user_own, item_own)
    dir_user, dir_item = (user_own, item_own)

    along_user, along_item, norm_now, curve = operate(res_user, res_item)
    step_len = norm_now / curve
    for iteration in range(ITERS):
        sol_user = sol_user + widen(step_len) * dir_user
        sol_item = sol_item + widen(step_len) * dir_item
        res_user = res_user - widen(step_len) * along_user
        res_item = res_item - widen(step_len) * along_item
        if iteration + 1 < ITERS:
            image_user, image_item, norm_next, curve = operate(res_user, res_item)
            beta_coef = norm_next / norm_now
            step_len = norm_next / (curve - beta_coef * norm_next / step_len)
            dir_user = res_user + widen(beta_coef) * dir_user
            dir_item = res_item + widen(beta_coef) * dir_item
            along_user = image_user + widen(beta_coef) * along_user
            along_item = image_item + widen(beta_coef) * along_item
            norm_now = norm_next
    return (sol_user[None], sol_item[None], res_user[None], res_item[None])


def solution(mesh):
    in_specs = (
        P("user", "item", None),
        P("item", "user", None),
        P(),
        P(),
        P("user", "item", None, None, None),
        P("user", "item", None, None),
        P("user", "item"),
    )
    out_specs = (
        P("user", "item", None),
        P("item", "user", None),
        P("user", "item", None),
        P("item", "user", None),
    )
    return jax.shard_map(
        per_device, mesh=mesh, in_specs=in_specs, out_specs=out_specs, check_vma=False
    )
```

```python
import jax
import jax.numpy as jnp
from jax import lax
from jax.sharding import PartitionSpec as P

DIM = 64
DRAWS = 4
TILE = 256
RB = 3
CB = 4
TMAX = 12
ITERS = 2


top_prec = lax.Precision.HIGHEST
noise_prec = 0.03125


def prior_term(field_vec, prior_mat):
    per_draw_block = jnp.kron(jnp.eye(DRAWS, dtype=prior_mat.dtype), prior_mat)
    return jnp.dot(field_vec, per_draw_block, precision=top_prec)


def per_draw(left, right):
    column_sums = jnp.sum(left * right, axis=0)
    return jnp.sum(column_sums.reshape(DRAWS, DIM), axis=1)


def widen(coef):
    return jnp.repeat(coef, DIM)


def bit_count(axis):
    size = lax.axis_size(axis)
    bits = size.bit_length() - 1
    assert size == 1 << bits
    return size, bits


def swap_with(value, axis, size, bit, mask=None):
    mask = (1 << bit) if mask is None else mask
    pairs = [(i, i ^ mask) for i in range(size)]
    return lax.ppermute(value, axis, pairs)


def butterfly_psum(values):
    values = jnp.stack(values)
    for axis in ("item", "user"):
        size, bits = bit_count(axis)
        for bit in range(bits):
            values = values + swap_with(values, axis, size, bit)
    return values[0], values[1]


def halve_sum(part, axis, send_type, extra=None):
    size, bits = bit_count(axis)
    me = lax.axis_index(axis)
    rows, width = part.shape[0] // size, part.shape[1]
    groups = [list(range(bits))[i : i + 2] for i in range(0, bits, 2)]
    left = list(range(bits))[::-1]
    buf = part.reshape([2] * bits + [rows, width])
    for group in groups:
        masks = [sum(1 << group[j] for j in range(len(group)) if (k >> j) & 1) for k in range(1 << len(group))]
        digit = sum(((me >> group[j]) & 1) << j for j in range(len(group)))

        def block_of(value):
            out = buf
            for j in sorted(range(len(group)), key=lambda j: -left.index(group[j])):
                out = lax.dynamic_index_in_dim(out, (value >> j) & 1, left.index(group[j]), keepdims=False)
            return out

        total = block_of(digit)
        shape = total.shape
        if extra is not None:
            total = jnp.concatenate([total.reshape(-1, width), extra])
        for k in range(1, len(masks)):
            send = block_of(digit ^ k).astype(send_type)
            if extra is not None:
                send = jnp.concatenate([send.reshape(-1, width), extra])
            total = total + swap_with(send, axis, size, None, masks[k]).astype(jnp.float32)
        if extra is not None:
            extra = total[-extra.shape[0] :]
            total = total[: -extra.shape[0]].reshape(shape)
        for bit in group:
            left.remove(bit)
        buf = total
    return buf.reshape(rows, width), extra


def double_gather(piece, axis):
    size, bits = bit_count(axis)
    me = lax.axis_index(axis)
    order = list(range(bits))[::-1]
    groups = [order[:1]] if bits % 2 else []
    groups += [order[i : i + 2] for i in range(bits % 2, bits, 2)]
    buf = piece[None]
    for group in groups:
        masks = [sum(1 << group[-1 - j] for j in range(len(group)) if (k >> j) & 1) for k in range(1 << len(group))]
        pieces = [buf] + [swap_with(buf, axis, size, None, mask) for mask in masks[1:]]
        digit = sum(((me >> group[-1 - j]) & 1) << j for j in range(len(group)))
        ordered = []
        for place in range(len(masks)):
            pick = pieces[place]
            for held in range(1, len(masks)):
                pick = jnp.where(digit == held, pieces[place ^ held], pick)
            ordered.append(pick)
        buf = jnp.stack(ordered, axis=1).reshape((-1,) + piece.shape)
    return buf.reshape((size * piece.shape[0],) + piece.shape[1:])

def per_device(
    draws_user, draws_item, prior_user, prior_item, count_tiles, tile_blocks, tile_count
):
    width = DRAWS * DIM
    user_own = draws_user[0]
    item_own = draws_item[0]
    in_use = jnp.arange(TMAX, dtype=jnp.int32) < tile_count[0, 0]
    row_pick = (tile_blocks[0, 0, :, 0][:, None] == jnp.arange(RB, dtype=jnp.int32)) & in_use[:, None]
    col_pick = (tile_blocks[0, 0, :, 1][:, None] == jnp.arange(CB, dtype=jnp.int32)) & in_use[:, None]
    place = (row_pick[:, :, None] & col_pick[:, None, :]).astype(jnp.bfloat16)
    tiles_bf = count_tiles[0, 0].astype(jnp.bfloat16)
    counts_bf = jnp.einsum(
        "trc,tij->ricj", place, tiles_bf, preferred_element_type=jnp.bfloat16
    ).reshape(RB * TILE, CB * TILE)
    tile_rows = jnp.sum(tiles_bf, axis=2, dtype=jnp.float32)
    tile_cols = jnp.sum(tiles_bf, axis=1, dtype=jnp.float32)
    user_deg = jnp.sum(jnp.where(row_pick[:, :, None], tile_rows[:, None, :], 0.0), axis=0).reshape(-1)
    item_deg = jnp.sum(jnp.where(col_pick[:, :, None], tile_cols[:, None, :], 0.0), axis=0).reshape(-1)

    def cross_parts(user_range, item_range):
        to_users = jnp.dot(counts_bf, item_range, preferred_element_type=jnp.float32)
        to_users = to_users + user_deg[:, None] * user_range.astype(jnp.float32)
        to_items = lax.dot_general(
            counts_bf, user_range, (((0,), (0,)), ((), ())), preferred_element_type=jnp.float32
        )
        to_items = to_items + item_deg[:, None] * item_range.astype(jnp.float32)
        return (to_users, to_items)

    def user_range_of(user_vec):
        return double_gather(user_vec.astype(jnp.bfloat16), "item")

    def item_range_of(item_vec):
        return double_gather(item_vec.astype(jnp.bfloat16), "user")

    def operate(user_vec, item_vec):
        user_range = user_range_of(user_vec)
        item_range = item_range_of(item_vec)
        part_user, part_item = cross_parts(user_range, item_range)
        prior_user_part = prior_term(user_vec, prior_user)
        prior_item_part = prior_term(item_vec, prior_item)
        norm_part = per_draw(user_vec, user_vec) + per_draw(item_vec, item_vec)
        cross_dot = per_draw(user_range.astype(jnp.float32), part_user) + per_draw(
            item_range.astype(jnp.float32), part_item
        )
        curve_part = (
            per_draw(user_vec, prior_user_part)
            + per_draw(item_vec, prior_item_part)
            + noise_prec * cross_dot
        )
        sums = jnp.concatenate([norm_part, curve_part]).reshape(1, 2 * DRAWS)
        sums = jnp.pad(sums, ((0, 7), (0, width - 2 * DRAWS)))
        total_user, _ = halve_sum(part_user, "item", jnp.bfloat16)
        total_item, sums = halve_sum(part_item, "user", jnp.float32, sums)
        sums = sums[0, : 2 * DRAWS]
        size, bits = bit_count("item")
        for bit in range(bits):
            sums = sums + swap_with(sums, "item", size, bit)
        image_user = prior_user_part + noise_prec * total_user
        image_item = prior_item_part + noise_prec * total_item
        return (image_user, image_item, sums[:DRAWS], sums[DRAWS:])

    sol_user = jnp.zeros_like(user_own)
    sol_item = jnp.zeros_like(item_own)
    res_user, res_item = (user_own, item_own)
    dir_user, dir_item = (user_own, item_own)

    along_user, along_item, norm_now, curve = operate(res_user, res_item)
    step_len = norm_now / curve
    for iteration in range(ITERS):
        sol_user = sol_user + widen(step_len) * dir_user
        sol_item = sol_item + widen(step_len) * dir_item
        res_user = res_user - widen(step_len) * along_user
        res_item = res_item - widen(step_len) * along_item
        if iteration + 1 < ITERS:
            image_user, image_item, norm_next, curve = operate(res_user, res_item)
            beta_coef = norm_next / norm_now
            step_len = norm_next / (curve - beta_coef * norm_next / step_len)
            dir_user = res_user + widen(beta_coef) * dir_user
            dir_item = res_item + widen(beta_coef) * dir_item
            along_user = image_user + widen(beta_coef) * along_user
            along_item = image_item + widen(beta_coef) * along_item
            norm_now = norm_next
    return (sol_user[None], sol_item[None], res_user[None], res_item[None])


def solution(mesh):
    in_specs = (
        P("user", "item", None),
        P("item", "user", None),
        P(),
        P(),
        P("user", "item", None, None, None),
        P("user", "item", None, None),
        P("user", "item"),
    )
    out_specs = (
        P("user", "item", None),
        P("item", "user", None),
        P("user", "item", None),
        P("item", "user", None),
    )
    return jax.shard_map(
        per_device, mesh=mesh, in_specs=in_specs, out_specs=out_specs, check_vma=False
    )
```

```python
import jax
import jax.numpy as jnp
from jax import lax
from jax.sharding import PartitionSpec as P

DIM = 64
DRAWS = 4
TILE = 256
RB = 3
CB = 4
TMAX = 12
ITERS = 2


top_prec = lax.Precision.HIGHEST
noise_prec = 0.03125


def prior_term(field_vec, prior_mat):
    row_total = field_vec.shape[0]
    grouped = field_vec.reshape(row_total, DRAWS, DIM)
    mixed = jnp.einsum("nde,ef->ndf", grouped, prior_mat, precision=top_prec)
    return mixed.reshape(row_total, DRAWS * DIM)


def per_draw(left, right):
    product = (left * right).reshape(-1, DRAWS, DIM)
    return jnp.sum(product, axis=(0, 2))


def widen(coef):
    return jnp.repeat(coef, DIM)


def bit_count(axis):
    size = lax.axis_size(axis)
    bits = size.bit_length() - 1
    assert size == 1 << bits
    return size, bits


def swap_with(value, axis, size, bit, mask=None):
    mask = (1 << bit) if mask is None else mask
    pairs = [(i, i ^ mask) for i in range(size)]
    return lax.ppermute(value, axis, pairs)


def butterfly_psum(values):
    values = jnp.stack(values)
    for axis in ("item", "user"):
        size, bits = bit_count(axis)
        for bit in range(bits):
            values = values + swap_with(values, axis, size, bit)
    return values[0], values[1]


def code_rows(extra):
    high = extra.astype(jnp.bfloat16)
    rest = extra - high.astype(jnp.float32)
    mid = rest.astype(jnp.bfloat16)
    low = (rest - mid.astype(jnp.float32)).astype(jnp.bfloat16)
    return jnp.concatenate([high, mid, low])


def halve_sum(part, axis, send_type, extra=None, first_type=None):
    size, bits = bit_count(axis)
    me = lax.axis_index(axis)
    rows, width = part.shape[0] // size, part.shape[1]
    groups = [list(range(bits))[i : i + 2] for i in range(0, bits, 2)]
    left = list(range(bits))[::-1]
    buf = part.reshape([2] * bits + [rows, width])
    for stage, group in enumerate(groups):
        masks = [sum(1 << group[j] for j in range(len(group)) if (k >> j) & 1) for k in range(1 << len(group))]
        digit = sum(((me >> group[j]) & 1) << j for j in range(len(group)))

        def block_of(value):
            out = buf
            for j in sorted(range(len(group)), key=lambda j: -left.index(group[j])):
                out = lax.dynamic_index_in_dim(out, (value >> j) & 1, left.index(group[j]), keepdims=False)
            return out

        coded = extra is not None and stage == 0 and first_type is not None
        stage_type = first_type if (stage == 0 and first_type is not None) else send_type
        total = block_of(digit)
        shape = total.shape
        if extra is not None:
            tail = jnp.concatenate([extra, jnp.zeros((2 * extra.shape[0], width), extra.dtype)]) if coded else extra
            total = jnp.concatenate([total.reshape(-1, width), tail])
        for k in range(1, len(masks)):
            send = block_of(digit ^ k).astype(stage_type)
            if extra is not None:
                tail = code_rows(extra) if coded else extra
                send = jnp.concatenate([send.reshape(-1, width), tail.astype(stage_type)])
            total = total + swap_with(send, axis, size, None, masks[k]).astype(jnp.float32)
        if extra is not None:
            count = extra.shape[0]
            if coded:
                tail = total[-3 * count :]
                total = total[: -3 * count].reshape(shape)
                extra = tail[:count] + tail[count : 2 * count] + tail[2 * count :]
            else:
                extra = total[-count:]
                total = total[:-count].reshape(shape)
        for bit in group:
            left.remove(bit)
        buf = total
    return buf.reshape(rows, width), extra


def double_gather(piece, axis):
    size, bits = bit_count(axis)
    me = lax.axis_index(axis)
    order = list(range(bits))[::-1]
    groups = [order[:1]] if bits % 2 else []
    groups += [order[i : i + 2] for i in range(bits % 2, bits, 2)]
    buf = piece[None]
    for group in groups:
        masks = [sum(1 << group[-1 - j] for j in range(len(group)) if (k >> j) & 1) for k in range(1 << len(group))]
        pieces = [buf] + [swap_with(buf, axis, size, None, mask) for mask in masks[1:]]
        digit = sum(((me >> group[-1 - j]) & 1) << j for j in range(len(group)))
        ordered = []
        for place in range(len(masks)):
            pick = pieces[place]
            for held in range(1, len(masks)):
                pick = jnp.where(digit == held, pieces[place ^ held], pick)
            ordered.append(pick)
        buf = jnp.stack(ordered, axis=1).reshape((-1,) + piece.shape)
    return buf.reshape((size * piece.shape[0],) + piece.shape[1:])

def per_device(
    draws_user, draws_item, prior_user, prior_item, count_tiles, tile_blocks, tile_count
):
    width = DRAWS * DIM
    user_own = draws_user[0]
    item_own = draws_item[0]
    in_use = jnp.arange(TMAX, dtype=jnp.int32) < tile_count[0, 0]
    row_pick = (tile_blocks[0, 0, :, 0][:, None] == jnp.arange(RB, dtype=jnp.int32)) & in_use[:, None]
    col_pick = (tile_blocks[0, 0, :, 1][:, None] == jnp.arange(CB, dtype=jnp.int32)) & in_use[:, None]
    place = (row_pick[:, :, None] & col_pick[:, None, :]).astype(jnp.bfloat16)
    tiles_bf = count_tiles[0, 0].astype(jnp.bfloat16)
    counts_bf = jnp.einsum(
        "trc,tij->ricj", place, tiles_bf, preferred_element_type=jnp.bfloat16
    ).reshape(RB * TILE, CB * TILE)
    tile_rows = jnp.sum(tiles_bf, axis=2, dtype=jnp.float32)
    tile_cols = jnp.sum(tiles_bf, axis=1, dtype=jnp.float32)
    user_deg = jnp.sum(jnp.where(row_pick[:, :, None], tile_rows[:, None, :], 0.0), axis=0).reshape(-1)
    item_deg = jnp.sum(jnp.where(col_pick[:, :, None], tile_cols[:, None, :], 0.0), axis=0).reshape(-1)

    def cross_parts(user_range, item_range):
        to_users = jnp.dot(counts_bf, item_range, preferred_element_type=jnp.float32)
        to_users = to_users + user_deg[:, None] * user_range.astype(jnp.float32)
        to_items = lax.dot_general(
            counts_bf, user_range, (((0,), (0,)), ((), ())), preferred_element_type=jnp.float32
        )
        to_items = to_items + item_deg[:, None] * item_range.astype(jnp.float32)
        return (to_users, to_items)

    def user_range_of(user_vec):
        return double_gather(user_vec.astype(jnp.bfloat16), "item")

    def item_range_of(item_vec):
        return double_gather(item_vec.astype(jnp.bfloat16), "user")

    def operate(user_vec, item_vec):
        user_range = user_range_of(user_vec)
        item_range = item_range_of(item_vec)
        part_user, part_item = cross_parts(user_range, item_range)
        prior_user_part = prior_term(user_vec, prior_user)
        prior_item_part = prior_term(item_vec, prior_item)
        norm_part = per_draw(user_vec, user_vec) + per_draw(item_vec, item_vec)
        cross_dot = per_draw(user_range.astype(jnp.float32), part_user) + per_draw(
            item_range.astype(jnp.float32), part_item
        )
        curve_part = (
            per_draw(user_vec, prior_user_part)
            + per_draw(item_vec, prior_item_part)
            + noise_prec * cross_dot
        )
        sums = jnp.concatenate([norm_part, curve_part]).reshape(1, 2 * DRAWS)
        sums = jnp.pad(sums, ((0, 7), (0, width - 2 * DRAWS)))
        total_user, _ = halve_sum(part_user, "item", jnp.bfloat16)
        total_item, sums = halve_sum(part_item, "user", jnp.float32, sums, jnp.bfloat16)
        sums = sums[0, : 2 * DRAWS]
        size, bits = bit_count("item")
        for bit in range(bits):
            sums = sums + swap_with(sums, "item", size, bit)
        image_user = prior_user_part + noise_prec * total_user
        image_item = prior_item_part + noise_prec * total_item
        return (image_user, image_item, sums[:DRAWS], sums[DRAWS:])

    sol_user = jnp.zeros_like(user_own)
    sol_item = jnp.zeros_like(item_own)
    res_user, res_item = (user_own, item_own)
    dir_user, dir_item = (user_own, item_own)

    along_user, along_item, norm_now, curve = operate(res_user, res_item)
    step_len = norm_now / curve
    for iteration in range(ITERS):
        sol_user = sol_user + widen(step_len) * dir_user
        sol_item = sol_item + widen(step_len) * dir_item
        res_user = res_user - widen(step_len) * along_user
        res_item = res_item - widen(step_len) * along_item
        if iteration + 1 < ITERS:
            image_user, image_item, norm_next, curve = operate(res_user, res_item)
            beta_coef = norm_next / norm_now
            step_len = norm_next / (curve - beta_coef * norm_next / step_len)
            dir_user = res_user + widen(beta_coef) * dir_user
            dir_item = res_item + widen(beta_coef) * dir_item
            along_user = image_user + widen(beta_coef) * along_user
            along_item = image_item + widen(beta_coef) * along_item
            norm_now = norm_next
    return (sol_user[None], sol_item[None], res_user[None], res_item[None])


def solution(mesh):
    in_specs = (
        P("user", "item", None),
        P("item", "user", None),
        P(),
        P(),
        P("user", "item", None, None, None),
        P("user", "item", None, None),
        P("user", "item"),
    )
    out_specs = (
        P("user", "item", None),
        P("item", "user", None),
        P("user", "item", None),
        P("item", "user", None),
    )
    return jax.shard_map(
        per_device, mesh=mesh, in_specs=in_specs, out_specs=out_specs, check_vma=False
    )
```

```python
import jax
import jax.numpy as jnp
from jax import lax
from jax.sharding import PartitionSpec as P

DIM = 64
DRAWS = 4
TILE = 256
RB = 3
CB = 4
TMAX = 12
ITERS = 2


top_prec = lax.Precision.HIGHEST
noise_prec = 0.03125


def prior_term(field_vec, prior_mat):
    row_total = field_vec.shape[0]
    grouped = field_vec.reshape(row_total, DRAWS, DIM)
    mixed = jnp.einsum("nde,ef->ndf", grouped, prior_mat, precision=top_prec)
    return mixed.reshape(row_total, DRAWS * DIM)


def per_draw(left, right):
    product = (left * right).reshape(-1, DRAWS, DIM)
    return jnp.sum(product, axis=(0, 2))


def widen(coef):
    return jnp.repeat(coef, DIM)


def bit_count(axis):
    size = lax.axis_size(axis)
    bits = size.bit_length() - 1
    assert size == 1 << bits
    return size, bits


def swap_with(value, axis, size, bit, mask=None):
    mask = (1 << bit) if mask is None else mask
    pairs = [(i, i ^ mask) for i in range(size)]
    return lax.ppermute(value, axis, pairs)


def butterfly_psum(values):
    values = jnp.stack(values)
    for axis in ("item", "user"):
        size, bits = bit_count(axis)
        for bit in range(bits):
            values = values + swap_with(values, axis, size, bit)
    return values[0], values[1]


def code_rows(extra):
    high = extra.astype(jnp.bfloat16)
    rest = extra - high.astype(jnp.float32)
    mid = rest.astype(jnp.bfloat16)
    low = (rest - mid.astype(jnp.float32)).astype(jnp.bfloat16)
    return jnp.concatenate([high, mid, low])


def halve_sum(part, axis, send_type, extra=None, first_type=None):
    size, bits = bit_count(axis)
    me = lax.axis_index(axis)
    rows, width = part.shape[0] // size, part.shape[1]
    groups = [list(range(bits))[i : i + 2] for i in range(0, bits, 2)]
    left = list(range(bits))[::-1]
    buf = part.reshape([2] * bits + [rows, width])
    for stage, group in enumerate(groups):
        masks = [sum(1 << group[j] for j in range(len(group)) if (k >> j) & 1) for k in range(1 << len(group))]
        digit = sum(((me >> group[j]) & 1) << j for j in range(len(group)))

        def block_of(value):
            out = buf
            for j in sorted(range(len(group)), key=lambda j: -left.index(group[j])):
                out = lax.dynamic_index_in_dim(out, (value >> j) & 1, left.index(group[j]), keepdims=False)
            return out

        coded = extra is not None and stage == 0 and first_type is not None
        stage_type = first_type if (stage == 0 and first_type is not None) else send_type
        total = block_of(digit)
        shape = total.shape
        if extra is not None:
            tail = jnp.concatenate([extra, jnp.zeros((2 * extra.shape[0], width), extra.dtype)]) if coded else extra
            total = jnp.concatenate([total.reshape(-1, width), tail])
        for k in range(1, len(masks)):
            send = block_of(digit ^ k).astype(stage_type)
            if extra is not None:
                tail = code_rows(extra) if coded else extra
                send = jnp.concatenate([send.reshape(-1, width), tail.astype(stage_type)])
            total = total + swap_with(send, axis, size, None, masks[k]).astype(jnp.float32)
        if extra is not None:
            count = extra.shape[0]
            if coded:
                tail = total[-3 * count :]
                total = total[: -3 * count].reshape(shape)
                extra = tail[:count] + tail[count : 2 * count] + tail[2 * count :]
            else:
                extra = total[-count:]
                total = total[:-count].reshape(shape)
        for bit in group:
            left.remove(bit)
        buf = total
    return buf.reshape(rows, width), extra


def double_gather(piece, axis, hold=None):
    size, bits = bit_count(axis)
    me = lax.axis_index(axis)
    order = list(range(bits))[::-1]
    groups = [order[:1]] if bits % 2 else []
    groups += [order[i : i + 2] for i in range(bits % 2, bits, 2)]
    buf = piece[None]
    kept = None
    for group in groups:
        masks = [sum(1 << group[-1 - j] for j in range(len(group)) if (k >> j) & 1) for k in range(1 << len(group))]
        pieces = [buf] + [swap_with(buf, axis, size, None, mask) for mask in masks[1:]]
        digit = sum(((me >> group[-1 - j]) & 1) << j for j in range(len(group)))
        ordered = []
        for place in range(len(masks)):
            pick = pieces[place]
            for held in range(1, len(masks)):
                pick = jnp.where(digit == held, pieces[place ^ held], pick)
            ordered.append(pick)
        buf = jnp.stack(ordered, axis=1).reshape((-1,) + piece.shape)
        if hold is not None and kept is None:
            buf, kept = lax.optimization_barrier((buf, hold))
    result = buf.reshape((size * piece.shape[0],) + piece.shape[1:])
    return result if hold is None else (result, kept)

def per_device(
    draws_user, draws_item, prior_user, prior_item, count_tiles, tile_blocks, tile_count
):
    width = DRAWS * DIM
    user_own = draws_user[0]
    item_own = draws_item[0]
    in_use = jnp.arange(TMAX, dtype=jnp.int32) < tile_count[0, 0]
    row_pick = (tile_blocks[0, 0, :, 0][:, None] == jnp.arange(RB, dtype=jnp.int32)) & in_use[:, None]
    col_pick = (tile_blocks[0, 0, :, 1][:, None] == jnp.arange(CB, dtype=jnp.int32)) & in_use[:, None]
    place = (row_pick[:, :, None] & col_pick[:, None, :]).astype(jnp.bfloat16)

    def build_counts(tiles):
        tiles_bf = tiles.astype(jnp.bfloat16)
        counts_bf = jnp.einsum(
            "trc,tij->ricj", place, tiles_bf, preferred_element_type=jnp.bfloat16
        ).reshape(RB * TILE, CB * TILE)
        tile_rows = jnp.sum(tiles_bf, axis=2, dtype=jnp.float32)
        tile_cols = jnp.sum(tiles_bf, axis=1, dtype=jnp.float32)
        user_deg = jnp.sum(jnp.where(row_pick[:, :, None], tile_rows[:, None, :], 0.0), axis=0)
        item_deg = jnp.sum(jnp.where(col_pick[:, :, None], tile_cols[:, None, :], 0.0), axis=0)
        return (counts_bf, user_deg.reshape(-1), item_deg.reshape(-1))

    def cross_parts(user_range, item_range, counts):
        counts_bf, user_deg, item_deg = counts
        to_users = jnp.dot(counts_bf, item_range, preferred_element_type=jnp.float32)
        to_users = to_users + user_deg[:, None] * user_range.astype(jnp.float32)
        to_items = lax.dot_general(
            counts_bf, user_range, (((0,), (0,)), ((), ())), preferred_element_type=jnp.float32
        )
        to_items = to_items + item_deg[:, None] * item_range.astype(jnp.float32)
        return (to_users, to_items)

    def user_range_of(user_vec):
        return double_gather(user_vec.astype(jnp.bfloat16), "item")

    def operate(user_vec, item_vec, counts):
        user_range = user_range_of(user_vec)
        if counts is None:
            item_range, tiles = double_gather(item_vec.astype(jnp.bfloat16), "user", count_tiles[0, 0])
            counts = build_counts(tiles)
        else:
            item_range = double_gather(item_vec.astype(jnp.bfloat16), "user")
        part_user, part_item = cross_parts(user_range, item_range, counts)
        prior_user_part = prior_term(user_vec, prior_user)
        prior_item_part = prior_term(item_vec, prior_item)
        norm_part = per_draw(user_vec, user_vec) + per_draw(item_vec, item_vec)
        cross_dot = per_draw(user_range.astype(jnp.float32), part_user) + per_draw(
            item_range.astype(jnp.float32), part_item
        )
        curve_part = (
            per_draw(user_vec, prior_user_part)
            + per_draw(item_vec, prior_item_part)
            + noise_prec * cross_dot
        )
        sums = jnp.concatenate([norm_part, curve_part]).reshape(1, 2 * DRAWS)
        sums = jnp.pad(sums, ((0, 7), (0, width - 2 * DRAWS)))
        total_user, _ = halve_sum(part_user, "item", jnp.bfloat16)
        total_item, sums = halve_sum(part_item, "user", jnp.float32, sums, jnp.bfloat16)
        sums = sums[0, : 2 * DRAWS]
        size, bits = bit_count("item")
        for bit in range(bits):
            sums = sums + swap_with(sums, "item", size, bit)
        image_user = prior_user_part + noise_prec * total_user
        image_item = prior_item_part + noise_prec * total_item
        return (image_user, image_item, sums[:DRAWS], sums[DRAWS:], counts)

    sol_user = jnp.zeros_like(user_own)
    sol_item = jnp.zeros_like(item_own)
    res_user, res_item = (user_own, item_own)
    dir_user, dir_item = (user_own, item_own)

    along_user, along_item, norm_now, curve, counts = operate(res_user, res_item, None)
    step_len = norm_now / curve
    for iteration in range(ITERS):
        sol_user = sol_user + widen(step_len) * dir_user
        sol_item = sol_item + widen(step_len) * dir_item
        res_user = res_user - widen(step_len) * along_user
        res_item = res_item - widen(step_len) * along_item
        if iteration + 1 < ITERS:
            image_user, image_item, norm_next, curve, _ = operate(res_user, res_item, counts)
            beta_coef = norm_next / norm_now
            step_len = norm_next / (curve - beta_coef * norm_next / step_len)
            dir_user = res_user + widen(beta_coef) * dir_user
            dir_item = res_item + widen(beta_coef) * dir_item
            along_user = image_user + widen(beta_coef) * along_user
            along_item = image_item + widen(beta_coef) * along_item
            norm_now = norm_next
    return (sol_user[None], sol_item[None], res_user[None], res_item[None])


def solution(mesh):
    in_specs = (
        P("user", "item", None),
        P("item", "user", None),
        P(),
        P(),
        P("user", "item", None, None, None),
        P("user", "item", None, None),
        P("user", "item"),
    )
    out_specs = (
        P("user", "item", None),
        P("item", "user", None),
        P("user", "item", None),
        P("item", "user", None),
    )
    return jax.shard_map(
        per_device, mesh=mesh, in_specs=in_specs, out_specs=out_specs, check_vma=False
    )
```

```python
import jax
import jax.numpy as jnp
from jax import lax
from jax.sharding import PartitionSpec as P

DIM = 64
DRAWS = 4
TILE = 256
RB = 3
CB = 4
TMAX = 12
ITERS = 2


top_prec = lax.Precision.HIGHEST
noise_prec = 0.03125


def prior_term(field_vec, prior_mat):
    row_total = field_vec.shape[0]
    grouped = field_vec.reshape(row_total, DRAWS, DIM)
    mixed = jnp.einsum("nde,ef->ndf", grouped, prior_mat, precision=top_prec)
    return mixed.reshape(row_total, DRAWS * DIM)


def per_draw(left, right):
    product = (left * right).reshape(-1, DRAWS, DIM)
    return jnp.sum(product, axis=(0, 2))


def widen(coef):
    return jnp.repeat(coef, DIM)


def bit_count(axis):
    size = lax.axis_size(axis)
    bits = size.bit_length() - 1
    assert size == 1 << bits
    return size, bits


def swap_with(value, axis, size, bit, mask=None):
    mask = (1 << bit) if mask is None else mask
    pairs = [(i, i ^ mask) for i in range(size)]
    return lax.ppermute(value, axis, pairs)


def butterfly_psum(values):
    values = jnp.stack(values)
    for axis in ("item", "user"):
        size, bits = bit_count(axis)
        for bit in range(bits):
            values = values + swap_with(values, axis, size, bit)
    return values[0], values[1]


def code_rows(extra):
    high = extra.astype(jnp.bfloat16)
    rest = extra - high.astype(jnp.float32)
    mid = rest.astype(jnp.bfloat16)
    low = (rest - mid.astype(jnp.float32)).astype(jnp.bfloat16)
    return jnp.concatenate([high, mid, low])


def halve_sum(part, axis, send_type, extra=None, first_type=None):
    size, bits = bit_count(axis)
    rows, width = part.shape[0] // size, part.shape[1]
    groups = [list(range(bits))[i : i + 2] for i in range(0, bits, 2)]
    left = list(range(bits))[::-1]
    buf = part.reshape([2] * bits + [rows, width])
    for stage, group in enumerate(groups):
        masks = [sum(1 << group[j] for j in range(len(group)) if (k >> j) & 1) for k in range(1 << len(group))]

        def block_of(value):
            out = buf
            for j in sorted(range(len(group)), key=lambda j: -left.index(group[j])):
                out = lax.index_in_dim(out, (value >> j) & 1, left.index(group[j]), keepdims=False)
            return out

        coded = extra is not None and stage == 0 and first_type is not None
        stage_type = first_type if (stage == 0 and first_type is not None) else send_type
        total = block_of(0)
        shape = total.shape
        if extra is not None:
            tail = jnp.concatenate([extra, jnp.zeros((2 * extra.shape[0], width), extra.dtype)]) if coded else extra
            total = jnp.concatenate([total.reshape(-1, width), tail])
        for k in range(1, len(masks)):
            send = block_of(k).astype(stage_type)
            if extra is not None:
                tail = code_rows(extra) if coded else extra
                send = jnp.concatenate([send.reshape(-1, width), tail.astype(stage_type)])
            total = total + swap_with(send, axis, size, None, masks[k]).astype(jnp.float32)
        if extra is not None:
            count = extra.shape[0]
            if coded:
                tail = total[-3 * count :]
                total = total[: -3 * count].reshape(shape)
                extra = tail[:count] + tail[count : 2 * count] + tail[2 * count :]
            else:
                extra = total[-count:]
                total = total[:-count].reshape(shape)
        for bit in group:
            left.remove(bit)
        buf = total
    return buf.reshape(rows, width), extra


def double_gather(piece, axis, hold=None):
    size, bits = bit_count(axis)
    order = list(range(bits))[::-1]
    groups = [order[:1]] if bits % 2 else []
    groups += [order[i : i + 2] for i in range(bits % 2, bits, 2)]
    buf = piece[None]
    kept = None
    for group in groups:
        masks = [sum(1 << group[-1 - j] for j in range(len(group)) if (k >> j) & 1) for k in range(1 << len(group))]
        pieces = [buf] + [swap_with(buf, axis, size, None, mask) for mask in masks[1:]]
        buf = jnp.stack(pieces, axis=1).reshape((-1,) + piece.shape)
        if hold is not None and kept is None:
            buf, kept = lax.optimization_barrier((buf, hold))
    result = buf.reshape((size * piece.shape[0],) + piece.shape[1:])
    return result if hold is None else (result, kept)


def xor_order(value, axis, dim):
    size = lax.axis_size(axis)
    me = lax.axis_index(axis)
    shape = value.shape
    split = shape[:dim] + (size, shape[dim] // size) + shape[dim + 1 :]
    picked = jnp.take(value.reshape(split), jnp.arange(size) ^ me, axis=dim)
    return picked.reshape(shape)

def per_device(
    draws_user, draws_item, prior_user, prior_item, count_tiles, tile_blocks, tile_count
):
    width = DRAWS * DIM
    user_own = draws_user[0]
    item_own = draws_item[0]
    in_use = jnp.arange(TMAX, dtype=jnp.int32) < tile_count[0, 0]
    row_pick = (tile_blocks[0, 0, :, 0][:, None] == jnp.arange(RB, dtype=jnp.int32)) & in_use[:, None]
    col_pick = (tile_blocks[0, 0, :, 1][:, None] == jnp.arange(CB, dtype=jnp.int32)) & in_use[:, None]
    place = (row_pick[:, :, None] & col_pick[:, None, :]).astype(jnp.bfloat16)

    def build_counts(tiles):
        tiles_bf = tiles.astype(jnp.bfloat16)
        counts_bf = jnp.einsum(
            "trc,tij->ricj", place, tiles_bf, preferred_element_type=jnp.bfloat16
        ).reshape(RB * TILE, CB * TILE)
        tile_rows = jnp.sum(tiles_bf, axis=2, dtype=jnp.float32)
        tile_cols = jnp.sum(tiles_bf, axis=1, dtype=jnp.float32)
        user_deg = jnp.sum(jnp.where(row_pick[:, :, None], tile_rows[:, None, :], 0.0), axis=0)
        item_deg = jnp.sum(jnp.where(col_pick[:, :, None], tile_cols[:, None, :], 0.0), axis=0)
        counts_bf = xor_order(xor_order(counts_bf, "item", 0), "user", 1)
        user_deg = xor_order(user_deg.reshape(-1), "item", 0)
        item_deg = xor_order(item_deg.reshape(-1), "user", 0)
        return (counts_bf, user_deg, item_deg)

    def cross_parts(user_range, item_range, counts):
        counts_bf, user_deg, item_deg = counts
        to_users = jnp.dot(counts_bf, item_range, preferred_element_type=jnp.float32)
        to_users = to_users + user_deg[:, None] * user_range.astype(jnp.float32)
        to_items = lax.dot_general(
            counts_bf, user_range, (((0,), (0,)), ((), ())), preferred_element_type=jnp.float32
        )
        to_items = to_items + item_deg[:, None] * item_range.astype(jnp.float32)
        return (to_users, to_items)

    def user_range_of(user_vec):
        return double_gather(user_vec.astype(jnp.bfloat16), "item")

    def operate(user_vec, item_vec, counts):
        user_range = user_range_of(user_vec)
        if counts is None:
            item_range, tiles = double_gather(item_vec.astype(jnp.bfloat16), "user", count_tiles[0, 0])
            counts = build_counts(tiles)
        else:
            item_range = double_gather(item_vec.astype(jnp.bfloat16), "user")
        part_user, part_item = cross_parts(user_range, item_range, counts)
        prior_user_part = prior_term(user_vec, prior_user)
        prior_item_part = prior_term(item_vec, prior_item)
        norm_part = per_draw(user_vec, user_vec) + per_draw(item_vec, item_vec)
        cross_dot = per_draw(user_range.astype(jnp.float32), part_user) + per_draw(
            item_range.astype(jnp.float32), part_item
        )
        curve_part = (
            per_draw(user_vec, prior_user_part)
            + per_draw(item_vec, prior_item_part)
            + noise_prec * cross_dot
        )
        sums = jnp.concatenate([norm_part, curve_part]).reshape(1, 2 * DRAWS)
        sums = jnp.pad(sums, ((0, 7), (0, width - 2 * DRAWS)))
        total_user, _ = halve_sum(part_user, "item", jnp.bfloat16)
        total_item, sums = halve_sum(part_item, "user", jnp.float32, sums, jnp.bfloat16)
        sums = sums[0, : 2 * DRAWS]
        size, bits = bit_count("item")
        for bit in range(bits):
            sums = sums + swap_with(sums, "item", size, bit)
        image_user = prior_user_part + noise_prec * total_user
        image_item = prior_item_part + noise_prec * total_item
        return (image_user, image_item, sums[:DRAWS], sums[DRAWS:], counts)

    sol_user = jnp.zeros_like(user_own)
    sol_item = jnp.zeros_like(item_own)
    res_user, res_item = (user_own, item_own)
    dir_user, dir_item = (user_own, item_own)

    along_user, along_item, norm_now, curve, counts = operate(res_user, res_item, None)
    step_len = norm_now / curve
    for iteration in range(ITERS):
        sol_user = sol_user + widen(step_len) * dir_user
        sol_item = sol_item + widen(step_len) * dir_item
        res_user = res_user - widen(step_len) * along_user
        res_item = res_item - widen(step_len) * along_item
        if iteration + 1 < ITERS:
            image_user, image_item, norm_next, curve, _ = operate(res_user, res_item, counts)
            beta_coef = norm_next / norm_now
            step_len = norm_next / (curve - beta_coef * norm_next / step_len)
            dir_user = res_user + widen(beta_coef) * dir_user
            dir_item = res_item + widen(beta_coef) * dir_item
            along_user = image_user + widen(beta_coef) * along_user
            along_item = image_item + widen(beta_coef) * along_item
            norm_now = norm_next
    return (sol_user[None], sol_item[None], res_user[None], res_item[None])


def solution(mesh):
    in_specs = (
        P("user", "item", None),
        P("item", "user", None),
        P(),
        P(),
        P("user", "item", None, None, None),
        P("user", "item", None, None),
        P("user", "item"),
    )
    out_specs = (
        P("user", "item", None),
        P("item", "user", None),
        P("user", "item", None),
        P("item", "user", None),
    )
    return jax.shard_map(
        per_device, mesh=mesh, in_specs=in_specs, out_specs=out_specs, check_vma=False
    )
```

```python
import jax
import jax.numpy as jnp
from jax import lax
from jax.sharding import PartitionSpec as P

DIM = 64
DRAWS = 4
TILE = 256
RB = 3
CB = 4
TMAX = 12
ITERS = 2


top_prec = lax.Precision.HIGHEST
noise_prec = 0.03125


def prior_term(field_vec, prior_mat):
    row_total = field_vec.shape[0]
    grouped = field_vec.reshape(row_total, DRAWS, DIM)
    mixed = jnp.einsum("nde,ef->ndf", grouped, prior_mat, precision=top_prec)
    return mixed.reshape(row_total, DRAWS * DIM)


def per_draw(left, right):
    product = (left * right).reshape(-1, DRAWS, DIM)
    return jnp.sum(product, axis=(0, 2))


def widen(coef):
    return jnp.repeat(coef, DIM)


def bit_count(axis):
    size = lax.axis_size(axis)
    bits = size.bit_length() - 1
    assert size == 1 << bits
    return size, bits


def swap_with(value, axis, size, bit, mask=None):
    mask = (1 << bit) if mask is None else mask
    pairs = [(i, i ^ mask) for i in range(size)]
    return lax.ppermute(value, axis, pairs)


def butterfly_psum(values):
    values = jnp.stack(values)
    for axis in ("item", "user"):
        size, bits = bit_count(axis)
        for bit in range(bits):
            values = values + swap_with(values, axis, size, bit)
    return values[0], values[1]


def code_rows(extra):
    high = extra.astype(jnp.bfloat16)
    rest = extra - high.astype(jnp.float32)
    mid = rest.astype(jnp.bfloat16)
    low = (rest - mid.astype(jnp.float32)).astype(jnp.bfloat16)
    return jnp.concatenate([high, mid, low])


def halve_sum(part, axis, send_type, extra=None, first_type=None):
    size, bits = bit_count(axis)
    rows, width = part.shape[0] // size, part.shape[1]
    groups = [list(range(bits))[i : i + 2] for i in range(0, bits, 2)]
    left = list(range(bits))[::-1]
    buf = part.reshape([2] * bits + [rows, width])
    for stage, group in enumerate(groups):
        masks = [sum(1 << group[j] for j in range(len(group)) if (k >> j) & 1) for k in range(1 << len(group))]

        def block_of(value):
            out = buf
            for j in sorted(range(len(group)), key=lambda j: -left.index(group[j])):
                out = lax.index_in_dim(out, (value >> j) & 1, left.index(group[j]), keepdims=False)
            return out

        coded = extra is not None and stage == 0 and first_type is not None
        stage_type = first_type if (stage == 0 and first_type is not None) else send_type
        total = block_of(0)
        shape = total.shape
        if extra is not None:
            tail = jnp.concatenate([extra, jnp.zeros((2 * extra.shape[0], width), extra.dtype)]) if coded else extra
            total = jnp.concatenate([total.reshape(-1, width), tail])
        for k in range(1, len(masks)):
            send = block_of(k).astype(stage_type)
            if extra is not None:
                tail = code_rows(extra) if coded else extra
                send = jnp.concatenate([send.reshape(-1, width), tail.astype(stage_type)])
            total = total + swap_with(send, axis, size, None, masks[k]).astype(jnp.float32)
        if extra is not None:
            count = extra.shape[0]
            if coded:
                tail = total[-3 * count :]
                total = total[: -3 * count].reshape(shape)
                extra = tail[:count] + tail[count : 2 * count] + tail[2 * count :]
            else:
                extra = total[-count:]
                total = total[:-count].reshape(shape)
        for bit in group:
            left.remove(bit)
        buf = total
    return buf.reshape(rows, width), extra


def double_gather(piece, axis, hold=None):
    size, bits = bit_count(axis)
    order = list(range(bits))[::-1]
    groups = [order[:1]] if bits % 2 else []
    groups += [order[i : i + 2] for i in range(bits % 2, bits, 2)]
    buf = piece[None]
    kept = None
    for group in groups:
        masks = [sum(1 << group[-1 - j] for j in range(len(group)) if (k >> j) & 1) for k in range(1 << len(group))]
        pieces = [buf] + [swap_with(buf, axis, size, None, mask) for mask in masks[1:]]
        buf = jnp.stack(pieces, axis=1).reshape((-1,) + piece.shape)
        if hold is not None and kept is None:
            buf, kept = lax.optimization_barrier((buf, hold))
    result = buf.reshape((size * piece.shape[0],) + piece.shape[1:])
    return result if hold is None else (result, kept)


def xor_order(value, axis, dim):
    size = lax.axis_size(axis)
    me = lax.axis_index(axis)
    shape = value.shape
    split = shape[:dim] + (size, shape[dim] // size) + shape[dim + 1 :]
    if size == 2:
        parts = value.reshape(split)
        swapped = jnp.concatenate(
            [lax.index_in_dim(parts, 1, dim), lax.index_in_dim(parts, 0, dim)], axis=dim
        )
        return jnp.where(me == 1, swapped, parts).reshape(shape)
    picked = jnp.take(value.reshape(split), jnp.arange(size) ^ me, axis=dim)
    return picked.reshape(shape)

def per_device(
    draws_user, draws_item, prior_user, prior_item, count_tiles, tile_blocks, tile_count
):
    width = DRAWS * DIM
    user_own = draws_user[0]
    item_own = draws_item[0]
    in_use = jnp.arange(TMAX, dtype=jnp.int32) < tile_count[0, 0]
    row_pick = (tile_blocks[0, 0, :, 0][:, None] == jnp.arange(RB, dtype=jnp.int32)) & in_use[:, None]
    col_pick = (tile_blocks[0, 0, :, 1][:, None] == jnp.arange(CB, dtype=jnp.int32)) & in_use[:, None]
    place = (row_pick[:, :, None] & col_pick[:, None, :]).astype(jnp.bfloat16)

    def build_counts(tiles):
        me_user = lax.axis_index("user")
        n_user, _ = bit_count("user")
        subs = n_user // CB
        low = me_user & (subs - 1)
        high = me_user // subs
        tiles_bf = tiles.astype(jnp.bfloat16).reshape(TMAX, TILE, subs, TILE // subs)
        tiles_bf = jnp.take(tiles_bf, jnp.arange(subs) ^ low, axis=2).reshape(TMAX, TILE, TILE)
        moved = jnp.take(place, jnp.arange(CB) ^ high, axis=2)
        counts_bf = jnp.einsum(
            "trc,tij->ricj", moved, tiles_bf, preferred_element_type=jnp.bfloat16
        ).reshape(RB * TILE, CB * TILE)
        tile_rows = jnp.sum(tiles_bf, axis=2, dtype=jnp.float32)
        tile_cols = jnp.sum(tiles_bf, axis=1, dtype=jnp.float32)
        moved_cols = jnp.take(col_pick, jnp.arange(CB) ^ high, axis=1)
        user_deg = jnp.sum(jnp.where(row_pick[:, :, None], tile_rows[:, None, :], 0.0), axis=0)
        item_deg = jnp.sum(jnp.where(moved_cols[:, :, None], tile_cols[:, None, :], 0.0), axis=0)
        counts_bf = xor_order(counts_bf, "item", 0)
        user_deg = xor_order(user_deg.reshape(-1), "item", 0)
        return (counts_bf, user_deg, item_deg.reshape(-1))

    def cross_parts(user_range, item_range, counts):
        counts_bf, user_deg, item_deg = counts
        to_users = jnp.dot(counts_bf, item_range, preferred_element_type=jnp.float32)
        to_users = to_users + user_deg[:, None] * user_range.astype(jnp.float32)
        to_items = lax.dot_general(
            counts_bf, user_range, (((0,), (0,)), ((), ())), preferred_element_type=jnp.float32
        )
        to_items = to_items + item_deg[:, None] * item_range.astype(jnp.float32)
        return (to_users, to_items)

    def user_range_of(user_vec):
        return double_gather(user_vec.astype(jnp.bfloat16), "item")

    def operate(user_vec, item_vec, counts):
        user_range = user_range_of(user_vec)
        if counts is None:
            item_range, tiles = double_gather(item_vec.astype(jnp.bfloat16), "user", count_tiles[0, 0])
            counts = build_counts(tiles)
        else:
            item_range = double_gather(item_vec.astype(jnp.bfloat16), "user")
        part_user, part_item = cross_parts(user_range, item_range, counts)
        prior_user_part = prior_term(user_vec, prior_user)
        prior_item_part = prior_term(item_vec, prior_item)
        norm_part = per_draw(user_vec, user_vec) + per_draw(item_vec, item_vec)
        cross_dot = per_draw(user_range.astype(jnp.float32), part_user) + per_draw(
            item_range.astype(jnp.float32), part_item
        )
        curve_part = (
            per_draw(user_vec, prior_user_part)
            + per_draw(item_vec, prior_item_part)
            + noise_prec * cross_dot
        )
        sums = jnp.concatenate([norm_part, curve_part]).reshape(1, 2 * DRAWS)
        sums = jnp.pad(sums, ((0, 7), (0, width - 2 * DRAWS)))
        total_user, _ = halve_sum(part_user, "item", jnp.bfloat16)
        total_item, sums = halve_sum(part_item, "user", jnp.float32, sums, jnp.bfloat16)
        sums = sums[0, : 2 * DRAWS]
        size, bits = bit_count("item")
        for bit in range(bits):
            sums = sums + swap_with(sums, "item", size, bit)
        image_user = prior_user_part + noise_prec * total_user
        image_item = prior_item_part + noise_prec * total_item
        return (image_user, image_item, sums[:DRAWS], sums[DRAWS:], counts)

    sol_user = jnp.zeros_like(user_own)
    sol_item = jnp.zeros_like(item_own)
    res_user, res_item = (user_own, item_own)
    dir_user, dir_item = (user_own, item_own)

    along_user, along_item, norm_now, curve, counts = operate(res_user, res_item, None)
    step_len = norm_now / curve
    for iteration in range(ITERS):
        sol_user = sol_user + widen(step_len) * dir_user
        sol_item = sol_item + widen(step_len) * dir_item
        res_user = res_user - widen(step_len) * along_user
        res_item = res_item - widen(step_len) * along_item
        if iteration + 1 < ITERS:
            image_user, image_item, norm_next, curve, _ = operate(res_user, res_item, counts)
            beta_coef = norm_next / norm_now
            step_len = norm_next / (curve - beta_coef * norm_next / step_len)
            dir_user = res_user + widen(beta_coef) * dir_user
            dir_item = res_item + widen(beta_coef) * dir_item
            along_user = image_user + widen(beta_coef) * along_user
            along_item = image_item + widen(beta_coef) * along_item
            norm_now = norm_next
    return (sol_user[None], sol_item[None], res_user[None], res_item[None])


def solution(mesh):
    in_specs = (
        P("user", "item", None),
        P("item", "user", None),
        P(),
        P(),
        P("user", "item", None, None, None),
        P("user", "item", None, None),
        P("user", "item"),
    )
    out_specs = (
        P("user", "item", None),
        P("item", "user", None),
        P("user", "item", None),
        P("item", "user", None),
    )
    return jax.shard_map(
        per_device, mesh=mesh, in_specs=in_specs, out_specs=out_specs, check_vma=False
    )
```

```python
import jax
import jax.numpy as jnp
from jax import lax
from jax.sharding import PartitionSpec as P

DIM = 64
DRAWS = 4
TILE = 256
RB = 3
CB = 4
TMAX = 12
ITERS = 2


top_prec = lax.Precision.HIGHEST
noise_prec = 0.03125


def prior_term(field_vec, prior_mat):
    row_total = field_vec.shape[0]
    grouped = field_vec.reshape(row_total * DRAWS, DIM)
    mixed = jnp.dot(grouped, prior_mat, precision=top_prec)
    return mixed.reshape(row_total, DRAWS * DIM)


def per_draw(left, right):
    product = (left * right).reshape(-1, DRAWS, DIM)
    return jnp.sum(product, axis=(0, 2))


def widen(coef):
    return jnp.repeat(coef, DIM)


def bit_count(axis):
    size = lax.axis_size(axis)
    bits = size.bit_length() - 1
    assert size == 1 << bits
    return size, bits


def swap_with(value, axis, size, bit, mask=None):
    mask = (1 << bit) if mask is None else mask
    pairs = [(i, i ^ mask) for i in range(size)]
    return lax.ppermute(value, axis, pairs)


def butterfly_psum(values):
    values = jnp.stack(values)
    for axis in ("item", "user"):
        size, bits = bit_count(axis)
        for bit in range(bits):
            values = values + swap_with(values, axis, size, bit)
    return values[0], values[1]


def code_rows(extra):
    high = extra.astype(jnp.bfloat16)
    rest = extra - high.astype(jnp.float32)
    mid = rest.astype(jnp.bfloat16)
    low = (rest - mid.astype(jnp.float32)).astype(jnp.bfloat16)
    return jnp.concatenate([high, mid, low])


def halve_sum(part, axis, send_type, extra=None, first_type=None):
    size, bits = bit_count(axis)
    me = lax.axis_index(axis)
    rows, width = part.shape[0] // size, part.shape[1]
    groups = [list(range(bits))[i : i + 2] for i in range(0, bits, 2)]
    left = list(range(bits))[::-1]
    buf = part.reshape([2] * bits + [rows, width])
    for stage, group in enumerate(groups):
        masks = [sum(1 << group[j] for j in range(len(group)) if (k >> j) & 1) for k in range(1 << len(group))]
        digit = sum(((me >> group[j]) & 1) << j for j in range(len(group)))

        def block_of(value):
            out = buf
            for j in sorted(range(len(group)), key=lambda j: -left.index(group[j])):
                out = lax.dynamic_index_in_dim(out, (value >> j) & 1, left.index(group[j]), keepdims=False)
            return out

        coded = extra is not None and stage == 0 and first_type is not None
        stage_type = first_type if (stage == 0 and first_type is not None) else send_type
        total = block_of(digit)
        shape = total.shape
        if extra is not None:
            tail = jnp.concatenate([extra, jnp.zeros((2 * extra.shape[0], width), extra.dtype)]) if coded else extra
            total = jnp.concatenate([total.reshape(-1, width), tail])
        for k in range(1, len(masks)):
            send = block_of(digit ^ k).astype(stage_type)
            if extra is not None:
                tail = code_rows(extra) if coded else extra
                send = jnp.concatenate([send.reshape(-1, width), tail.astype(stage_type)])
            total = total + swap_with(send, axis, size, None, masks[k]).astype(jnp.float32)
        if extra is not None:
            count = extra.shape[0]
            if coded:
                tail = total[-3 * count :]
                total = total[: -3 * count].reshape(shape)
                extra = tail[:count] + tail[count : 2 * count] + tail[2 * count :]
            else:
                extra = total[-count:]
                total = total[:-count].reshape(shape)
        for bit in group:
            left.remove(bit)
        buf = total
    return buf.reshape(rows, width), extra


def double_gather(piece, axis, hold=None):
    size, bits = bit_count(axis)
    me = lax.axis_index(axis)
    order = list(range(bits))[::-1]
    groups = [order[:1]] if bits % 2 else []
    groups += [order[i : i + 2] for i in range(bits % 2, bits, 2)]
    buf = piece[None]
    kept = None
    for group in groups:
        masks = [sum(1 << group[-1 - j] for j in range(len(group)) if (k >> j) & 1) for k in range(1 << len(group))]
        pieces = [buf] + [swap_with(buf, axis, size, None, mask) for mask in masks[1:]]
        digit = sum(((me >> group[-1 - j]) & 1) << j for j in range(len(group)))
        ordered = []
        for place in range(len(masks)):
            pick = pieces[place]
            for held in range(1, len(masks)):
                pick = jnp.where(digit == held, pieces[place ^ held], pick)
            ordered.append(pick)
        buf = jnp.stack(ordered, axis=1).reshape((-1,) + piece.shape)
        if hold is not None and kept is None:
            buf, kept = lax.optimization_barrier((buf, hold))
    result = buf.reshape((size * piece.shape[0],) + piece.shape[1:])
    return result if hold is None else (result, kept)

def per_device(
    draws_user, draws_item, prior_user, prior_item, count_tiles, tile_blocks, tile_count
):
    width = DRAWS * DIM
    user_own = draws_user[0]
    item_own = draws_item[0]
    in_use = jnp.arange(TMAX, dtype=jnp.int32) < tile_count[0, 0]
    row_pick = (tile_blocks[0, 0, :, 0][:, None] == jnp.arange(RB, dtype=jnp.int32)) & in_use[:, None]
    col_pick = (tile_blocks[0, 0, :, 1][:, None] == jnp.arange(CB, dtype=jnp.int32)) & in_use[:, None]
    place = (row_pick[:, :, None] & col_pick[:, None, :]).astype(jnp.bfloat16)

    def build_counts(tiles):
        tiles_bf = tiles.astype(jnp.bfloat16)
        counts_bf = jnp.einsum(
            "trc,tij->ricj", place, tiles_bf, preferred_element_type=jnp.bfloat16
        ).reshape(RB * TILE, CB * TILE)
        tile_rows = jnp.sum(tiles_bf, axis=2, dtype=jnp.float32)
        tile_cols = jnp.sum(tiles_bf, axis=1, dtype=jnp.float32)
        user_deg = jnp.sum(jnp.where(row_pick[:, :, None], tile_rows[:, None, :], 0.0), axis=0)
        item_deg = jnp.sum(jnp.where(col_pick[:, :, None], tile_cols[:, None, :], 0.0), axis=0)
        return (counts_bf, user_deg.reshape(-1), item_deg.reshape(-1))

    def cross_parts(user_range, item_range, counts):
        counts_bf, user_deg, item_deg = counts
        to_users = jnp.dot(counts_bf, item_range, preferred_element_type=jnp.float32)
        to_users = to_users + user_deg[:, None] * user_range.astype(jnp.float32)
        to_items = lax.dot_general(
            counts_bf, user_range, (((0,), (0,)), ((), ())), preferred_element_type=jnp.float32
        )
        to_items = to_items + item_deg[:, None] * item_range.astype(jnp.float32)
        return (to_users, to_items)

    def user_range_of(user_vec):
        return double_gather(user_vec.astype(jnp.bfloat16), "item")

    def operate(user_vec, item_vec, counts):
        user_range = user_range_of(user_vec)
        if counts is None:
            item_range, tiles = double_gather(item_vec.astype(jnp.bfloat16), "user", count_tiles[0, 0])
            counts = build_counts(tiles)
        else:
            item_range = double_gather(item_vec.astype(jnp.bfloat16), "user")
        part_user, part_item = cross_parts(user_range, item_range, counts)
        prior_user_part = prior_term(user_vec, prior_user)
        prior_item_part = prior_term(item_vec, prior_item)
        norm_part = per_draw(user_vec, user_vec) + per_draw(item_vec, item_vec)
        cross_dot = per_draw(user_range.astype(jnp.float32), part_user) + per_draw(
            item_range.astype(jnp.float32), part_item
        )
        curve_part = (
            per_draw(user_vec, prior_user_part)
            + per_draw(item_vec, prior_item_part)
            + noise_prec * cross_dot
        )
        sums = jnp.concatenate([norm_part, curve_part]).reshape(1, 2 * DRAWS)
        sums = jnp.pad(sums, ((0, 7), (0, width - 2 * DRAWS)))
        total_user, _ = halve_sum(part_user, "item", jnp.bfloat16)
        total_item, sums = halve_sum(part_item, "user", jnp.float32, sums, jnp.bfloat16)
        sums = sums[0, : 2 * DRAWS]
        size, bits = bit_count("item")
        for bit in range(bits):
            sums = sums + swap_with(sums, "item", size, bit)
        image_user = prior_user_part + noise_prec * total_user
        image_item = prior_item_part + noise_prec * total_item
        return (image_user, image_item, sums[:DRAWS], sums[DRAWS:], counts)

    sol_user = jnp.zeros_like(user_own)
    sol_item = jnp.zeros_like(item_own)
    res_user, res_item = (user_own, item_own)
    dir_user, dir_item = (user_own, item_own)

    along_user, along_item, norm_now, curve, counts = operate(res_user, res_item, None)
    step_len = norm_now / curve
    for iteration in range(ITERS):
        sol_user = sol_user + widen(step_len) * dir_user
        sol_item = sol_item + widen(step_len) * dir_item
        res_user = res_user - widen(step_len) * along_user
        res_item = res_item - widen(step_len) * along_item
        if iteration + 1 < ITERS:
            image_user, image_item, norm_next, curve, _ = operate(res_user, res_item, counts)
            beta_coef = norm_next / norm_now
            step_len = norm_next / (curve - beta_coef * norm_next / step_len)
            dir_user = res_user + widen(beta_coef) * dir_user
            dir_item = res_item + widen(beta_coef) * dir_item
            along_user = image_user + widen(beta_coef) * along_user
            along_item = image_item + widen(beta_coef) * along_item
            norm_now = norm_next
    return (sol_user[None], sol_item[None], res_user[None], res_item[None])


def solution(mesh):
    in_specs = (
        P("user", "item", None),
        P("item", "user", None),
        P(),
        P(),
        P("user", "item", None, None, None),
        P("user", "item", None, None),
        P("user", "item"),
    )
    out_specs = (
        P("user", "item", None),
        P("item", "user", None),
        P("user", "item", None),
        P("item", "user", None),
    )
    return jax.shard_map(
        per_device, mesh=mesh, in_specs=in_specs, out_specs=out_specs, check_vma=False
    )
```

```python
import jax
import jax.numpy as jnp
from jax import lax
from jax.sharding import PartitionSpec as P

DIM = 64
DRAWS = 4
TILE = 256
RB = 3
CB = 4
TMAX = 12
ITERS = 2


top_prec = lax.Precision.HIGHEST
noise_prec = 0.03125


def prior_term(field_vec, prior_mat):
    row_total = field_vec.shape[0]
    grouped = field_vec.reshape(row_total * DRAWS, DIM)
    mixed = jnp.dot(grouped, prior_mat, precision=top_prec)
    return mixed.reshape(row_total, DRAWS * DIM)


def per_draw(left, right):
    product = (left * right).reshape(-1, DRAWS, DIM)
    return jnp.sum(product, axis=(0, 2))


def widen(coef):
    return jnp.repeat(coef, DIM)


def bit_count(axis):
    size = lax.axis_size(axis)
    bits = size.bit_length() - 1
    assert size == 1 << bits
    return size, bits


def swap_with(value, axis, size, bit, mask=None):
    mask = (1 << bit) if mask is None else mask
    pairs = [(i, i ^ mask) for i in range(size)]
    return lax.ppermute(value, axis, pairs)


def butterfly_psum(values):
    values = jnp.stack(values)
    for axis in ("item", "user"):
        size, bits = bit_count(axis)
        for bit in range(bits):
            values = values + swap_with(values, axis, size, bit)
    return values[0], values[1]


def code_rows(extra):
    high = extra.astype(jnp.bfloat16)
    rest = extra - high.astype(jnp.float32)
    mid = rest.astype(jnp.bfloat16)
    low = (rest - mid.astype(jnp.float32)).astype(jnp.bfloat16)
    return jnp.concatenate([high, mid, low])


def halve_sum(part, axis, send_type, extra=None, first_type=None):
    size, bits = bit_count(axis)
    me = lax.axis_index(axis)
    rows, width = part.shape[0] // size, part.shape[1]
    groups = [list(range(bits))[i : i + 2] for i in range(0, bits, 2)]
    left = list(range(bits))[::-1]
    buf = part.reshape([2] * bits + [rows, width])
    for stage, group in enumerate(groups):
        masks = [sum(1 << group[j] for j in range(len(group)) if (k >> j) & 1) for k in range(1 << len(group))]
        digit = sum(((me >> group[j]) & 1) << j for j in range(len(group)))

        def block_of(value):
            out = buf
            for j in sorted(range(len(group)), key=lambda j: -left.index(group[j])):
                out = lax.dynamic_index_in_dim(out, (value >> j) & 1, left.index(group[j]), keepdims=False)
            return out

        coded = extra is not None and stage == 0 and first_type is not None
        stage_type = first_type if (stage == 0 and first_type is not None) else send_type
        total = block_of(digit)
        shape = total.shape
        if extra is not None:
            tail = jnp.concatenate([extra, jnp.zeros((2 * extra.shape[0], width), extra.dtype)]) if coded else extra
            total = jnp.concatenate([total.reshape(-1, width), tail])
        for k in range(1, len(masks)):
            send = block_of(digit ^ k).astype(stage_type)
            if extra is not None:
                tail = code_rows(extra) if coded else extra
                send = jnp.concatenate([send.reshape(-1, width), tail.astype(stage_type)])
            total = total + swap_with(send, axis, size, None, masks[k]).astype(jnp.float32)
        if extra is not None:
            count = extra.shape[0]
            if coded:
                tail = total[-3 * count :]
                total = total[: -3 * count].reshape(shape)
                extra = tail[:count] + tail[count : 2 * count] + tail[2 * count :]
            else:
                extra = total[-count:]
                total = total[:-count].reshape(shape)
        for bit in group:
            left.remove(bit)
        buf = total
    return buf.reshape(rows, width), extra


def double_gather(piece, axis, hold=None):
    size, bits = bit_count(axis)
    me = lax.axis_index(axis)
    order = list(range(bits))[::-1]
    groups = [order[:1]] if bits % 2 else []
    groups += [order[i : i + 2] for i in range(bits % 2, bits, 2)]
    buf = piece[None]
    kept = None
    for group in groups:
        masks = [sum(1 << group[-1 - j] for j in range(len(group)) if (k >> j) & 1) for k in range(1 << len(group))]
        pieces = [buf] + [swap_with(buf, axis, size, None, mask) for mask in masks[1:]]
        digit = sum(((me >> group[-1 - j]) & 1) << j for j in range(len(group)))
        ordered = []
        for place in range(len(masks)):
            pick = pieces[place]
            for held in range(1, len(masks)):
                pick = jnp.where(digit == held, pieces[place ^ held], pick)
            ordered.append(pick)
        buf = jnp.stack(ordered, axis=1).reshape((-1,) + piece.shape)
        if hold is not None and kept is None:
            buf, kept = lax.optimization_barrier((buf, hold))
    result = buf.reshape((size * piece.shape[0],) + piece.shape[1:])
    return result if hold is None else (result, kept)

def per_device(
    draws_user, draws_item, prior_user, prior_item, count_tiles, tile_blocks, tile_count
):
    width = DRAWS * DIM
    user_own = draws_user[0]
    item_own = draws_item[0]
    in_use = jnp.arange(TMAX, dtype=jnp.int32) < tile_count[0, 0]
    row_pick = (tile_blocks[0, 0, :, 0][:, None] == jnp.arange(RB, dtype=jnp.int32)) & in_use[:, None]
    col_pick = (tile_blocks[0, 0, :, 1][:, None] == jnp.arange(CB, dtype=jnp.int32)) & in_use[:, None]
    place = (row_pick[:, :, None] & col_pick[:, None, :]).astype(jnp.bfloat16)

    def build_counts(tiles):
        tiles_bf = tiles.astype(jnp.bfloat16)
        counts_bf = jnp.einsum(
            "trc,tij->ricj", place, tiles_bf, preferred_element_type=jnp.bfloat16
        ).reshape(RB * TILE, CB * TILE)
        counts_t = jnp.einsum(
            "trc,tij->cjri", place, tiles_bf, preferred_element_type=jnp.bfloat16
        ).reshape(CB * TILE, RB * TILE)
        tile_rows = jnp.sum(tiles_bf, axis=2, dtype=jnp.float32)
        tile_cols = jnp.sum(tiles_bf, axis=1, dtype=jnp.float32)
        user_deg = jnp.sum(jnp.where(row_pick[:, :, None], tile_rows[:, None, :], 0.0), axis=0)
        item_deg = jnp.sum(jnp.where(col_pick[:, :, None], tile_cols[:, None, :], 0.0), axis=0)
        return (counts_bf, counts_t, user_deg.reshape(-1), item_deg.reshape(-1))

    def cross_parts(user_range, item_range, counts):
        counts_bf, counts_t, user_deg, item_deg = counts
        to_users = jnp.dot(counts_bf, item_range, preferred_element_type=jnp.float32)
        to_users = to_users + user_deg[:, None] * user_range.astype(jnp.float32)
        to_items = jnp.dot(counts_t, user_range, preferred_element_type=jnp.float32)
        to_items = to_items + item_deg[:, None] * item_range.astype(jnp.float32)
        return (to_users, to_items)

    def user_range_of(user_vec):
        return double_gather(user_vec.astype(jnp.bfloat16), "item")

    def operate(user_vec, item_vec, counts):
        user_range = user_range_of(user_vec)
        if counts is None:
            item_range, tiles = double_gather(item_vec.astype(jnp.bfloat16), "user", count_tiles[0, 0])
            counts = build_counts(tiles)
        else:
            item_range = double_gather(item_vec.astype(jnp.bfloat16), "user")
        part_user, part_item = cross_parts(user_range, item_range, counts)
        prior_user_part = prior_term(user_vec, prior_user)
        prior_item_part = prior_term(item_vec, prior_item)
        norm_part = per_draw(user_vec, user_vec) + per_draw(item_vec, item_vec)
        cross_dot = per_draw(user_range.astype(jnp.float32), part_user) + per_draw(
            item_range.astype(jnp.float32), part_item
        )
        curve_part = (
            per_draw(user_vec, prior_user_part)
            + per_draw(item_vec, prior_item_part)
            + noise_prec * cross_dot
        )
        sums = jnp.concatenate([norm_part, curve_part]).reshape(1, 2 * DRAWS)
        sums = jnp.pad(sums, ((0, 7), (0, width - 2 * DRAWS)))
        total_user, _ = halve_sum(part_user, "item", jnp.bfloat16)
        total_item, sums = halve_sum(part_item, "user", jnp.float32, sums, jnp.bfloat16)
        sums = sums[0, : 2 * DRAWS]
        size, bits = bit_count("item")
        for bit in range(bits):
            sums = sums + swap_with(sums, "item", size, bit)
        image_user = prior_user_part + noise_prec * total_user
        image_item = prior_item_part + noise_prec * total_item
        return (image_user, image_item, sums[:DRAWS], sums[DRAWS:], counts)

    sol_user = jnp.zeros_like(user_own)
    sol_item = jnp.zeros_like(item_own)
    res_user, res_item = (user_own, item_own)
    dir_user, dir_item = (user_own, item_own)

    along_user, along_item, norm_now, curve, counts = operate(res_user, res_item, None)
    step_len = norm_now / curve
    for iteration in range(ITERS):
        sol_user = sol_user + widen(step_len) * dir_user
        sol_item = sol_item + widen(step_len) * dir_item
        res_user = res_user - widen(step_len) * along_user
        res_item = res_item - widen(step_len) * along_item
        if iteration + 1 < ITERS:
            image_user, image_item, norm_next, curve, _ = operate(res_user, res_item, counts)
            beta_coef = norm_next / norm_now
            step_len = norm_next / (curve - beta_coef * norm_next / step_len)
            dir_user = res_user + widen(beta_coef) * dir_user
            dir_item = res_item + widen(beta_coef) * dir_item
            along_user = image_user + widen(beta_coef) * along_user
            along_item = image_item + widen(beta_coef) * along_item
            norm_now = norm_next
    return (sol_user[None], sol_item[None], res_user[None], res_item[None])


def solution(mesh):
    in_specs = (
        P("user", "item", None),
        P("item", "user", None),
        P(),
        P(),
        P("user", "item", None, None, None),
        P("user", "item", None, None),
        P("user", "item"),
    )
    out_specs = (
        P("user", "item", None),
        P("item", "user", None),
        P("user", "item", None),
        P("item", "user", None),
    )
    return jax.shard_map(
        per_device, mesh=mesh, in_specs=in_specs, out_specs=out_specs, check_vma=False
    )
```

```python
import jax
import jax.numpy as jnp
from jax import lax
from jax.sharding import PartitionSpec as P

DIM = 64
DRAWS = 4
TILE = 256
RB = 3
CB = 4
TMAX = 12
ITERS = 2


top_prec = lax.Precision.HIGHEST
noise_prec = 0.03125


def prior_term(field_vec, prior_mat):
    row_total = field_vec.shape[0]
    grouped = field_vec.reshape(row_total * DRAWS, DIM)
    mixed = jnp.dot(grouped, prior_mat, precision=top_prec)
    return mixed.reshape(row_total, DRAWS * DIM)


def per_draw(left, right):
    product = (left * right).reshape(-1, DRAWS, DIM)
    return jnp.sum(product, axis=(0, 2))


def widen(coef):
    return jnp.repeat(coef, DIM)


def bit_count(axis):
    size = lax.axis_size(axis)
    bits = size.bit_length() - 1
    assert size == 1 << bits
    return size, bits


def swap_with(value, axis, size, bit, mask=None):
    mask = (1 << bit) if mask is None else mask
    pairs = [(i, i ^ mask) for i in range(size)]
    return lax.ppermute(value, axis, pairs)


def butterfly_psum(values):
    values = jnp.stack(values)
    for axis in ("item", "user"):
        size, bits = bit_count(axis)
        for bit in range(bits):
            values = values + swap_with(values, axis, size, bit)
    return values[0], values[1]


def code_rows(extra):
    high = extra.astype(jnp.bfloat16)
    rest = extra - high.astype(jnp.float32)
    mid = rest.astype(jnp.bfloat16)
    low = (rest - mid.astype(jnp.float32)).astype(jnp.bfloat16)
    return jnp.concatenate([high, mid, low])


def halve_sum(part, axis, send_type, extra=None, first_type=None):
    size, bits = bit_count(axis)
    me = lax.axis_index(axis)
    rows, width = part.shape[0] // size, part.shape[1]
    groups = [list(range(bits))[i : i + 2] for i in range(0, bits, 2)]
    left = list(range(bits))[::-1]
    buf = part.reshape([2] * bits + [rows, width])
    for stage, group in enumerate(groups):
        masks = [sum(1 << group[j] for j in range(len(group)) if (k >> j) & 1) for k in range(1 << len(group))]
        digit = sum(((me >> group[j]) & 1) << j for j in range(len(group)))

        def block_of(value):
            out = buf
            for j in sorted(range(len(group)), key=lambda j: -left.index(group[j])):
                out = lax.dynamic_index_in_dim(out, (value >> j) & 1, left.index(group[j]), keepdims=False)
            return out

        coded = extra is not None and first_type is not None
        stage_type = send_type if first_type is None else first_type
        total = block_of(digit)
        shape = total.shape
        if extra is not None:
            tail = jnp.concatenate([extra, jnp.zeros((2 * extra.shape[0], width), extra.dtype)]) if coded else extra
            total = jnp.concatenate([total.reshape(-1, width), tail])
        for k in range(1, len(masks)):
            send = block_of(digit ^ k).astype(stage_type)
            if extra is not None:
                tail = code_rows(extra) if coded else extra
                send = jnp.concatenate([send.reshape(-1, width), tail.astype(stage_type)])
            total = total + swap_with(send, axis, size, None, masks[k]).astype(jnp.float32)
        if extra is not None:
            count = extra.shape[0]
            if coded:
                tail = total[-3 * count :]
                total = total[: -3 * count].reshape(shape)
                extra = tail[:count] + tail[count : 2 * count] + tail[2 * count :]
            else:
                extra = total[-count:]
                total = total[:-count].reshape(shape)
        for bit in group:
            left.remove(bit)
        buf = total
    return buf.reshape(rows, width), extra


def double_gather(piece, axis, hold=None):
    size, bits = bit_count(axis)
    me = lax.axis_index(axis)
    order = list(range(bits))[::-1]
    groups = [order[:1]] if bits % 2 else []
    groups += [order[i : i + 2] for i in range(bits % 2, bits, 2)]
    buf = piece[None]
    kept = None
    for group in groups:
        masks = [sum(1 << group[-1 - j] for j in range(len(group)) if (k >> j) & 1) for k in range(1 << len(group))]
        pieces = [buf] + [swap_with(buf, axis, size, None, mask) for mask in masks[1:]]
        digit = sum(((me >> group[-1 - j]) & 1) << j for j in range(len(group)))
        ordered = []
        for place in range(len(masks)):
            pick = pieces[place]
            for held in range(1, len(masks)):
                pick = jnp.where(digit == held, pieces[place ^ held], pick)
            ordered.append(pick)
        buf = jnp.stack(ordered, axis=1).reshape((-1,) + piece.shape)
        if hold is not None and kept is None:
            buf, kept = lax.optimization_barrier((buf, hold))
    result = buf.reshape((size * piece.shape[0],) + piece.shape[1:])
    return result if hold is None else (result, kept)

def per_device(
    draws_user, draws_item, prior_user, prior_item, count_tiles, tile_blocks, tile_count
):
    width = DRAWS * DIM
    user_own = draws_user[0]
    item_own = draws_item[0]
    in_use = jnp.arange(TMAX, dtype=jnp.int32) < tile_count[0, 0]
    row_pick = (tile_blocks[0, 0, :, 0][:, None] == jnp.arange(RB, dtype=jnp.int32)) & in_use[:, None]
    col_pick = (tile_blocks[0, 0, :, 1][:, None] == jnp.arange(CB, dtype=jnp.int32)) & in_use[:, None]
    place = (row_pick[:, :, None] & col_pick[:, None, :]).astype(jnp.bfloat16)

    def build_counts(tiles):
        tiles_bf = tiles.astype(jnp.bfloat16)
        counts_bf = jnp.einsum(
            "trc,tij->ricj", place, tiles_bf, preferred_element_type=jnp.bfloat16
        ).reshape(RB * TILE, CB * TILE)
        counts_t = jnp.einsum(
            "trc,tij->cjri", place, tiles_bf, preferred_element_type=jnp.bfloat16
        ).reshape(CB * TILE, RB * TILE)
        tile_rows = jnp.sum(tiles_bf, axis=2, dtype=jnp.float32)
        tile_cols = jnp.sum(tiles_bf, axis=1, dtype=jnp.float32)
        user_deg = jnp.sum(jnp.where(row_pick[:, :, None], tile_rows[:, None, :], 0.0), axis=0)
        item_deg = jnp.sum(jnp.where(col_pick[:, :, None], tile_cols[:, None, :], 0.0), axis=0)
        return (counts_bf, counts_t, user_deg.reshape(-1), item_deg.reshape(-1))

    def cross_parts(user_range, item_range, counts):
        counts_bf, counts_t, user_deg, item_deg = counts
        to_users = jnp.dot(counts_bf, item_range, preferred_element_type=jnp.float32)
        to_users = to_users + user_deg[:, None] * user_range.astype(jnp.float32)
        to_items = jnp.dot(counts_t, user_range, preferred_element_type=jnp.float32)
        to_items = to_items + item_deg[:, None] * item_range.astype(jnp.float32)
        return (to_users, to_items)

    def user_range_of(user_vec):
        return double_gather(user_vec.astype(jnp.bfloat16), "item")

    def operate(user_vec, item_vec, counts):
        user_range = user_range_of(user_vec)
        if counts is None:
            item_range, tiles = double_gather(item_vec.astype(jnp.bfloat16), "user", count_tiles[0, 0])
            counts = build_counts(tiles)
        else:
            item_range = double_gather(item_vec.astype(jnp.bfloat16), "user")
        part_user, part_item = cross_parts(user_range, item_range, counts)
        prior_user_part = prior_term(user_vec, prior_user)
        prior_item_part = prior_term(item_vec, prior_item)
        norm_part = per_draw(user_vec, user_vec) + per_draw(item_vec, item_vec)
        cross_dot = per_draw(user_range.astype(jnp.float32), part_user) + per_draw(
            item_range.astype(jnp.float32), part_item
        )
        curve_part = (
            per_draw(user_vec, prior_user_part)
            + per_draw(item_vec, prior_item_part)
            + noise_prec * cross_dot
        )
        sums = jnp.concatenate([norm_part, curve_part]).reshape(1, 2 * DRAWS)
        sums = jnp.pad(sums, ((0, 7), (0, width - 2 * DRAWS)))
        total_user, _ = halve_sum(part_user, "item", jnp.bfloat16)
        total_item, sums = halve_sum(part_item, "user", jnp.float32, sums, jnp.bfloat16)
        sums = sums[0, : 2 * DRAWS]
        size, bits = bit_count("item")
        for bit in range(bits):
            sums = sums + swap_with(sums, "item", size, bit)
        image_user = prior_user_part + noise_prec * total_user
        image_item = prior_item_part + noise_prec * total_item
        return (image_user, image_item, sums[:DRAWS], sums[DRAWS:], counts)

    sol_user = jnp.zeros_like(user_own)
    sol_item = jnp.zeros_like(item_own)
    res_user, res_item = (user_own, item_own)
    dir_user, dir_item = (user_own, item_own)

    along_user, along_item, norm_now, curve, counts = operate(res_user, res_item, None)
    step_len = norm_now / curve
    for iteration in range(ITERS):
        sol_user = sol_user + widen(step_len) * dir_user
        sol_item = sol_item + widen(step_len) * dir_item
        res_user = res_user - widen(step_len) * along_user
        res_item = res_item - widen(step_len) * along_item
        if iteration + 1 < ITERS:
            image_user, image_item, norm_next, curve, _ = operate(res_user, res_item, counts)
            beta_coef = norm_next / norm_now
            step_len = norm_next / (curve - beta_coef * norm_next / step_len)
            dir_user = res_user + widen(beta_coef) * dir_user
            dir_item = res_item + widen(beta_coef) * dir_item
            along_user = image_user + widen(beta_coef) * along_user
            along_item = image_item + widen(beta_coef) * along_item
            norm_now = norm_next
    return (sol_user[None], sol_item[None], res_user[None], res_item[None])


def solution(mesh):
    in_specs = (
        P("user", "item", None),
        P("item", "user", None),
        P(),
        P(),
        P("user", "item", None, None, None),
        P("user", "item", None, None),
        P("user", "item"),
    )
    out_specs = (
        P("user", "item", None),
        P("item", "user", None),
        P("user", "item", None),
        P("item", "user", None),
    )
    return jax.shard_map(
        per_device, mesh=mesh, in_specs=in_specs, out_specs=out_specs, check_vma=False
    )
```

```python
import jax
import jax.numpy as jnp
from jax import lax
from jax.sharding import PartitionSpec as P

DIM = 64
DRAWS = 4
TILE = 256
RB = 3
CB = 4
TMAX = 12
ITERS = 2


top_prec = lax.Precision.HIGHEST
noise_prec = 0.03125


def prior_term(field_vec, prior_mat):
    row_total = field_vec.shape[0]
    grouped = field_vec.reshape(row_total, DRAWS, DIM)
    mixed = jnp.einsum("nde,ef->ndf", grouped, prior_mat, precision=top_prec)
    return mixed.reshape(row_total, DRAWS * DIM)


def per_draw(left, right):
    product = (left * right).reshape(-1, DRAWS, DIM)
    return jnp.sum(product, axis=(0, 2))


def widen(coef):
    return jnp.repeat(coef, DIM)


def bit_count(axis):
    size = lax.axis_size(axis)
    bits = size.bit_length() - 1
    assert size == 1 << bits
    return size, bits


def swap_with(value, axis, size, bit, mask=None):
    mask = (1 << bit) if mask is None else mask
    pairs = [(i, i ^ mask) for i in range(size)]
    return lax.ppermute(value, axis, pairs)


def butterfly_psum(values):
    values = jnp.stack(values)
    for axis in ("item", "user"):
        size, bits = bit_count(axis)
        for bit in range(bits):
            values = values + swap_with(values, axis, size, bit)
    return values[0], values[1]


def code_rows(extra):
    high = extra.astype(jnp.bfloat16)
    rest = extra - high.astype(jnp.float32)
    mid = rest.astype(jnp.bfloat16)
    low = (rest - mid.astype(jnp.float32)).astype(jnp.bfloat16)
    return jnp.concatenate([high, mid, low])


def halve_sum(part, axis, send_type, extra=None, first_type=None):
    size, bits = bit_count(axis)
    me = lax.axis_index(axis)
    rows, width = part.shape[0] // size, part.shape[1]
    groups = [list(range(bits))[i : i + 2] for i in range(0, bits, 2)]
    left = list(range(bits))[::-1]
    buf = part.reshape([2] * bits + [rows, width])
    for stage, group in enumerate(groups):
        masks = [sum(1 << group[j] for j in range(len(group)) if (k >> j) & 1) for k in range(1 << len(group))]
        digit = sum(((me >> group[j]) & 1) << j for j in range(len(group)))

        def block_of(value):
            out = buf
            for j in sorted(range(len(group)), key=lambda j: -left.index(group[j])):
                out = lax.dynamic_index_in_dim(out, (value >> j) & 1, left.index(group[j]), keepdims=False)
            return out

        coded = extra is not None and first_type is not None
        stage_type = send_type if first_type is None else first_type
        total = block_of(digit)
        shape = total.shape
        if extra is not None:
            tail = jnp.concatenate([extra, jnp.zeros((2 * extra.shape[0], width), extra.dtype)]) if coded else extra
            total = jnp.concatenate([total.reshape(-1, width), tail])
        for k in range(1, len(masks)):
            send = block_of(digit ^ k).astype(stage_type)
            if extra is not None:
                tail = code_rows(extra) if coded else extra
                send = jnp.concatenate([send.reshape(-1, width), tail.astype(stage_type)])
            total = total + swap_with(send, axis, size, None, masks[k]).astype(jnp.float32)
        if extra is not None:
            count = extra.shape[0]
            if coded:
                tail = total[-3 * count :]
                total = total[: -3 * count].reshape(shape)
                extra = tail[:count] + tail[count : 2 * count] + tail[2 * count :]
            else:
                extra = total[-count:]
                total = total[:-count].reshape(shape)
        for bit in group:
            left.remove(bit)
        buf = total
    return buf.reshape(rows, width), extra


def double_gather(piece, axis, hold=None):
    size, bits = bit_count(axis)
    me = lax.axis_index(axis)
    order = list(range(bits))[::-1]
    groups = [order[:1]] if bits % 2 else []
    groups += [order[i : i + 2] for i in range(bits % 2, bits, 2)]
    buf = piece[None]
    kept = None
    for group in groups:
        masks = [sum(1 << group[-1 - j] for j in range(len(group)) if (k >> j) & 1) for k in range(1 << len(group))]
        pieces = [buf] + [swap_with(buf, axis, size, None, mask) for mask in masks[1:]]
        digit = sum(((me >> group[-1 - j]) & 1) << j for j in range(len(group)))
        ordered = []
        for place in range(len(masks)):
            pick = pieces[place]
            for held in range(1, len(masks)):
                pick = jnp.where(digit == held, pieces[place ^ held], pick)
            ordered.append(pick)
        buf = jnp.stack(ordered, axis=1).reshape((-1,) + piece.shape)
        if hold is not None and kept is None:
            buf, kept = lax.optimization_barrier((buf, hold))
    result = buf.reshape((size * piece.shape[0],) + piece.shape[1:])
    return result if hold is None else (result, kept)

def per_device(
    draws_user, draws_item, prior_user, prior_item, count_tiles, tile_blocks, tile_count
):
    width = DRAWS * DIM
    user_own = draws_user[0]
    item_own = draws_item[0]
    in_use = jnp.arange(TMAX, dtype=jnp.int32) < tile_count[0, 0]
    row_pick = (tile_blocks[0, 0, :, 0][:, None] == jnp.arange(RB, dtype=jnp.int32)) & in_use[:, None]
    col_pick = (tile_blocks[0, 0, :, 1][:, None] == jnp.arange(CB, dtype=jnp.int32)) & in_use[:, None]
    place = (row_pick[:, :, None] & col_pick[:, None, :]).astype(jnp.bfloat16)

    def build_counts(tiles):
        tiles_bf = tiles.astype(jnp.bfloat16)
        counts_bf = jnp.einsum(
            "trc,tij->ricj", place, tiles_bf, preferred_element_type=jnp.bfloat16
        ).reshape(RB * TILE, CB * TILE)
        counts_t = jnp.einsum(
            "trc,tij->cjri", place, tiles_bf, preferred_element_type=jnp.bfloat16
        ).reshape(CB * TILE, RB * TILE)
        tile_rows = jnp.sum(tiles_bf, axis=2, dtype=jnp.float32)
        tile_cols = jnp.sum(tiles_bf, axis=1, dtype=jnp.float32)
        user_deg = jnp.sum(jnp.where(row_pick[:, :, None], tile_rows[:, None, :], 0.0), axis=0)
        item_deg = jnp.sum(jnp.where(col_pick[:, :, None], tile_cols[:, None, :], 0.0), axis=0)
        return (counts_bf, counts_t, user_deg.reshape(-1), item_deg.reshape(-1))

    def cross_parts(user_range, item_range, counts):
        counts_bf, counts_t, user_deg, item_deg = counts
        to_users = jnp.dot(counts_bf, item_range, preferred_element_type=jnp.float32)
        to_users = to_users + user_deg[:, None] * user_range.astype(jnp.float32)
        to_items = jnp.dot(counts_t, user_range, preferred_element_type=jnp.float32)
        to_items = to_items + item_deg[:, None] * item_range.astype(jnp.float32)
        return (to_users, to_items)

    def user_range_of(user_vec):
        return double_gather(user_vec.astype(jnp.bfloat16), "item")

    def operate(user_vec, item_vec, counts):
        user_range = user_range_of(user_vec)
        if counts is None:
            item_range, tiles = double_gather(item_vec.astype(jnp.bfloat16), "user", count_tiles[0, 0])
            counts = build_counts(tiles)
        else:
            item_range = double_gather(item_vec.astype(jnp.bfloat16), "user")
        part_user, part_item = cross_parts(user_range, item_range, counts)
        prior_user_part = prior_term(user_vec, prior_user)
        prior_item_part = prior_term(item_vec, prior_item)
        norm_part = per_draw(user_vec, user_vec) + per_draw(item_vec, item_vec)
        cross_dot = per_draw(user_range.astype(jnp.float32), part_user) + per_draw(
            item_range.astype(jnp.float32), part_item
        )
        curve_part = (
            per_draw(user_vec, prior_user_part)
            + per_draw(item_vec, prior_item_part)
            + noise_prec * cross_dot
        )
        sums = jnp.concatenate([norm_part, curve_part]).reshape(1, 2 * DRAWS)
        sums = jnp.pad(sums, ((0, 7), (0, width - 2 * DRAWS)))
        total_user, _ = halve_sum(part_user, "item", jnp.bfloat16)
        total_item, sums = halve_sum(part_item, "user", jnp.float32, sums, jnp.bfloat16)
        sums = sums[0, : 2 * DRAWS]
        size, bits = bit_count("item")
        for bit in range(bits):
            sums = sums + swap_with(sums, "item", size, bit)
        image_user = prior_user_part + noise_prec * total_user
        image_item = prior_item_part + noise_prec * total_item
        return (image_user, image_item, sums[:DRAWS], sums[DRAWS:], counts)

    sol_user = jnp.zeros_like(user_own)
    sol_item = jnp.zeros_like(item_own)
    res_user, res_item = (user_own, item_own)
    dir_user, dir_item = (user_own, item_own)

    along_user, along_item, norm_now, curve, counts = operate(res_user, res_item, None)
    step_len = norm_now / curve
    for iteration in range(ITERS):
        sol_user = sol_user + widen(step_len) * dir_user
        sol_item = sol_item + widen(step_len) * dir_item
        res_user = res_user - widen(step_len) * along_user
        res_item = res_item - widen(step_len) * along_item
        if iteration + 1 < ITERS:
            image_user, image_item, norm_next, curve, _ = operate(res_user, res_item, counts)
            beta_coef = norm_next / norm_now
            step_len = norm_next / (curve - beta_coef * norm_next / step_len)
            dir_user = res_user + widen(beta_coef) * dir_user
            dir_item = res_item + widen(beta_coef) * dir_item
            along_user = image_user + widen(beta_coef) * along_user
            along_item = image_item + widen(beta_coef) * along_item
            norm_now = norm_next
    return (sol_user[None], sol_item[None], res_user[None], res_item[None])


def solution(mesh):
    in_specs = (
        P("user", "item", None),
        P("item", "user", None),
        P(),
        P(),
        P("user", "item", None, None, None),
        P("user", "item", None, None),
        P("user", "item"),
    )
    out_specs = (
        P("user", "item", None),
        P("item", "user", None),
        P("user", "item", None),
        P("item", "user", None),
    )
    return jax.shard_map(
        per_device, mesh=mesh, in_specs=in_specs, out_specs=out_specs, check_vma=False
    )
```

```python
import jax
import jax.numpy as jnp
from jax import lax
from jax.sharding import PartitionSpec as P

DIM = 64
DRAWS = 4
TILE = 256
RB = 3
CB = 4
TMAX = 12
ITERS = 2


top_prec = lax.Precision.HIGHEST
noise_prec = 0.03125


def prior_term(field_vec, prior_mat):
    row_total = field_vec.shape[0]
    grouped = field_vec.reshape(row_total * DRAWS, DIM)
    mixed = jnp.dot(grouped, prior_mat, precision=top_prec)
    return mixed.reshape(row_total, DRAWS * DIM)


def per_draw(left, right):
    product = (left * right).reshape(-1, DRAWS, DIM)
    return jnp.sum(product, axis=(0, 2))


def widen(coef):
    return jnp.repeat(coef, DIM)


def bit_count(axis):
    size = lax.axis_size(axis)
    bits = size.bit_length() - 1
    assert size == 1 << bits
    return size, bits


def swap_with(value, axis, size, bit, mask=None):
    mask = (1 << bit) if mask is None else mask
    pairs = [(i, i ^ mask) for i in range(size)]
    return lax.ppermute(value, axis, pairs)


def butterfly_psum(values):
    values = jnp.stack(values)
    for axis in ("item", "user"):
        size, bits = bit_count(axis)
        for bit in range(bits):
            values = values + swap_with(values, axis, size, bit)
    return values[0], values[1]


def code_rows(extra):
    high = extra.astype(jnp.bfloat16)
    rest = extra - high.astype(jnp.float32)
    mid = rest.astype(jnp.bfloat16)
    low = (rest - mid.astype(jnp.float32)).astype(jnp.bfloat16)
    return jnp.concatenate([high, mid, low])


def halve_sum(part, axis, send_type, extra=None, first_type=None):
    size, bits = bit_count(axis)
    me = lax.axis_index(axis)
    rows, width = part.shape[0] // size, part.shape[1]
    groups = [list(range(bits))[i : i + 2] for i in range(0, bits, 2)]
    left = list(range(bits))[::-1]
    buf = part.reshape([2] * bits + [rows, width])
    for stage, group in enumerate(groups):
        masks = [sum(1 << group[j] for j in range(len(group)) if (k >> j) & 1) for k in range(1 << len(group))]
        digit = sum(((me >> group[j]) & 1) << j for j in range(len(group)))

        def block_of(value):
            out = buf
            for j in sorted(range(len(group)), key=lambda j: -left.index(group[j])):
                out = lax.dynamic_index_in_dim(out, (value >> j) & 1, left.index(group[j]), keepdims=False)
            return out

        coded = extra is not None and first_type is not None
        stage_type = send_type if first_type is None else first_type
        total = block_of(digit)
        shape = total.shape
        if extra is not None:
            tail = jnp.concatenate([extra, jnp.zeros((2 * extra.shape[0], width), extra.dtype)]) if coded else extra
            total = jnp.concatenate([total.reshape(-1, width), tail])
        for k in range(1, len(masks)):
            send = block_of(digit ^ k).astype(stage_type)
            if extra is not None:
                tail = code_rows(extra) if coded else extra
                send = jnp.concatenate([send.reshape(-1, width), tail.astype(stage_type)])
            total = total + swap_with(send, axis, size, None, masks[k]).astype(jnp.float32)
        if extra is not None:
            count = extra.shape[0]
            if coded:
                tail = total[-3 * count :]
                total = total[: -3 * count].reshape(shape)
                extra = tail[:count] + tail[count : 2 * count] + tail[2 * count :]
            else:
                extra = total[-count:]
                total = total[:-count].reshape(shape)
        for bit in group:
            left.remove(bit)
        buf = total
    return buf.reshape(rows, width), extra


def double_gather(piece, axis, hold=None):
    size, bits = bit_count(axis)
    me = lax.axis_index(axis)
    order = list(range(bits))[::-1]
    groups = [order[:1]] if bits % 2 else []
    groups += [order[i : i + 2] for i in range(bits % 2, bits, 2)]
    buf = piece[None]
    kept = None
    for group in groups:
        masks = [sum(1 << group[-1 - j] for j in range(len(group)) if (k >> j) & 1) for k in range(1 << len(group))]
        pieces = [buf] + [swap_with(buf, axis, size, None, mask) for mask in masks[1:]]
        digit = sum(((me >> group[-1 - j]) & 1) << j for j in range(len(group)))
        ordered = []
        for place in range(len(masks)):
            pick = pieces[place]
            for held in range(1, len(masks)):
                pick = jnp.where(digit == held, pieces[place ^ held], pick)
            ordered.append(pick)
        buf = jnp.stack(ordered, axis=1).reshape((-1,) + piece.shape)
        if hold is not None and kept is None:
            buf, kept = lax.optimization_barrier((buf, hold))
    result = buf.reshape((size * piece.shape[0],) + piece.shape[1:])
    return result if hold is None else (result, kept)

def per_device(
    draws_user, draws_item, prior_user, prior_item, count_tiles, tile_blocks, tile_count
):
    width = DRAWS * DIM
    user_own = draws_user[0]
    item_own = draws_item[0]
    in_use = jnp.arange(TMAX, dtype=jnp.int32) < tile_count[0, 0]
    row_pick = (tile_blocks[0, 0, :, 0][:, None] == jnp.arange(RB, dtype=jnp.int32)) & in_use[:, None]
    col_pick = (tile_blocks[0, 0, :, 1][:, None] == jnp.arange(CB, dtype=jnp.int32)) & in_use[:, None]
    place = (row_pick[:, :, None] & col_pick[:, None, :]).astype(jnp.bfloat16)

    def build_counts(tiles):
        tiles_bf = tiles.astype(jnp.bfloat16)
        counts_bf = jnp.einsum(
            "trc,tij->ricj", place, tiles_bf, preferred_element_type=jnp.bfloat16
        ).reshape(RB * TILE, CB * TILE)
        counts_t = jnp.einsum(
            "trc,tij->cjri", place, tiles_bf, preferred_element_type=jnp.bfloat16
        ).reshape(CB * TILE, RB * TILE)
        tile_rows = jnp.sum(tiles_bf, axis=2, dtype=jnp.float32)
        tile_cols = jnp.sum(tiles_bf, axis=1, dtype=jnp.float32)
        user_deg = jnp.sum(jnp.where(row_pick[:, :, None], tile_rows[:, None, :], 0.0), axis=0)
        item_deg = jnp.sum(jnp.where(col_pick[:, :, None], tile_cols[:, None, :], 0.0), axis=0)
        return (counts_bf, counts_t, user_deg.reshape(-1), item_deg.reshape(-1))

    def cross_parts(user_range, item_range, counts):
        counts_bf, counts_t, user_deg, item_deg = counts
        to_users = jnp.dot(counts_bf, item_range, preferred_element_type=jnp.float32)
        to_users = to_users + user_deg[:, None] * user_range.astype(jnp.float32)
        to_items = jnp.dot(counts_t, user_range, preferred_element_type=jnp.float32)
        to_items = to_items + item_deg[:, None] * item_range.astype(jnp.float32)
        return (to_users, to_items)

    def user_range_of(user_vec):
        return double_gather(user_vec.astype(jnp.bfloat16), "item")

    def operate(user_vec, item_vec, counts):
        user_range = user_range_of(user_vec)
        if counts is None:
            item_range, (tiles, user_vec, item_vec) = double_gather(
                item_vec.astype(jnp.bfloat16), "user", (count_tiles[0, 0], user_vec, item_vec)
            )
            counts = build_counts(tiles)
        else:
            item_range = double_gather(item_vec.astype(jnp.bfloat16), "user")
        part_user, part_item = cross_parts(user_range, item_range, counts)
        prior_user_part = prior_term(user_vec, prior_user)
        prior_item_part = prior_term(item_vec, prior_item)
        norm_part = per_draw(user_vec, user_vec) + per_draw(item_vec, item_vec)
        cross_dot = per_draw(user_range.astype(jnp.float32), part_user) + per_draw(
            item_range.astype(jnp.float32), part_item
        )
        curve_part = (
            per_draw(user_vec, prior_user_part)
            + per_draw(item_vec, prior_item_part)
            + noise_prec * cross_dot
        )
        sums = jnp.concatenate([norm_part, curve_part]).reshape(1, 2 * DRAWS)
        sums = jnp.pad(sums, ((0, 7), (0, width - 2 * DRAWS)))
        total_user, _ = halve_sum(part_user, "item", jnp.bfloat16)
        total_item, sums = halve_sum(part_item, "user", jnp.float32, sums, jnp.bfloat16)
        sums = sums[0, : 2 * DRAWS]
        size, bits = bit_count("item")
        for bit in range(bits):
            sums = sums + swap_with(sums, "item", size, bit)
        image_user = prior_user_part + noise_prec * total_user
        image_item = prior_item_part + noise_prec * total_item
        return (image_user, image_item, sums[:DRAWS], sums[DRAWS:], counts)

    sol_user = jnp.zeros_like(user_own)
    sol_item = jnp.zeros_like(item_own)
    res_user, res_item = (user_own, item_own)
    dir_user, dir_item = (user_own, item_own)

    along_user, along_item, norm_now, curve, counts = operate(res_user, res_item, None)
    step_len = norm_now / curve
    for iteration in range(ITERS):
        sol_user = sol_user + widen(step_len) * dir_user
        sol_item = sol_item + widen(step_len) * dir_item
        res_user = res_user - widen(step_len) * along_user
        res_item = res_item - widen(step_len) * along_item
        if iteration + 1 < ITERS:
            image_user, image_item, norm_next, curve, _ = operate(res_user, res_item, counts)
            beta_coef = norm_next / norm_now
            step_len = norm_next / (curve - beta_coef * norm_next / step_len)
            dir_user = res_user + widen(beta_coef) * dir_user
            dir_item = res_item + widen(beta_coef) * dir_item
            along_user = image_user + widen(beta_coef) * along_user
            along_item = image_item + widen(beta_coef) * along_item
            norm_now = norm_next
    return (sol_user[None], sol_item[None], res_user[None], res_item[None])


def solution(mesh):
    in_specs = (
        P("user", "item", None),
        P("item", "user", None),
        P(),
        P(),
        P("user", "item", None, None, None),
        P("user", "item", None, None),
        P("user", "item"),
    )
    out_specs = (
        P("user", "item", None),
        P("item", "user", None),
        P("user", "item", None),
        P("item", "user", None),
    )
    return jax.shard_map(
        per_device, mesh=mesh, in_specs=in_specs, out_specs=out_specs, check_vma=False
    )
```

```python
import jax
import jax.numpy as jnp
from jax import lax
from jax.sharding import PartitionSpec as P

DIM = 64
DRAWS = 4
TILE = 256
RB = 3
CB = 4
TMAX = 12
ITERS = 2


top_prec = lax.Precision.HIGHEST
noise_prec = 0.03125


def prior_term(field_vec, prior_mat):
    row_total = field_vec.shape[0]
    grouped = field_vec.reshape(row_total * DRAWS, DIM)
    mixed = jnp.dot(grouped, prior_mat, precision=top_prec)
    return mixed.reshape(row_total, DRAWS * DIM)


def per_draw(left, right):
    product = (left * right).reshape(-1, DRAWS, DIM)
    return jnp.sum(product, axis=(0, 2))


def widen(coef):
    return jnp.repeat(coef, DIM)


def bit_count(axis):
    size = lax.axis_size(axis)
    bits = size.bit_length() - 1
    assert size == 1 << bits
    return size, bits


def swap_with(value, axis, size, bit, mask=None):
    mask = (1 << bit) if mask is None else mask
    pairs = [(i, i ^ mask) for i in range(size)]
    return lax.ppermute(value, axis, pairs)


def butterfly_psum(values):
    values = jnp.stack(values)
    for axis in ("item", "user"):
        size, bits = bit_count(axis)
        for bit in range(bits):
            values = values + swap_with(values, axis, size, bit)
    return values[0], values[1]


def code_rows(extra):
    high = extra.astype(jnp.bfloat16)
    rest = extra - high.astype(jnp.float32)
    mid = rest.astype(jnp.bfloat16)
    low = (rest - mid.astype(jnp.float32)).astype(jnp.bfloat16)
    return jnp.concatenate([high, mid, low])


def halve_sum(part, axis, send_type, extra=None, first_type=None):
    size, bits = bit_count(axis)
    me = lax.axis_index(axis)
    rows, width = part.shape[0] // size, part.shape[1]
    groups = [list(range(bits))[i : i + 2] for i in range(0, bits, 2)]
    left = list(range(bits))[::-1]
    buf = part.reshape([2] * bits + [rows, width])
    for stage, group in enumerate(groups):
        masks = [sum(1 << group[j] for j in range(len(group)) if (k >> j) & 1) for k in range(1 << len(group))]
        digit = sum(((me >> group[j]) & 1) << j for j in range(len(group)))

        def block_of(value):
            out = buf
            for j in sorted(range(len(group)), key=lambda j: -left.index(group[j])):
                out = lax.dynamic_index_in_dim(out, (value >> j) & 1, left.index(group[j]), keepdims=False)
            return out

        coded = extra is not None and first_type is not None
        stage_type = send_type if first_type is None else first_type
        total = block_of(digit)
        shape = total.shape
        if extra is not None:
            tail = jnp.concatenate([extra, jnp.zeros((2 * extra.shape[0], width), extra.dtype)]) if coded else extra
            total = jnp.concatenate([total.reshape(-1, width), tail])
        for k in range(1, len(masks)):
            send = block_of(digit ^ k).astype(stage_type)
            if extra is not None:
                tail = code_rows(extra) if coded else extra
                send = jnp.concatenate([send.reshape(-1, width), tail.astype(stage_type)])
            total = total + swap_with(send, axis, size, None, masks[k]).astype(jnp.float32)
        if extra is not None:
            count = extra.shape[0]
            if coded:
                tail = total[-3 * count :]
                total = total[: -3 * count].reshape(shape)
                extra = tail[:count] + tail[count : 2 * count] + tail[2 * count :]
            else:
                extra = total[-count:]
                total = total[:-count].reshape(shape)
        for bit in group:
            left.remove(bit)
        buf = total
    return buf.reshape(rows, width), extra


def double_gather(piece, axis, hold=None):
    size, bits = bit_count(axis)
    me = lax.axis_index(axis)
    order = list(range(bits))[::-1]
    groups = [order[:1]] if bits % 2 else []
    groups += [order[i : i + 2] for i in range(bits % 2, bits, 2)]
    buf = piece[None]
    kept = None
    for group in groups:
        masks = [sum(1 << group[-1 - j] for j in range(len(group)) if (k >> j) & 1) for k in range(1 << len(group))]
        pieces = [buf] + [swap_with(buf, axis, size, None, mask) for mask in masks[1:]]
        digit = sum(((me >> group[-1 - j]) & 1) << j for j in range(len(group)))
        ordered = []
        for place in range(len(masks)):
            pick = pieces[place]
            for held in range(1, len(masks)):
                pick = jnp.where(digit == held, pieces[place ^ held], pick)
            ordered.append(pick)
        buf = jnp.stack(ordered, axis=1).reshape((-1,) + piece.shape)
        if hold is not None and kept is None:
            buf, kept = lax.optimization_barrier((buf, hold))
    result = buf.reshape((size * piece.shape[0],) + piece.shape[1:])
    return result if hold is None else (result, kept)

def per_device(
    draws_user, draws_item, prior_user, prior_item, count_tiles, tile_blocks, tile_count
):
    width = DRAWS * DIM
    user_own = draws_user[0]
    item_own = draws_item[0]
    in_use = jnp.arange(TMAX, dtype=jnp.int32) < tile_count[0, 0]
    row_pick = (tile_blocks[0, 0, :, 0][:, None] == jnp.arange(RB, dtype=jnp.int32)) & in_use[:, None]
    col_pick = (tile_blocks[0, 0, :, 1][:, None] == jnp.arange(CB, dtype=jnp.int32)) & in_use[:, None]
    place = (row_pick[:, :, None] & col_pick[:, None, :]).astype(jnp.bfloat16)

    def build_counts(tiles):
        tiles_bf = tiles.astype(jnp.bfloat16)
        counts_bf = jnp.einsum(
            "trc,tij->ricj", place, tiles_bf, preferred_element_type=jnp.bfloat16
        ).reshape(RB * TILE, CB * TILE)
        counts_t = jnp.einsum(
            "trc,tij->cjri", place, tiles_bf, preferred_element_type=jnp.bfloat16
        ).reshape(CB * TILE, RB * TILE)
        tile_rows = jnp.sum(tiles_bf, axis=2, dtype=jnp.float32)
        tile_cols = jnp.sum(tiles_bf, axis=1, dtype=jnp.float32)
        user_deg = jnp.sum(jnp.where(row_pick[:, :, None], tile_rows[:, None, :], 0.0), axis=0)
        item_deg = jnp.sum(jnp.where(col_pick[:, :, None], tile_cols[:, None, :], 0.0), axis=0)
        return (counts_bf, counts_t, user_deg.reshape(-1), item_deg.reshape(-1))

    def cross_parts(user_range, item_range, counts):
        counts_bf, counts_t, user_deg, item_deg = counts
        to_users = jnp.dot(counts_bf, item_range, preferred_element_type=jnp.float32)
        to_users = to_users + user_deg[:, None] * user_range.astype(jnp.float32)
        to_items = jnp.dot(counts_t, user_range, preferred_element_type=jnp.float32)
        to_items = to_items + item_deg[:, None] * item_range.astype(jnp.float32)
        return (to_users, to_items)

    def user_range_of(user_vec):
        return double_gather(user_vec.astype(jnp.bfloat16), "item")

    def operate(user_vec, item_vec, counts):
        user_range = user_range_of(user_vec)
        if counts is None:
            item_range, (tiles, user_vec, item_vec) = double_gather(
                item_vec.astype(jnp.bfloat16), "user", (count_tiles[0, 0], user_vec, item_vec)
            )
            counts = build_counts(tiles)
        else:
            item_range = double_gather(item_vec.astype(jnp.bfloat16), "user")
        part_user, part_item = cross_parts(user_range, item_range, counts)
        prior_user_part = prior_term(user_vec, prior_user)
        prior_item_part = prior_term(item_vec, prior_item)
        norm_part = per_draw(user_vec, user_vec) + per_draw(item_vec, item_vec)
        cross_dot = per_draw(user_range.astype(jnp.float32), part_user) + per_draw(
            item_range.astype(jnp.float32), part_item
        )
        curve_part = (
            per_draw(user_vec, prior_user_part)
            + per_draw(item_vec, prior_item_part)
            + noise_prec * cross_dot
        )
        sums = jnp.concatenate([norm_part, curve_part]).reshape(1, 2 * DRAWS)
        sums = jnp.pad(sums, ((0, 0), (0, width - 2 * DRAWS)))
        total_user, _ = halve_sum(part_user, "item", jnp.bfloat16)
        total_item, sums = halve_sum(part_item, "user", jnp.float32, sums, jnp.bfloat16)
        sums = sums[0, : 2 * DRAWS]
        size, bits = bit_count("item")
        for bit in range(bits):
            sums = sums + swap_with(sums, "item", size, bit)
        image_user = prior_user_part + noise_prec * total_user
        image_item = prior_item_part + noise_prec * total_item
        return (image_user, image_item, sums[:DRAWS], sums[DRAWS:], counts)

    sol_user = jnp.zeros_like(user_own)
    sol_item = jnp.zeros_like(item_own)
    res_user, res_item = (user_own, item_own)
    dir_user, dir_item = (user_own, item_own)

    along_user, along_item, norm_now, curve, counts = operate(res_user, res_item, None)
    step_len = norm_now / curve
    for iteration in range(ITERS):
        sol_user = sol_user + widen(step_len) * dir_user
        sol_item = sol_item + widen(step_len) * dir_item
        res_user = res_user - widen(step_len) * along_user
        res_item = res_item - widen(step_len) * along_item
        if iteration + 1 < ITERS:
            image_user, image_item, norm_next, curve, _ = operate(res_user, res_item, counts)
            beta_coef = norm_next / norm_now
            step_len = norm_next / (curve - beta_coef * norm_next / step_len)
            dir_user = res_user + widen(beta_coef) * dir_user
            dir_item = res_item + widen(beta_coef) * dir_item
            along_user = image_user + widen(beta_coef) * along_user
            along_item = image_item + widen(beta_coef) * along_item
            norm_now = norm_next
    return (sol_user[None], sol_item[None], res_user[None], res_item[None])


def solution(mesh):
    in_specs = (
        P("user", "item", None),
        P("item", "user", None),
        P(),
        P(),
        P("user", "item", None, None, None),
        P("user", "item", None, None),
        P("user", "item"),
    )
    out_specs = (
        P("user", "item", None),
        P("item", "user", None),
        P("user", "item", None),
        P("item", "user", None),
    )
    return jax.shard_map(
        per_device, mesh=mesh, in_specs=in_specs, out_specs=out_specs, check_vma=False
    )
```

```python
import jax
import jax.numpy as jnp
from jax import lax
from jax.sharding import PartitionSpec as P

DIM = 64
DRAWS = 4
TILE = 256
RB = 3
CB = 4
TMAX = 12
ITERS = 2


top_prec = lax.Precision.HIGHEST
noise_prec = 0.03125


def prior_term(field_vec, prior_mat):
    row_total = field_vec.shape[0]
    grouped = field_vec.reshape(row_total * DRAWS, DIM)
    mixed = jnp.dot(grouped, prior_mat, precision=top_prec)
    return mixed.reshape(row_total, DRAWS * DIM)


def per_draw(left, right):
    product = (left * right).reshape(-1, DRAWS, DIM)
    return jnp.sum(product, axis=(0, 2))


def widen(coef):
    return jnp.repeat(coef, DIM)


def bit_count(axis):
    size = lax.axis_size(axis)
    bits = size.bit_length() - 1
    assert size == 1 << bits
    return size, bits


def swap_with(value, axis, size, bit, mask=None):
    mask = (1 << bit) if mask is None else mask
    pairs = [(i, i ^ mask) for i in range(size)]
    return lax.ppermute(value, axis, pairs)


def butterfly_psum(values):
    values = jnp.stack(values)
    for axis in ("item", "user"):
        size, bits = bit_count(axis)
        for bit in range(bits):
            values = values + swap_with(values, axis, size, bit)
    return values[0], values[1]


def code_rows(extra):
    high = extra.astype(jnp.bfloat16)
    rest = extra - high.astype(jnp.float32)
    mid = rest.astype(jnp.bfloat16)
    low = (rest - mid.astype(jnp.float32)).astype(jnp.bfloat16)
    return jnp.concatenate([high, mid, low])


def halve_sum(part, axis, send_type, extra=None, first_type=None):
    size, bits = bit_count(axis)
    me = lax.axis_index(axis)
    rows, width = part.shape[0] // size, part.shape[1]
    groups = [list(range(bits))[i : i + 2] for i in range(0, bits, 2)]
    left = list(range(bits))[::-1]
    buf = part.reshape([2] * bits + [rows, width])
    for stage, group in enumerate(groups):
        masks = [sum(1 << group[j] for j in range(len(group)) if (k >> j) & 1) for k in range(1 << len(group))]
        digit = sum(((me >> group[j]) & 1) << j for j in range(len(group)))

        def block_of(value):
            out = buf
            for j in sorted(range(len(group)), key=lambda j: -left.index(group[j])):
                out = lax.dynamic_index_in_dim(out, (value >> j) & 1, left.index(group[j]), keepdims=False)
            return out

        coded = extra is not None and first_type is not None
        stage_type = send_type if first_type is None else first_type
        total = block_of(digit)
        shape = total.shape
        if extra is not None:
            tail = jnp.concatenate([extra, jnp.zeros((2 * extra.shape[0], width), extra.dtype)]) if coded else extra
            total = jnp.concatenate([total.reshape(-1, width), tail])
        for k in range(1, len(masks)):
            send = block_of(digit ^ k).astype(stage_type)
            if extra is not None:
                tail = code_rows(extra) if coded else extra
                send = jnp.concatenate([send.reshape(-1, width), tail.astype(stage_type)])
            total = total + swap_with(send, axis, size, None, masks[k]).astype(jnp.float32)
        if extra is not None:
            count = extra.shape[0]
            if coded:
                tail = total[-3 * count :]
                total = total[: -3 * count].reshape(shape)
                extra = tail[:count] + tail[count : 2 * count] + tail[2 * count :]
            else:
                extra = total[-count:]
                total = total[:-count].reshape(shape)
        for bit in group:
            left.remove(bit)
        buf = total
    return buf.reshape(rows, width), extra


def double_gather(piece, axis, hold=None):
    size, bits = bit_count(axis)
    me = lax.axis_index(axis)
    order = list(range(bits))[::-1]
    groups = [order[:1]] if bits % 2 else []
    groups += [order[i : i + 2] for i in range(bits % 2, bits, 2)]
    buf = piece[None]
    kept = None
    for group in groups:
        masks = [sum(1 << group[-1 - j] for j in range(len(group)) if (k >> j) & 1) for k in range(1 << len(group))]
        pieces = [buf] + [swap_with(buf, axis, size, None, mask) for mask in masks[1:]]
        digit = sum(((me >> group[-1 - j]) & 1) << j for j in range(len(group)))
        ordered = []
        for place in range(len(masks)):
            pick = pieces[place]
            for held in range(1, len(masks)):
                pick = jnp.where(digit == held, pieces[place ^ held], pick)
            ordered.append(pick)
        buf = jnp.stack(ordered, axis=1).reshape((-1,) + piece.shape)
        if hold is not None and kept is None:
            buf, kept = lax.optimization_barrier((buf, hold))
    result = buf.reshape((size * piece.shape[0],) + piece.shape[1:])
    return result if hold is None else (result, kept)

def per_device(
    draws_user, draws_item, prior_user, prior_item, count_tiles, tile_blocks, tile_count
):
    width = DRAWS * DIM
    user_own = draws_user[0]
    item_own = draws_item[0]
    in_use = jnp.arange(TMAX, dtype=jnp.int32) < tile_count[0, 0]
    row_pick = (tile_blocks[0, 0, :, 0][:, None] == jnp.arange(RB, dtype=jnp.int32)) & in_use[:, None]
    col_pick = (tile_blocks[0, 0, :, 1][:, None] == jnp.arange(CB, dtype=jnp.int32)) & in_use[:, None]
    place = (row_pick[:, :, None] & col_pick[:, None, :]).astype(jnp.bfloat16)

    def build_counts(tiles):
        tiles_bf = tiles.astype(jnp.bfloat16)
        counts_bf = jnp.einsum(
            "trc,tij->ricj", place, tiles_bf, preferred_element_type=jnp.bfloat16
        ).reshape(RB * TILE, CB * TILE)
        counts_t = jnp.einsum(
            "trc,tij->cjri", place, tiles_bf, preferred_element_type=jnp.bfloat16
        ).reshape(CB * TILE, RB * TILE)
        tile_rows = jnp.sum(tiles_bf, axis=2, dtype=jnp.float32)
        tile_cols = jnp.sum(tiles_bf, axis=1, dtype=jnp.float32)
        user_deg = jnp.sum(jnp.where(row_pick[:, :, None], tile_rows[:, None, :], 0.0), axis=0)
        item_deg = jnp.sum(jnp.where(col_pick[:, :, None], tile_cols[:, None, :], 0.0), axis=0)
        return (counts_bf, counts_t, user_deg.reshape(-1), item_deg.reshape(-1))

    def cross_parts(user_range, item_range, counts):
        counts_bf, counts_t, user_deg, item_deg = counts
        to_users = jnp.dot(counts_bf, item_range, preferred_element_type=jnp.float32)
        to_users = to_users + user_deg[:, None] * user_range.astype(jnp.float32)
        to_items = jnp.dot(counts_t, user_range, preferred_element_type=jnp.float32)
        to_items = to_items + item_deg[:, None] * item_range.astype(jnp.float32)
        return (to_users, to_items)

    def user_range_of(user_vec):
        return double_gather(user_vec.astype(jnp.bfloat16), "item")

    def operate(user_vec, item_vec, counts):
        user_range = user_range_of(user_vec)
        if counts is None:
            item_range, (tiles, user_vec, item_vec) = double_gather(
                item_vec.astype(jnp.bfloat16), "user", (count_tiles[0, 0], user_vec, item_vec)
            )
            counts = build_counts(tiles)
        else:
            item_range, (user_vec, item_vec) = double_gather(
                item_vec.astype(jnp.bfloat16), "user", (user_vec, item_vec)
            )
        part_user, part_item = cross_parts(user_range, item_range, counts)
        prior_user_part = prior_term(user_vec, prior_user)
        prior_item_part = prior_term(item_vec, prior_item)
        norm_part = per_draw(user_vec, user_vec) + per_draw(item_vec, item_vec)
        cross_dot = per_draw(user_range.astype(jnp.float32), part_user) + per_draw(
            item_range.astype(jnp.float32), part_item
        )
        curve_part = (
            per_draw(user_vec, prior_user_part)
            + per_draw(item_vec, prior_item_part)
            + noise_prec * cross_dot
        )
        sums = jnp.concatenate([norm_part, curve_part]).reshape(1, 2 * DRAWS)
        sums = jnp.pad(sums, ((0, 0), (0, width - 2 * DRAWS)))
        total_user, _ = halve_sum(part_user, "item", jnp.bfloat16)
        total_item, sums = halve_sum(part_item, "user", jnp.float32, sums, jnp.bfloat16)
        sums = sums[0, : 2 * DRAWS]
        size, bits = bit_count("item")
        for bit in range(bits):
            sums = sums + swap_with(sums, "item", size, bit)
        image_user = prior_user_part + noise_prec * total_user
        image_item = prior_item_part + noise_prec * total_item
        return (image_user, image_item, sums[:DRAWS], sums[DRAWS:], counts)

    sol_user = jnp.zeros_like(user_own)
    sol_item = jnp.zeros_like(item_own)
    res_user, res_item = (user_own, item_own)
    dir_user, dir_item = (user_own, item_own)

    along_user, along_item, norm_now, curve, counts = operate(res_user, res_item, None)
    step_len = norm_now / curve
    for iteration in range(ITERS):
        sol_user = sol_user + widen(step_len) * dir_user
        sol_item = sol_item + widen(step_len) * dir_item
        res_user = res_user - widen(step_len) * along_user
        res_item = res_item - widen(step_len) * along_item
        if iteration + 1 < ITERS:
            image_user, image_item, norm_next, curve, _ = operate(res_user, res_item, counts)
            beta_coef = norm_next / norm_now
            step_len = norm_next / (curve - beta_coef * norm_next / step_len)
            dir_user = res_user + widen(beta_coef) * dir_user
            dir_item = res_item + widen(beta_coef) * dir_item
            along_user = image_user + widen(beta_coef) * along_user
            along_item = image_item + widen(beta_coef) * along_item
            norm_now = norm_next
    return (sol_user[None], sol_item[None], res_user[None], res_item[None])


def solution(mesh):
    in_specs = (
        P("user", "item", None),
        P("item", "user", None),
        P(),
        P(),
        P("user", "item", None, None, None),
        P("user", "item", None, None),
        P("user", "item"),
    )
    out_specs = (
        P("user", "item", None),
        P("item", "user", None),
        P("user", "item", None),
        P("item", "user", None),
    )
    return jax.shard_map(
        per_device, mesh=mesh, in_specs=in_specs, out_specs=out_specs, check_vma=False
    )
```

```python
import jax
import jax.numpy as jnp
from jax import lax
from jax.sharding import PartitionSpec as P

DIM = 64
DRAWS = 4
TILE = 256
RB = 3
CB = 4
TMAX = 12
ITERS = 2


top_prec = lax.Precision.HIGHEST
noise_prec = 0.03125


def prior_term(field_vec, prior_mat):
    row_total = field_vec.shape[0]
    grouped = field_vec.reshape(row_total * DRAWS, DIM)
    mixed = jnp.dot(grouped, prior_mat, precision=top_prec)
    return mixed.reshape(row_total, DRAWS * DIM)


def per_draw(left, right):
    product = (left * right).reshape(-1, DRAWS, DIM)
    return jnp.sum(product, axis=(0, 2))


def widen(coef):
    return jnp.repeat(coef, DIM)


def bit_count(axis):
    size = lax.axis_size(axis)
    bits = size.bit_length() - 1
    assert size == 1 << bits
    return size, bits


def swap_with(value, axis, size, bit, mask=None):
    mask = (1 << bit) if mask is None else mask
    pairs = [(i, i ^ mask) for i in range(size)]
    return lax.ppermute(value, axis, pairs)


def butterfly_psum(values):
    values = jnp.stack(values)
    for axis in ("item", "user"):
        size, bits = bit_count(axis)
        for bit in range(bits):
            values = values + swap_with(values, axis, size, bit)
    return values[0], values[1]


def code_rows(extra):
    high = extra.astype(jnp.bfloat16)
    rest = extra - high.astype(jnp.float32)
    mid = rest.astype(jnp.bfloat16)
    low = (rest - mid.astype(jnp.float32)).astype(jnp.bfloat16)
    return jnp.concatenate([high, mid, low])


def halve_sum(part, axis, send_type, extra=None, first_type=None):
    size, bits = bit_count(axis)
    me = lax.axis_index(axis)
    rows, width = part.shape[0] // size, part.shape[1]
    groups = [list(range(bits))[i : i + 2] for i in range(0, bits, 2)]
    left = list(range(bits))[::-1]
    buf = part.reshape([2] * bits + [rows, width])
    for stage, group in enumerate(groups):
        masks = [sum(1 << group[j] for j in range(len(group)) if (k >> j) & 1) for k in range(1 << len(group))]
        digit = sum(((me >> group[j]) & 1) << j for j in range(len(group)))

        def block_of(value):
            out = buf
            for j in sorted(range(len(group)), key=lambda j: -left.index(group[j])):
                out = lax.dynamic_index_in_dim(out, (value >> j) & 1, left.index(group[j]), keepdims=False)
            return out

        coded = extra is not None and first_type is not None
        stage_type = send_type if first_type is None else first_type
        total = block_of(digit)
        shape = total.shape
        if extra is not None:
            tail = jnp.concatenate([extra, jnp.zeros((2 * extra.shape[0], width), extra.dtype)]) if coded else extra
            total = jnp.concatenate([total.reshape(-1, width), tail])
        for k in range(1, len(masks)):
            send = block_of(digit ^ k).astype(stage_type)
            if extra is not None:
                tail = code_rows(extra) if coded else extra
                send = jnp.concatenate([send.reshape(-1, width), tail.astype(stage_type)])
            total = total + swap_with(send, axis, size, None, masks[k]).astype(jnp.float32)
        if extra is not None:
            count = extra.shape[0]
            if coded:
                tail = total[-3 * count :]
                total = total[: -3 * count].reshape(shape)
                extra = tail[:count] + tail[count : 2 * count] + tail[2 * count :]
            else:
                extra = total[-count:]
                total = total[:-count].reshape(shape)
        for bit in group:
            left.remove(bit)
        buf = total
    return buf.reshape(rows, width), extra


def double_gather(piece, axis, hold=None):
    size, bits = bit_count(axis)
    me = lax.axis_index(axis)
    groups = [list(range(bits))[i : i + 2] for i in range(0, bits, 2)]
    buf = piece[None]
    kept = None
    for group in groups:
        masks = [sum(1 << group[j] for j in range(len(group)) if (k >> j) & 1) for k in range(1 << len(group))]
        pieces = [buf] + [swap_with(buf, axis, size, None, mask) for mask in masks[1:]]
        digit = sum(((me >> group[j]) & 1) << j for j in range(len(group)))
        ordered = []
        for place in range(len(masks)):
            pick = pieces[place]
            for held in range(1, len(masks)):
                pick = jnp.where(digit == held, pieces[place ^ held], pick)
            ordered.append(pick)
        buf = jnp.stack(ordered, axis=0).reshape((-1,) + piece.shape)
        if hold is not None and kept is None:
            buf, kept = lax.optimization_barrier((buf, hold))
    result = buf.reshape((size * piece.shape[0],) + piece.shape[1:])
    return result if hold is None else (result, kept)

def per_device(
    draws_user, draws_item, prior_user, prior_item, count_tiles, tile_blocks, tile_count
):
    width = DRAWS * DIM
    user_own = draws_user[0]
    item_own = draws_item[0]
    in_use = jnp.arange(TMAX, dtype=jnp.int32) < tile_count[0, 0]
    row_pick = (tile_blocks[0, 0, :, 0][:, None] == jnp.arange(RB, dtype=jnp.int32)) & in_use[:, None]
    col_pick = (tile_blocks[0, 0, :, 1][:, None] == jnp.arange(CB, dtype=jnp.int32)) & in_use[:, None]
    place = (row_pick[:, :, None] & col_pick[:, None, :]).astype(jnp.bfloat16)

    def build_counts(tiles):
        tiles_bf = tiles.astype(jnp.bfloat16)
        counts_bf = jnp.einsum(
            "trc,tij->ricj", place, tiles_bf, preferred_element_type=jnp.bfloat16
        ).reshape(RB * TILE, CB * TILE)
        counts_t = jnp.einsum(
            "trc,tij->cjri", place, tiles_bf, preferred_element_type=jnp.bfloat16
        ).reshape(CB * TILE, RB * TILE)
        tile_rows = jnp.sum(tiles_bf, axis=2, dtype=jnp.float32)
        tile_cols = jnp.sum(tiles_bf, axis=1, dtype=jnp.float32)
        user_deg = jnp.sum(jnp.where(row_pick[:, :, None], tile_rows[:, None, :], 0.0), axis=0)
        item_deg = jnp.sum(jnp.where(col_pick[:, :, None], tile_cols[:, None, :], 0.0), axis=0)
        return (counts_bf, counts_t, user_deg.reshape(-1), item_deg.reshape(-1))

    def cross_parts(user_range, item_range, counts):
        counts_bf, counts_t, user_deg, item_deg = counts
        to_users = jnp.dot(counts_bf, item_range, preferred_element_type=jnp.float32)
        to_users = to_users + user_deg[:, None] * user_range.astype(jnp.float32)
        to_items = jnp.dot(counts_t, user_range, preferred_element_type=jnp.float32)
        to_items = to_items + item_deg[:, None] * item_range.astype(jnp.float32)
        return (to_users, to_items)

    def user_range_of(user_vec):
        return double_gather(user_vec.astype(jnp.bfloat16), "item")

    def operate(user_vec, item_vec, counts):
        user_range = user_range_of(user_vec)
        if counts is None:
            item_range, (tiles, user_vec, item_vec) = double_gather(
                item_vec.astype(jnp.bfloat16), "user", (count_tiles[0, 0], user_vec, item_vec)
            )
            counts = build_counts(tiles)
        else:
            item_range, (user_vec, item_vec) = double_gather(
                item_vec.astype(jnp.bfloat16), "user", (user_vec, item_vec)
            )
        part_user, part_item = cross_parts(user_range, item_range, counts)
        prior_user_part = prior_term(user_vec, prior_user)
        prior_item_part = prior_term(item_vec, prior_item)
        norm_part = per_draw(user_vec, user_vec) + per_draw(item_vec, item_vec)
        cross_dot = per_draw(user_range.astype(jnp.float32), part_user) + per_draw(
            item_range.astype(jnp.float32), part_item
        )
        curve_part = (
            per_draw(user_vec, prior_user_part)
            + per_draw(item_vec, prior_item_part)
            + noise_prec * cross_dot
        )
        sums = jnp.concatenate([norm_part, curve_part]).reshape(1, 2 * DRAWS)
        sums = jnp.pad(sums, ((0, 0), (0, width - 2 * DRAWS)))
        total_user, _ = halve_sum(part_user, "item", jnp.bfloat16)
        total_item, sums = halve_sum(part_item, "user", jnp.float32, sums, jnp.bfloat16)
        sums = sums[0, : 2 * DRAWS]
        size, bits = bit_count("item")
        for bit in range(bits):
            sums = sums + swap_with(sums, "item", size, bit)
        image_user = prior_user_part + noise_prec * total_user
        image_item = prior_item_part + noise_prec * total_item
        return (image_user, image_item, sums[:DRAWS], sums[DRAWS:], counts)

    sol_user = jnp.zeros_like(user_own)
    sol_item = jnp.zeros_like(item_own)
    res_user, res_item = (user_own, item_own)
    dir_user, dir_item = (user_own, item_own)

    along_user, along_item, norm_now, curve, counts = operate(res_user, res_item, None)
    step_len = norm_now / curve
    for iteration in range(ITERS):
        sol_user = sol_user + widen(step_len) * dir_user
        sol_item = sol_item + widen(step_len) * dir_item
        res_user = res_user - widen(step_len) * along_user
        res_item = res_item - widen(step_len) * along_item
        if iteration + 1 < ITERS:
            image_user, image_item, norm_next, curve, _ = operate(res_user, res_item, counts)
            beta_coef = norm_next / norm_now
            step_len = norm_next / (curve - beta_coef * norm_next / step_len)
            dir_user = res_user + widen(beta_coef) * dir_user
            dir_item = res_item + widen(beta_coef) * dir_item
            along_user = image_user + widen(beta_coef) * along_user
            along_item = image_item + widen(beta_coef) * along_item
            norm_now = norm_next
    return (sol_user[None], sol_item[None], res_user[None], res_item[None])


def solution(mesh):
    in_specs = (
        P("user", "item", None),
        P("item", "user", None),
        P(),
        P(),
        P("user", "item", None, None, None),
        P("user", "item", None, None),
        P("user", "item"),
    )
    out_specs = (
        P("user", "item", None),
        P("item", "user", None),
        P("user", "item", None),
        P("item", "user", None),
    )
    return jax.shard_map(
        per_device, mesh=mesh, in_specs=in_specs, out_specs=out_specs, check_vma=False
    )
```

```python
import jax
import jax.numpy as jnp
from jax import lax
from jax.sharding import PartitionSpec as P

DIM = 64
DRAWS = 4
TILE = 256
RB = 3
CB = 4
TMAX = 12
ITERS = 2


top_prec = lax.Precision.HIGHEST
noise_prec = 0.03125


def prior_term(field_vec, prior_mat):
    row_total = field_vec.shape[0]
    grouped = field_vec.reshape(row_total * DRAWS, DIM)
    mixed = jnp.dot(grouped, prior_mat, precision=top_prec)
    return mixed.reshape(row_total, DRAWS * DIM)


def per_draw(left, right):
    product = (left * right).reshape(-1, DRAWS, DIM)
    return jnp.sum(product, axis=(0, 2))


def widen(coef):
    return jnp.repeat(coef, DIM)


def bit_count(axis):
    size = lax.axis_size(axis)
    bits = size.bit_length() - 1
    assert size == 1 << bits
    return size, bits


def swap_with(value, axis, size, bit, mask=None):
    mask = (1 << bit) if mask is None else mask
    pairs = [(i, i ^ mask) for i in range(size)]
    return lax.ppermute(value, axis, pairs)


def butterfly_psum(values):
    values = jnp.stack(values)
    for axis in ("item", "user"):
        size, bits = bit_count(axis)
        for bit in range(bits):
            values = values + swap_with(values, axis, size, bit)
    return values[0], values[1]


def code_rows(extra):
    high = extra.astype(jnp.bfloat16)
    rest = extra - high.astype(jnp.float32)
    mid = rest.astype(jnp.bfloat16)
    low = (rest - mid.astype(jnp.float32)).astype(jnp.bfloat16)
    return jnp.concatenate([high, mid, low])


def halve_sum(part, axis, send_type, extra=None, first_type=None, relative=False):
    size, bits = bit_count(axis)
    me = lax.axis_index(axis)
    rows, width = part.shape[0] // size, part.shape[1]
    groups = [list(range(bits))[i : i + 2] for i in range(0, bits, 2)]
    left = list(range(bits))[::-1]
    buf = part.reshape([2] * bits + [rows, width])
    for stage, group in enumerate(groups):
        masks = [sum(1 << group[j] for j in range(len(group)) if (k >> j) & 1) for k in range(1 << len(group))]
        digit = sum(((me >> group[j]) & 1) << j for j in range(len(group)))

        def block_of(value):
            out = buf
            for j in sorted(range(len(group)), key=lambda j: -left.index(group[j])):
                if relative:
                    out = lax.index_in_dim(out, (value >> j) & 1, left.index(group[j]), keepdims=False)
                else:
                    out = lax.dynamic_index_in_dim(out, (value >> j) & 1, left.index(group[j]), keepdims=False)
            return out

        coded = extra is not None and first_type is not None
        stage_type = send_type if first_type is None else first_type
        total = block_of(0 if relative else digit)
        shape = total.shape
        if extra is not None:
            tail = jnp.concatenate([extra, jnp.zeros((2 * extra.shape[0], width), extra.dtype)]) if coded else extra
            total = jnp.concatenate([total.reshape(-1, width), tail])
        for k in range(1, len(masks)):
            send = block_of(k if relative else digit ^ k).astype(stage_type)
            if extra is not None:
                tail = code_rows(extra) if coded else extra
                send = jnp.concatenate([send.reshape(-1, width), tail.astype(stage_type)])
            total = total + swap_with(send, axis, size, None, masks[k]).astype(jnp.float32)
        if extra is not None:
            count = extra.shape[0]
            if coded:
                tail = total[-3 * count :]
                total = total[: -3 * count].reshape(shape)
                extra = tail[:count] + tail[count : 2 * count] + tail[2 * count :]
            else:
                extra = total[-count:]
                total = total[:-count].reshape(shape)
        for bit in group:
            left.remove(bit)
        buf = total
    return buf.reshape(rows, width), extra


def double_gather(piece, axis, hold=None):
    size, bits = bit_count(axis)
    me = lax.axis_index(axis)
    order = list(range(bits))[::-1]
    groups = [order[:1]] if bits % 2 else []
    groups += [order[i : i + 2] for i in range(bits % 2, bits, 2)]
    buf = piece[None]
    kept = None
    for group in groups:
        masks = [sum(1 << group[-1 - j] for j in range(len(group)) if (k >> j) & 1) for k in range(1 << len(group))]
        pieces = [buf] + [swap_with(buf, axis, size, None, mask) for mask in masks[1:]]
        digit = sum(((me >> group[-1 - j]) & 1) << j for j in range(len(group)))
        ordered = []
        for place in range(len(masks)):
            pick = pieces[place]
            for held in range(1, len(masks)):
                pick = jnp.where(digit == held, pieces[place ^ held], pick)
            ordered.append(pick)
        buf = jnp.stack(ordered, axis=1).reshape((-1,) + piece.shape)
        if hold is not None and kept is None:
            buf, kept = lax.optimization_barrier((buf, hold))
    result = buf.reshape((size * piece.shape[0],) + piece.shape[1:])
    return result if hold is None else (result, kept)

def xor_gather(piece, axis):
    size, bits = bit_count(axis)
    buf = piece[None]
    for bit in reversed(range(bits)):
        buf = jnp.stack([buf, swap_with(buf, axis, size, bit)], axis=1).reshape((-1,) + piece.shape)
    return buf.reshape((size * piece.shape[0],) + piece.shape[1:])


def xor_order(value, axis, dim):
    size = lax.axis_size(axis)
    me = lax.axis_index(axis)
    shape = value.shape
    split = shape[:dim] + (size, shape[dim] // size) + shape[dim + 1 :]
    picked = jnp.take(value.reshape(split), jnp.arange(size) ^ me, axis=dim)
    return picked.reshape(shape)


def per_device(
    draws_user, draws_item, prior_user, prior_item, count_tiles, tile_blocks, tile_count
):
    width = DRAWS * DIM
    user_own = draws_user[0]
    item_own = draws_item[0]
    in_use = jnp.arange(TMAX, dtype=jnp.int32) < tile_count[0, 0]
    row_pick = (tile_blocks[0, 0, :, 0][:, None] == jnp.arange(RB, dtype=jnp.int32)) & in_use[:, None]
    col_pick = (tile_blocks[0, 0, :, 1][:, None] == jnp.arange(CB, dtype=jnp.int32)) & in_use[:, None]
    place = (row_pick[:, :, None] & col_pick[:, None, :]).astype(jnp.bfloat16)

    def build_counts(tiles):
        tiles_bf = tiles.astype(jnp.bfloat16)
        counts_bf = jnp.einsum(
            "trc,tij->ricj", place, tiles_bf, preferred_element_type=jnp.bfloat16
        ).reshape(RB * TILE, CB * TILE)
        counts_t = jnp.einsum(
            "trc,tij->cjri", place, tiles_bf, preferred_element_type=jnp.bfloat16
        ).reshape(CB * TILE, RB * TILE)
        tile_rows = jnp.sum(tiles_bf, axis=2, dtype=jnp.float32)
        tile_cols = jnp.sum(tiles_bf, axis=1, dtype=jnp.float32)
        user_deg = jnp.sum(jnp.where(row_pick[:, :, None], tile_rows[:, None, :], 0.0), axis=0)
        item_deg = jnp.sum(jnp.where(col_pick[:, :, None], tile_cols[:, None, :], 0.0), axis=0)
        counts_bf = xor_order(counts_bf, "item", 0)
        counts_t = xor_order(counts_t, "item", 1)
        user_deg = xor_order(user_deg.reshape(-1), "item", 0)
        return (counts_bf, counts_t, user_deg, item_deg.reshape(-1))

    def cross_parts(user_range, item_range, counts):
        counts_bf, counts_t, user_deg, item_deg = counts
        to_users = jnp.dot(counts_bf, item_range, preferred_element_type=jnp.float32)
        to_users = to_users + user_deg[:, None] * user_range.astype(jnp.float32)
        to_items = jnp.dot(counts_t, user_range, preferred_element_type=jnp.float32)
        to_items = to_items + item_deg[:, None] * item_range.astype(jnp.float32)
        return (to_users, to_items)

    def user_range_of(user_vec):
        return xor_gather(user_vec.astype(jnp.bfloat16), "item")

    def operate(user_vec, item_vec, counts):
        user_range = user_range_of(user_vec)
        if counts is None:
            item_range, (tiles, user_vec, item_vec) = double_gather(
                item_vec.astype(jnp.bfloat16), "user", (count_tiles[0, 0], user_vec, item_vec)
            )
            counts = build_counts(tiles)
        else:
            item_range, (user_vec, item_vec) = double_gather(
                item_vec.astype(jnp.bfloat16), "user", (user_vec, item_vec)
            )
        part_user, part_item = cross_parts(user_range, item_range, counts)
        prior_user_part = prior_term(user_vec, prior_user)
        prior_item_part = prior_term(item_vec, prior_item)
        norm_part = per_draw(user_vec, user_vec) + per_draw(item_vec, item_vec)
        cross_dot = per_draw(user_range.astype(jnp.float32), part_user) + per_draw(
            item_range.astype(jnp.float32), part_item
        )
        curve_part = (
            per_draw(user_vec, prior_user_part)
            + per_draw(item_vec, prior_item_part)
            + noise_prec * cross_dot
        )
        sums = jnp.concatenate([norm_part, curve_part]).reshape(1, 2 * DRAWS)
        sums = jnp.pad(sums, ((0, 0), (0, width - 2 * DRAWS)))
        total_user, _ = halve_sum(part_user, "item", jnp.bfloat16, relative=True)
        total_item, sums = halve_sum(part_item, "user", jnp.float32, sums, jnp.bfloat16)
        sums = sums[0, : 2 * DRAWS]
        size, bits = bit_count("item")
        for bit in range(bits):
            sums = sums + swap_with(sums, "item", size, bit)
        image_user = prior_user_part + noise_prec * total_user
        image_item = prior_item_part + noise_prec * total_item
        return (image_user, image_item, sums[:DRAWS], sums[DRAWS:], counts)

    sol_user = jnp.zeros_like(user_own)
    sol_item = jnp.zeros_like(item_own)
    res_user, res_item = (user_own, item_own)
    dir_user, dir_item = (user_own, item_own)

    along_user, along_item, norm_now, curve, counts = operate(res_user, res_item, None)
    step_len = norm_now / curve
    for iteration in range(ITERS):
        sol_user = sol_user + widen(step_len) * dir_user
        sol_item = sol_item + widen(step_len) * dir_item
        res_user = res_user - widen(step_len) * along_user
        res_item = res_item - widen(step_len) * along_item
        if iteration + 1 < ITERS:
            image_user, image_item, norm_next, curve, _ = operate(res_user, res_item, counts)
            beta_coef = norm_next / norm_now
            step_len = norm_next / (curve - beta_coef * norm_next / step_len)
            dir_user = res_user + widen(beta_coef) * dir_user
            dir_item = res_item + widen(beta_coef) * dir_item
            along_user = image_user + widen(beta_coef) * along_user
            along_item = image_item + widen(beta_coef) * along_item
            norm_now = norm_next
    return (sol_user[None], sol_item[None], res_user[None], res_item[None])


def solution(mesh):
    in_specs = (
        P("user", "item", None),
        P("item", "user", None),
        P(),
        P(),
        P("user", "item", None, None, None),
        P("user", "item", None, None),
        P("user", "item"),
    )
    out_specs = (
        P("user", "item", None),
        P("item", "user", None),
        P("user", "item", None),
        P("item", "user", None),
    )
    return jax.shard_map(
        per_device, mesh=mesh, in_specs=in_specs, out_specs=out_specs, check_vma=False
    )
```

```python
import jax
import jax.numpy as jnp
from jax import lax
from jax.sharding import PartitionSpec as P

DIM = 64
DRAWS = 4
TILE = 256
RB = 3
CB = 4
TMAX = 12
ITERS = 2


top_prec = lax.Precision.HIGHEST
noise_prec = 0.03125


def prior_term(field_vec, prior_mat):
    row_total = field_vec.shape[0]
    grouped = field_vec.reshape(row_total * DRAWS, DIM)
    mixed = jnp.dot(grouped, prior_mat, precision=top_prec)
    return mixed.reshape(row_total, DRAWS * DIM)


def per_draw(left, right):
    product = (left * right).reshape(-1, DRAWS, DIM)
    return jnp.sum(product, axis=(0, 2))


def widen(coef):
    return jnp.repeat(coef, DIM)


def bit_count(axis):
    size = lax.axis_size(axis)
    bits = size.bit_length() - 1
    assert size == 1 << bits
    return size, bits


def swap_with(value, axis, size, bit, mask=None):
    mask = (1 << bit) if mask is None else mask
    pairs = [(i, i ^ mask) for i in range(size)]
    return lax.ppermute(value, axis, pairs)


def butterfly_psum(values):
    values = jnp.stack(values)
    for axis in ("item", "user"):
        size, bits = bit_count(axis)
        for bit in range(bits):
            values = values + swap_with(values, axis, size, bit)
    return values[0], values[1]


def code_rows(extra):
    high = extra.astype(jnp.bfloat16)
    rest = extra - high.astype(jnp.float32)
    mid = rest.astype(jnp.bfloat16)
    low = (rest - mid.astype(jnp.float32)).astype(jnp.bfloat16)
    return jnp.concatenate([high, mid, low])


def halve_sum(part, axis, send_type, extra=None, first_type=None):
    size, bits = bit_count(axis)
    me = lax.axis_index(axis)
    rows, width = part.shape[0] // size, part.shape[1]
    groups = [list(range(bits))[i : i + 2] for i in range(0, bits, 2)]
    left = list(range(bits))[::-1]
    buf = part.reshape([2] * bits + [rows, width])
    for stage, group in enumerate(groups):
        masks = [sum(1 << group[j] for j in range(len(group)) if (k >> j) & 1) for k in range(1 << len(group))]
        digit = sum(((me >> group[j]) & 1) << j for j in range(len(group)))

        def block_of(value):
            out = buf
            for j in sorted(range(len(group)), key=lambda j: -left.index(group[j])):
                pos = left.index(group[j])
                upper = ((value >> j) & 1) == 1
                out = jnp.where(
                    upper,
                    lax.index_in_dim(out, 1, pos, keepdims=False),
                    lax.index_in_dim(out, 0, pos, keepdims=False),
                )
            return out

        coded = extra is not None and first_type is not None
        stage_type = send_type if first_type is None else first_type
        total = block_of(digit)
        shape = total.shape
        if extra is not None:
            tail = jnp.concatenate([extra, jnp.zeros((2 * extra.shape[0], width), extra.dtype)]) if coded else extra
            total = jnp.concatenate([total.reshape(-1, width), tail])
        for k in range(1, len(masks)):
            send = block_of(digit ^ k).astype(stage_type)
            if extra is not None:
                tail = code_rows(extra) if coded else extra
                send = jnp.concatenate([send.reshape(-1, width), tail.astype(stage_type)])
            total = total + swap_with(send, axis, size, None, masks[k]).astype(jnp.float32)
        if extra is not None:
            count = extra.shape[0]
            if coded:
                tail = total[-3 * count :]
                total = total[: -3 * count].reshape(shape)
                extra = tail[:count] + tail[count : 2 * count] + tail[2 * count :]
            else:
                extra = total[-count:]
                total = total[:-count].reshape(shape)
        for bit in group:
            left.remove(bit)
        buf = total
    return buf.reshape(rows, width), extra


def double_gather(piece, axis, hold=None):
    size, bits = bit_count(axis)
    me = lax.axis_index(axis)
    order = list(range(bits))[::-1]
    groups = [order[:1]] if bits % 2 else []
    groups += [order[i : i + 2] for i in range(bits % 2, bits, 2)]
    buf = piece[None]
    kept = None
    for group in groups:
        masks = [sum(1 << group[-1 - j] for j in range(len(group)) if (k >> j) & 1) for k in range(1 << len(group))]
        pieces = [buf] + [swap_with(buf, axis, size, None, mask) for mask in masks[1:]]
        digit = sum(((me >> group[-1 - j]) & 1) << j for j in range(len(group)))
        ordered = []
        for place in range(len(masks)):
            pick = pieces[place]
            for held in range(1, len(masks)):
                pick = jnp.where(digit == held, pieces[place ^ held], pick)
            ordered.append(pick)
        buf = jnp.stack(ordered, axis=1).reshape((-1,) + piece.shape)
        if hold is not None and kept is None:
            buf, kept = lax.optimization_barrier((buf, hold))
    result = buf.reshape((size * piece.shape[0],) + piece.shape[1:])
    return result if hold is None else (result, kept)

def per_device(
    draws_user, draws_item, prior_user, prior_item, count_tiles, tile_blocks, tile_count
):
    width = DRAWS * DIM
    user_own = draws_user[0]
    item_own = draws_item[0]
    in_use = jnp.arange(TMAX, dtype=jnp.int32) < tile_count[0, 0]
    row_pick = (tile_blocks[0, 0, :, 0][:, None] == jnp.arange(RB, dtype=jnp.int32)) & in_use[:, None]
    col_pick = (tile_blocks[0, 0, :, 1][:, None] == jnp.arange(CB, dtype=jnp.int32)) & in_use[:, None]
    place = (row_pick[:, :, None] & col_pick[:, None, :]).astype(jnp.bfloat16)

    def build_counts(tiles):
        tiles_bf = tiles.astype(jnp.bfloat16)
        counts_bf = jnp.einsum(
            "trc,tij->ricj", place, tiles_bf, preferred_element_type=jnp.bfloat16
        ).reshape(RB * TILE, CB * TILE)
        counts_t = jnp.einsum(
            "trc,tij->cjri", place, tiles_bf, preferred_element_type=jnp.bfloat16
        ).reshape(CB * TILE, RB * TILE)
        tile_rows = jnp.sum(tiles_bf, axis=2, dtype=jnp.float32)
        tile_cols = jnp.sum(tiles_bf, axis=1, dtype=jnp.float32)
        user_deg = jnp.sum(jnp.where(row_pick[:, :, None], tile_rows[:, None, :], 0.0), axis=0)
        item_deg = jnp.sum(jnp.where(col_pick[:, :, None], tile_cols[:, None, :], 0.0), axis=0)
        return (counts_bf, counts_t, user_deg.reshape(-1), item_deg.reshape(-1))

    def cross_parts(user_range, item_range, counts):
        counts_bf, counts_t, user_deg, item_deg = counts
        to_users = jnp.dot(counts_bf, item_range, preferred_element_type=jnp.float32)
        to_users = to_users + user_deg[:, None] * user_range.astype(jnp.float32)
        to_items = jnp.dot(counts_t, user_range, preferred_element_type=jnp.float32)
        to_items = to_items + item_deg[:, None] * item_range.astype(jnp.float32)
        return (to_users, to_items)

    def user_range_of(user_vec):
        return double_gather(user_vec.astype(jnp.bfloat16), "item")

    def operate(user_vec, item_vec, counts):
        user_range = user_range_of(user_vec)
        if counts is None:
            item_range, (tiles, user_vec, item_vec) = double_gather(
                item_vec.astype(jnp.bfloat16), "user", (count_tiles[0, 0], user_vec, item_vec)
            )
            counts = build_counts(tiles)
        else:
            item_range, (user_vec, item_vec) = double_gather(
                item_vec.astype(jnp.bfloat16), "user", (user_vec, item_vec)
            )
        part_user, part_item = cross_parts(user_range, item_range, counts)
        prior_user_part = prior_term(user_vec, prior_user)
        prior_item_part = prior_term(item_vec, prior_item)
        norm_part = per_draw(user_vec, user_vec) + per_draw(item_vec, item_vec)
        cross_dot = per_draw(user_range.astype(jnp.float32), part_user) + per_draw(
            item_range.astype(jnp.float32), part_item
        )
        curve_part = (
            per_draw(user_vec, prior_user_part)
            + per_draw(item_vec, prior_item_part)
            + noise_prec * cross_dot
        )
        sums = jnp.concatenate([norm_part, curve_part]).reshape(1, 2 * DRAWS)
        sums = jnp.pad(sums, ((0, 0), (0, width - 2 * DRAWS)))
        total_user, _ = halve_sum(part_user, "item", jnp.bfloat16)
        total_item, sums = halve_sum(part_item, "user", jnp.float32, sums, jnp.bfloat16)
        sums = sums[0, : 2 * DRAWS]
        size, bits = bit_count("item")
        for bit in range(bits):
            sums = sums + swap_with(sums, "item", size, bit)
        image_user = prior_user_part + noise_prec * total_user
        image_item = prior_item_part + noise_prec * total_item
        return (image_user, image_item, sums[:DRAWS], sums[DRAWS:], counts)

    sol_user = jnp.zeros_like(user_own)
    sol_item = jnp.zeros_like(item_own)
    res_user, res_item = (user_own, item_own)
    dir_user, dir_item = (user_own, item_own)

    along_user, along_item, norm_now, curve, counts = operate(res_user, res_item, None)
    step_len = norm_now / curve
    for iteration in range(ITERS):
        sol_user = sol_user + widen(step_len) * dir_user
        sol_item = sol_item + widen(step_len) * dir_item
        res_user = res_user - widen(step_len) * along_user
        res_item = res_item - widen(step_len) * along_item
        if iteration + 1 < ITERS:
            image_user, image_item, norm_next, curve, _ = operate(res_user, res_item, counts)
            beta_coef = norm_next / norm_now
            step_len = norm_next / (curve - beta_coef * norm_next / step_len)
            dir_user = res_user + widen(beta_coef) * dir_user
            dir_item = res_item + widen(beta_coef) * dir_item
            along_user = image_user + widen(beta_coef) * along_user
            along_item = image_item + widen(beta_coef) * along_item
            norm_now = norm_next
    return (sol_user[None], sol_item[None], res_user[None], res_item[None])


def solution(mesh):
    in_specs = (
        P("user", "item", None),
        P("item", "user", None),
        P(),
        P(),
        P("user", "item", None, None, None),
        P("user", "item", None, None),
        P("user", "item"),
    )
    out_specs = (
        P("user", "item", None),
        P("item", "user", None),
        P("user", "item", None),
        P("item", "user", None),
    )
    return jax.shard_map(
        per_device, mesh=mesh, in_specs=in_specs, out_specs=out_specs, check_vma=False
    )
```
